32 devices in a mesh: sep: 2 (over x), row: 16 (over z, y, core).
Axes of the slice: x: 2, y: 2, z: 4, core: 2. Of those that a mesh axis runs over, the one named last changes fastest.
Arguments:
- right_sides: bfloat16 [256, 256, 128], P(('sep', 'row')), parts along dimension 0, may hold values from -6 to 6
- diagonal_blocks: bfloat16 [256, 256, 256], P(('sep', 'row')), parts along dimension 0, may hold values from -0.375 to 0.375
- lower_rows: bfloat16 [256, 256, 256], P(('sep', 'row')), parts along dimension 0, may hold values from -0.375 to 0.375
- lower_cols: bfloat16 [256, 256, 256], P(('sep', 'row')), parts along dimension 0, may hold values from -0.09375 to 0.09375
- lower_trans: bfloat16 [256, 256, 256], P(('sep', 'row')), parts along dimension 0, may hold values from -2 to 2
- upper_rows: bfloat16 [256, 256, 256], P(('sep', 'row')), parts along dimension 0, may hold values from -0.375 to 0.375
- upper_cols: bfloat16 [256, 256, 256], P(('sep', 'row')), parts along dimension 0, may hold values from -0.09375 to 0.09375
- upper_trans: bfloat16 [256, 256, 256], P(('sep', 'row')), parts along dimension 0, may hold values from -2 to 2
Outputs:
- product: bfloat16 [256, 256, 128], P(('sep', 'row')), parts along dimension 0
The draws below stay inside these ranges and needn't reach their ends.
There are 2 independent parts, one for each index of `sep`. The reference program is written for one: setup_inputs(seed, part) draws one part's arguments, and reference() takes and returns one part's arrays. A program takes and returns all parts, laid end to end along the dimension named above; each array names one. Nothing has to cross between parts.
All inputs are finite; a program needn't handle non-finite values.
Results may differ from the reference program's by a relative error of at most 0.0045.
Values sent between devices are 32-bit elements; how exact they have to be, the bound alone decides.
No kernel may reach another device: no remote copies, remote signals or barrier semaphores. Data moves between devices by JAX's collectives and lax.ppermute only.
A program may use at most 192 MiB of HBM per device.

```python
import math
import jax
import jax.numpy as jnp
from jax import lax

BS = 256
GENERATOR_RANK = 256
RHS = 128
BLOCK_COUNT = 128


mixing_scale = 0.3


def transfer_matrices(key):
    random_subkeys = jax.random.split(key, 6)
    slow_share = 0.5
    decay_mask = jax.random.uniform(random_subkeys[0], (GENERATOR_RANK,)) < slow_share
    slow_fraction = jnp.mean(decay_mask.astype(jnp.float32))
    spread = jax.random.uniform(random_subkeys[1], (GENERATOR_RANK,))
    keep_rate = 0.6 ** (spread / BLOCK_COUNT) / jnp.sqrt(1.0 + mixing_scale ** 2 * slow_fraction)
    fast_span = jnp.exp(jax.random.uniform(random_subkeys[2], (BLOCK_COUNT, GENERATOR_RANK), minval=0.0, maxval=math.log(3.0)))
    fast_rate = jnp.exp(-1.0 / fast_span)
    diagonal_part = jnp.where(decay_mask[None, :], keep_rate[None, :], fast_rate)
    spike_positions = jax.random.randint(random_subkeys[3], (3,), 0, BLOCK_COUNT)
    spike_row_list = jnp.any(jnp.arange(BLOCK_COUNT)[:, None] == spike_positions[None, :], axis=1)
    spike_cutoff = jax.random.uniform(random_subkeys[4], (BLOCK_COUNT, GENERATOR_RANK), minval=0.5, maxval=0.8)
    diagonal_part = jnp.where(spike_row_list[:, None] & decay_mask[None, :], diagonal_part * spike_cutoff, diagonal_part)
    identity = jnp.eye(GENERATOR_RANK, dtype=jnp.float32)
    off_diagonal = 1.0 - identity
    mixing_noise = jnp.clip(jax.random.normal(random_subkeys[5], (BLOCK_COUNT, GENERATOR_RANK, GENERATOR_RANK), jnp.float32), -4.0, 4.0)
    row_scale = mixing_scale * diagonal_part / math.sqrt(GENERATOR_RANK - 1.0)
    mixing = mixing_noise * off_diagonal[None, :, :] * row_scale[:, :, None]
    return diagonal_part[:, :, None] * identity[None, :, :] + mixing


def draw_lower_trans(key, part):
    return transfer_matrices(jax.random.fold_in(key, 11)).astype(jnp.bfloat16)


def draw_upper_trans(key, part):
    return transfer_matrices(jax.random.fold_in(key, 23)).astype(jnp.bfloat16)


def levels(stream_key, shape, pieces, least, top_value):
    level = 1.0
    for axis_at, shards_of in pieces:
        draws = jax.random.uniform(jax.random.fold_in(jax.random.fold_in(stream_key, 6), axis_at), (shards_of,), jnp.float32, least / len(pieces), top_value / len(pieces))
        level = level * jnp.repeat(jnp.exp(draws), shape[axis_at] // shards_of).reshape((-1,) + (1,) * (len(shape) - 1 - axis_at))
    return level


def bell_draw(stream_key, shape, scale, limit, cuts=(), kind=jnp.bfloat16):
    level = levels(stream_key, shape, cuts, -0.22, 0.18) if cuts else 1.0
    entries = jax.random.normal(stream_key, shape, jnp.float32) * scale * level
    return jnp.minimum(jnp.maximum(entries, -limit), limit).astype(kind)


def setup_inputs(seed: int = 0, part: int = 0) -> dict:
    splits = jax.random.split(jax.random.key(seed), 9)
    part_keys = jax.random.split(jax.random.fold_in(splits[8], part), 9)
    return {
        "right_sides": bell_draw(part_keys[0], (BLOCK_COUNT, BS, RHS), 1.0, 6.0, ((0, 16),)),
        "diagonal_blocks": bell_draw(part_keys[1], (BLOCK_COUNT, BS, BS), BS ** -0.5, 0.375, ((0, 16),)),
        "lower_rows": bell_draw(part_keys[2], (BLOCK_COUNT, BS, GENERATOR_RANK), GENERATOR_RANK ** -0.5, 0.375, ((0, 16),)),
        "lower_cols": bell_draw(part_keys[3], (BLOCK_COUNT, BS, GENERATOR_RANK), (BS * 16) ** -0.5, 0.09375, ((0, 16),)),
        "lower_trans": draw_lower_trans(jax.random.fold_in(jax.random.fold_in(splits[8], part), 71), part),
        "upper_rows": bell_draw(part_keys[5], (BLOCK_COUNT, BS, GENERATOR_RANK), GENERATOR_RANK ** -0.5, 0.375, ((0, 16),)),
        "upper_cols": bell_draw(part_keys[6], (BLOCK_COUNT, BS, GENERATOR_RANK), (BS * 16) ** -0.5, 0.09375, ((0, 16),)),
        "upper_trans": draw_upper_trans(jax.random.fold_in(jax.random.fold_in(splits[8], part), 71), part),
    }


def carry_states(transfer, sources, backward):
    def advance(state, pair):
        matrix, source = pair
        return jnp.dot(matrix, state, precision=lax.Precision.HIGHEST) + source, state

    start = jnp.zeros((transfer.shape[1], sources.shape[2]), jnp.float32)
    _, states = lax.scan(advance, start, (transfer, sources), reverse=backward)
    return states


def reference(right_sides, diagonal_blocks, lower_rows, lower_cols, lower_trans, upper_rows, upper_cols, upper_trans):
    highest = lax.Precision.HIGHEST
    sides_wide = right_sides.astype(jnp.float32)
    lower_source = jnp.einsum('kbr,kbc->krc', lower_cols.astype(jnp.float32), sides_wide, precision=highest)
    upper_source = jnp.einsum('kbr,kbc->krc', upper_cols.astype(jnp.float32), sides_wide, precision=highest)
    lower_state = carry_states(lower_trans.astype(jnp.float32), lower_source, False)
    upper_state = carry_states(upper_trans.astype(jnp.float32), upper_source, True)
    rounded = lax.optimization_barrier((lower_state.astype(jnp.bfloat16), upper_state.astype(jnp.bfloat16)))
    lower_round = rounded[0].astype(jnp.float32)
    upper_round = rounded[1].astype(jnp.float32)
    total = jnp.einsum('kab,kbc->kac', diagonal_blocks.astype(jnp.float32), sides_wide, precision=highest)
    total = total + jnp.einsum('kbr,krc->kbc', lower_rows.astype(jnp.float32), lower_round, precision=highest)
    total = total + jnp.einsum('kbr,krc->kbc', upper_rows.astype(jnp.float32), upper_round, precision=highest)
    return total.astype(jnp.bfloat16)
```

```python
import jax
import jax.numpy as jnp
from jax import lax
from jax.sharding import PartitionSpec as P


def compose(earlier, later):
    early_map, early_state = earlier
    late_map, late_state = later
    joined_map = jnp.dot(late_map, early_map, precision=lax.Precision.HIGHEST)
    joined_state = jnp.dot(late_map, early_state, precision=lax.Precision.HIGHEST) + late_state
    return (joined_map, joined_state)


def scan_enter(summary, axis, reverse):
    count = lax.axis_size(axis)
    early_map, early_state = summary
    shift = 1
    while shift < count:
        if reverse:
            pairs = [(i + shift, i) for i in range(count - shift)]
        else:
            pairs = [(i, i + shift) for i in range(count - shift)]
        last = 2 * shift >= count
        got_state = lax.ppermute(early_state, axis, pairs)
        if last:
            early_state = jnp.dot(early_map, got_state, precision=lax.Precision.HIGHEST) + early_state
        else:
            got_map = lax.ppermute(early_map, axis, pairs)
            early_map, early_state = compose((got_map, got_state), (early_map, early_state))
        shift *= 2
    if reverse:
        pairs = [(i + 1, i) for i in range(count - 1)]
    else:
        pairs = [(i, i + 1) for i in range(count - 1)]
    return lax.ppermute(early_state, axis, pairs)


def local_sweep(transfer, sources, backward):
    order_rank = transfer.shape[1]

    def advance(carry, pair):
        product_now, state_now = carry
        matrix, source = pair
        state_next = jnp.dot(matrix, state_now, precision=lax.Precision.HIGHEST) + source
        product_next = jnp.dot(matrix, product_now, precision=lax.Precision.HIGHEST)
        return ((product_next, state_next), (product_now, state_now))

    start = (
        jnp.eye(order_rank, dtype=jnp.float32),
        jnp.zeros((order_rank, sources.shape[2]), jnp.float32),
    )
    summary, entering = lax.scan(advance, start, (transfer, sources), reverse=backward)
    return (summary, entering[0], entering[1])


def shards(
    right_sides,
    diagonal_blocks,
    lower_rows,
    lower_cols,
    lower_trans,
    upper_rows,
    upper_cols,
    upper_trans,
):
    lower_source = jnp.einsum(
        "kbr,kbc->krc", lower_cols, right_sides, preferred_element_type=jnp.float32
    )
    upper_source = jnp.einsum(
        "kbr,kbc->krc", upper_cols, right_sides, preferred_element_type=jnp.float32
    )
    lower_summary, lower_prefix, lower_local = local_sweep(
        lower_trans.astype(jnp.float32), lower_source, False
    )
    upper_summary, upper_prefix, upper_local = local_sweep(
        upper_trans.astype(jnp.float32), upper_source, True
    )
    lower_enter = scan_enter(lower_summary, "row", False)
    upper_enter = scan_enter(upper_summary, "row", True)
    lower_state = lower_local + jnp.einsum(
        "kij,jc->kic", lower_prefix, lower_enter, precision=lax.Precision.HIGHEST
    )
    upper_state = upper_local + jnp.einsum(
        "kij,jc->kic", upper_prefix, upper_enter, precision=lax.Precision.HIGHEST
    )
    total = jnp.einsum(
        "kab,kbc->kac", diagonal_blocks, right_sides, preferred_element_type=jnp.float32
    )
    total = total + jnp.einsum(
        "kbr,krc->kbc",
        lower_rows,
        lower_state.astype(jnp.bfloat16),
        preferred_element_type=jnp.float32,
    )
    total = total + jnp.einsum(
        "kbr,krc->kbc",
        upper_rows,
        upper_state.astype(jnp.bfloat16),
        preferred_element_type=jnp.float32,
    )
    return total.astype(jnp.bfloat16)


def solution(mesh):
    in_specs = (
        P(("sep", "row"), None, None),
        P(("sep", "row"), None, None),
        P(("sep", "row"), None, None),
        P(("sep", "row"), None, None),
        P(("sep", "row"), None, None),
        P(("sep", "row"), None, None),
        P(("sep", "row"), None, None),
        P(("sep", "row"), None, None),
    )
    out_specs = P(("sep", "row"), None, None)
    return jax.shard_map(shards, mesh=mesh, in_specs=in_specs, out_specs=out_specs, check_vma=False)
```

```python
import jax
import jax.numpy as jnp
from jax import lax
from jax.experimental import pallas as pl
from jax.experimental.pallas import tpu as pltpu
from jax.sharding import PartitionSpec as P

F32 = jnp.float32
BF16 = jnp.bfloat16
HIGHEST = lax.Precision.HIGHEST


def split_dot(matrix, value):
    high = value.astype(BF16)
    low = (value - high.astype(F32)).astype(BF16)
    return jnp.dot(matrix, high, preferred_element_type=F32) + jnp.dot(
        matrix, low, preferred_element_type=F32
    )


def sweep_kernel(
    rhs_ref, lcols_ref, ltrans_ref, ucols_ref, utrans_ref,
    lmap_ref, lstate_ref, lsrc_ref, umap_ref, ustate_ref, usrc_ref,
):
    count = rhs_ref.shape[0]
    lmap = lstate = umap = ustate = None
    for step in range(count):
        lk = step
        uk = count - 1 - step
        lsrc = lax.dot_general(lcols_ref[lk], rhs_ref[lk], (((0,), (0,)), ((), ())), preferred_element_type=F32)
        usrc = lax.dot_general(ucols_ref[uk], rhs_ref[uk], (((0,), (0,)), ((), ())), preferred_element_type=F32)
        lsrc_ref[lk] = lsrc
        usrc_ref[uk] = usrc
        ltrans = ltrans_ref[lk]
        utrans = utrans_ref[uk]
        if step == 0:
            lstate = lsrc
            ustate = usrc
            lmap = ltrans.astype(F32)
            umap = utrans.astype(F32)
        else:
            lstate = split_dot(ltrans, lstate) + lsrc
            ustate = split_dot(utrans, ustate) + usrc
            lmap = split_dot(ltrans, lmap)
            umap = split_dot(utrans, umap)
    lmap_ref[...] = lmap
    lstate_ref[...] = lstate
    umap_ref[...] = umap
    ustate_ref[...] = ustate


def apply_kernel(
    lenter_ref, uenter_ref, ltrans_ref, utrans_ref, lsrc_ref, usrc_ref,
    diag_ref, lrows_ref, urows_ref, out_ref, lround_ref, uround_ref,
):
    count = ltrans_ref.shape[0]
    lstate = lenter_ref[...]
    ustate = uenter_ref[...]
    for step in range(count):
        lk = step
        uk = count - 1 - step
        lround_ref[lk] = lstate.astype(BF16)
        uround_ref[uk] = ustate.astype(BF16)
        if step + 1 < count:
            lstate = split_dot(ltrans_ref[lk], lstate) + lsrc_ref[lk]
            ustate = split_dot(utrans_ref[uk], ustate) + usrc_ref[uk]
    for k in range(count):
        total = diag_ref[k]
        total = total + jnp.dot(lrows_ref[k], lround_ref[k], preferred_element_type=F32)
        total = total + jnp.dot(urows_ref[k], uround_ref[k], preferred_element_type=F32)
        out_ref[k] = total.astype(out_ref.dtype)


def shifted(value, axis, count, shift, reverse):
    if reverse:
        pairs = [(i + shift, i) for i in range(count - shift)]
    else:
        pairs = [(i, i + shift) for i in range(count - shift)]
    return lax.ppermute(value, axis, pairs)


def scan_enter(summary_map, summary_state, axis, reverse):
    count = lax.axis_size(axis)
    rank = summary_map.shape[0]
    both = jnp.concatenate([summary_map, summary_state], axis=1)
    rounds = 0
    while 2 ** (rounds + 1) < count - 1:
        rounds += 1
    shift = 1
    for _ in range(rounds):
        got = shifted(both, axis, count, shift, reverse)
        joined = jnp.dot(both[:, :rank], got, precision=HIGHEST)
        both = joined + jnp.concatenate(
            [jnp.zeros_like(summary_map), both[:, rank:]], axis=1
        )
        shift *= 2
    near = shifted(both, axis, count, 1, reverse)
    far = shifted(both[:, rank:], axis, count, 1 + shift, reverse)
    return jnp.dot(near[:, :rank], far, precision=HIGHEST) + near[:, rank:]


def shards(
    right_sides,
    diagonal_blocks,
    lower_rows,
    lower_cols,
    lower_trans,
    upper_rows,
    upper_cols,
    upper_trans,
):
    count, rows, rhs = right_sides.shape
    rank = lower_trans.shape[1]
    lmap, lstate, lsrc, umap, ustate, usrc = pl.pallas_call(
        sweep_kernel,
        out_shape=(
            jax.ShapeDtypeStruct((rank, rank), F32),
            jax.ShapeDtypeStruct((rank, rhs), F32),
            jax.ShapeDtypeStruct((count, rank, rhs), F32),
            jax.ShapeDtypeStruct((rank, rank), F32),
            jax.ShapeDtypeStruct((rank, rhs), F32),
            jax.ShapeDtypeStruct((count, rank, rhs), F32),
        ),
        name="sweep",
    )(right_sides, lower_cols, lower_trans, upper_cols, upper_trans)
    diag = jnp.einsum(
        "kab,kbc->kac", diagonal_blocks, right_sides, preferred_element_type=F32
    )
    lenter = scan_enter(lmap, lstate, "row", False)
    uenter = scan_enter(umap, ustate, "row", True)
    return pl.pallas_call(
        apply_kernel,
        out_shape=jax.ShapeDtypeStruct((count, rows, rhs), BF16),
        scratch_shapes=[
            pltpu.VMEM((count, rank, rhs), BF16),
            pltpu.VMEM((count, rank, rhs), BF16),
        ],
        name="apply",
    )(lenter, uenter, lower_trans, upper_trans, lsrc, usrc, diag, lower_rows, upper_rows)


def solution(mesh):
    spec = P(("sep", "row"), None, None)
    return jax.shard_map(
        shards, mesh=mesh, in_specs=(spec,) * 8, out_specs=spec, check_vma=False
    )
```

```python
import jax
import jax.numpy as jnp
from jax import lax
from jax.experimental import pallas as pl
from jax.experimental.pallas import tpu as pltpu
from jax.sharding import PartitionSpec as P

F32 = jnp.float32
BF16 = jnp.bfloat16
HIGHEST = lax.Precision.HIGHEST


def split_dot(matrix, value):
    high = value.astype(BF16)
    low = (value - high.astype(F32)).astype(BF16)
    return jnp.dot(matrix, high, preferred_element_type=F32) + jnp.dot(
        matrix, low, preferred_element_type=F32
    )


def sweep_kernel(
    rhs_ref, lcols_ref, ltrans_ref, ucols_ref, utrans_ref,
    lmap_ref, lstate_ref, lsrc_ref, umap_ref, ustate_ref, usrc_ref,
):
    count = rhs_ref.shape[0]
    lmap = lstate = umap = ustate = None
    for step in range(count):
        lk = step
        uk = count - 1 - step
        lsrc = lax.dot_general(lcols_ref[lk], rhs_ref[lk], (((0,), (0,)), ((), ())), preferred_element_type=F32)
        usrc = lax.dot_general(ucols_ref[uk], rhs_ref[uk], (((0,), (0,)), ((), ())), preferred_element_type=F32)
        lsrc_ref[lk] = lsrc
        usrc_ref[uk] = usrc
        ltrans = ltrans_ref[lk]
        utrans = utrans_ref[uk]
        if step == 0:
            lstate = lsrc
            ustate = usrc
            lmap = ltrans.astype(F32)
            umap = utrans.astype(F32)
        else:
            lstate = split_dot(ltrans, lstate) + lsrc
            ustate = split_dot(utrans, ustate) + usrc
            lmap = split_dot(ltrans, lmap)
            umap = split_dot(utrans, umap)
    lmap_ref[...] = lmap
    lstate_ref[...] = lstate
    umap_ref[...] = umap
    ustate_ref[...] = ustate


def apply_kernel(
    lenter_ref, uenter_ref, ltrans_ref, utrans_ref, lsrc_ref, usrc_ref,
    diag_ref, lrows_ref, urows_ref, out_ref, lround_ref, uround_ref,
):
    count = ltrans_ref.shape[0]
    lstate = lenter_ref[...]
    ustate = uenter_ref[...]
    for step in range(count):
        lk = step
        uk = count - 1 - step
        lround_ref[lk] = lstate.astype(BF16)
        uround_ref[uk] = ustate.astype(BF16)
        if step + 1 < count:
            lstate = split_dot(ltrans_ref[lk], lstate) + lsrc_ref[lk]
            ustate = split_dot(utrans_ref[uk], ustate) + usrc_ref[uk]
    for k in range(count):
        total = diag_ref[k]
        total = total + jnp.dot(lrows_ref[k], lround_ref[k], preferred_element_type=F32)
        total = total + jnp.dot(urows_ref[k], uround_ref[k], preferred_element_type=F32)
        out_ref[k] = total.astype(out_ref.dtype)


def shifted(value, axis, count, shift, reverse):
    if reverse:
        pairs = [(i + shift, i) for i in range(count - shift)]
    else:
        pairs = [(i, i + shift) for i in range(count - shift)]
    return lax.ppermute(value, axis, pairs)


def scan_enter(summary_map, summary_state, axis, reverse):
    count = lax.axis_size(axis)
    rank = summary_map.shape[0]
    both = jnp.concatenate([summary_map, summary_state], axis=1)
    rounds = 0
    while 2 ** (rounds + 1) < count - 1:
        rounds += 1
    shift = 1
    for _ in range(rounds):
        got = shifted(both, axis, count, shift, reverse)
        joined = jnp.dot(both[:, :rank], got, precision=HIGHEST)
        both = joined + jnp.concatenate(
            [jnp.zeros_like(summary_map), both[:, rank:]], axis=1
        )
        shift *= 2
    near = shifted(both, axis, count, 1, reverse)
    far = shifted(both[:, rank:], axis, count, 1 + shift, reverse)
    return jnp.dot(near[:, :rank], far, precision=HIGHEST) + near[:, rank:]


def chip_shift(value, axis, chips, shift):
    pairs = [(2 * c, 2 * (c + shift)) for c in range(chips - shift)]
    pairs += [(2 * c + 1, 2 * (c - shift) + 1) for c in range(shift, chips)]
    return lax.ppermute(value, axis, pairs)


def scan_chips(lmap, lstate, umap, ustate, axis):
    count = lax.axis_size(axis)
    chips = count // 2
    rank = lmap.shape[0]
    first = lax.axis_index(axis) % 2 == 0
    lower = jnp.concatenate([lmap, lstate], axis=1)
    upper = jnp.concatenate([umap, ustate], axis=1)
    own = jnp.where(first, lower, upper)
    partner = [(2 * c, 2 * c + 1) for c in range(chips)]
    partner += [(2 * c + 1, 2 * c) for c in range(chips)]
    got = lax.ppermute(jnp.where(first, upper, lower), axis, partner)
    tail = jnp.concatenate([jnp.zeros_like(lmap), got[:, rank:]], axis=1)
    both = jnp.dot(got[:, :rank], own, precision=HIGHEST) + tail
    rounds = 0
    while 2 ** (rounds + 1) < chips - 1:
        rounds += 1
    shift = 1
    for _ in range(rounds):
        got = chip_shift(both, axis, chips, shift)
        tail = jnp.concatenate([jnp.zeros_like(lmap), both[:, rank:]], axis=1)
        both = jnp.dot(both[:, :rank], got, precision=HIGHEST) + tail
        shift *= 2
    near = chip_shift(both, axis, chips, 1)
    far = chip_shift(both[:, rank:], axis, chips, 1 + shift)
    enter = jnp.dot(near[:, :rank], far, precision=HIGHEST) + near[:, rank:]
    send = jnp.dot(own[:, :rank], enter, precision=HIGHEST) + own[:, rank:]
    other = lax.ppermute(send, axis, partner)
    return jnp.where(first, enter, other), jnp.where(first, other, enter)


def shards(
    right_sides,
    diagonal_blocks,
    lower_rows,
    lower_cols,
    lower_trans,
    upper_rows,
    upper_cols,
    upper_trans,
):
    count, rows, rhs = right_sides.shape
    rank = lower_trans.shape[1]
    lmap, lstate, lsrc, umap, ustate, usrc = pl.pallas_call(
        sweep_kernel,
        out_shape=(
            jax.ShapeDtypeStruct((rank, rank), F32),
            jax.ShapeDtypeStruct((rank, rhs), F32),
            jax.ShapeDtypeStruct((count, rank, rhs), F32),
            jax.ShapeDtypeStruct((rank, rank), F32),
            jax.ShapeDtypeStruct((rank, rhs), F32),
            jax.ShapeDtypeStruct((count, rank, rhs), F32),
        ),
        name="sweep",
    )(right_sides, lower_cols, lower_trans, upper_cols, upper_trans)
    diag = jnp.einsum(
        "kab,kbc->kac", diagonal_blocks, right_sides, preferred_element_type=F32
    )
    count_row = lax.axis_size("row")
    if count_row % 2 == 0 and count_row >= 4:
        lenter, uenter = scan_chips(lmap, lstate, umap, ustate, "row")
    else:
        lenter = scan_enter(lmap, lstate, "row", False)
        uenter = scan_enter(umap, ustate, "row", True)
    return pl.pallas_call(
        apply_kernel,
        out_shape=jax.ShapeDtypeStruct((count, rows, rhs), BF16),
        scratch_shapes=[
            pltpu.VMEM((count, rank, rhs), BF16),
            pltpu.VMEM((count, rank, rhs), BF16),
        ],
        name="apply",
    )(lenter, uenter, lower_trans, upper_trans, lsrc, usrc, diag, lower_rows, upper_rows)


def solution(mesh):
    spec = P(("sep", "row"), None, None)
    return jax.shard_map(
        shards, mesh=mesh, in_specs=(spec,) * 8, out_specs=spec, check_vma=False
    )
```

```python
import jax
import jax.numpy as jnp
from jax import lax
from jax.experimental import pallas as pl
from jax.experimental.pallas import tpu as pltpu
from jax.sharding import PartitionSpec as P

F32 = jnp.float32
BF16 = jnp.bfloat16
HIGHEST = lax.Precision.HIGHEST


def split_dot(matrix, value):
    high = value.astype(BF16)
    low = (value - high.astype(F32)).astype(BF16)
    return jnp.dot(matrix, high, preferred_element_type=F32) + jnp.dot(
        matrix, low, preferred_element_type=F32
    )


def sweep_kernel(
    rhs_ref, lcols_ref, ltrans_ref, ucols_ref, utrans_ref,
    lmap_ref, lstate_ref, lsrc_ref, umap_ref, ustate_ref, usrc_ref,
):
    count = rhs_ref.shape[0]
    lmap = lstate = umap = ustate = None
    for step in range(count):
        lk = step
        uk = count - 1 - step
        lsrc = lax.dot_general(lcols_ref[lk], rhs_ref[lk], (((0,), (0,)), ((), ())), preferred_element_type=F32)
        usrc = lax.dot_general(ucols_ref[uk], rhs_ref[uk], (((0,), (0,)), ((), ())), preferred_element_type=F32)
        lsrc_ref[lk] = lsrc
        usrc_ref[uk] = usrc
        ltrans = ltrans_ref[lk]
        utrans = utrans_ref[uk]
        if step == 0:
            lstate = lsrc
            ustate = usrc
            lmap = ltrans.astype(F32)
            umap = utrans.astype(F32)
        else:
            lstate = split_dot(ltrans, lstate) + lsrc
            ustate = split_dot(utrans, ustate) + usrc
            lmap = split_dot(ltrans, lmap)
            umap = split_dot(utrans, umap)
    lmap_ref[...] = lmap
    lstate_ref[...] = lstate
    umap_ref[...] = umap
    ustate_ref[...] = ustate


def apply_kernel(
    lenter_ref, uenter_ref, ltrans_ref, utrans_ref, lsrc_ref, usrc_ref,
    diag_ref, lrows_ref, urows_ref, out_ref, lround_ref, uround_ref,
):
    count = ltrans_ref.shape[0]
    lstate = lenter_ref[...]
    ustate = uenter_ref[...]
    for step in range(count):
        lk = step
        uk = count - 1 - step
        lround_ref[lk] = lstate.astype(BF16)
        uround_ref[uk] = ustate.astype(BF16)
        if step + 1 < count:
            lstate = split_dot(ltrans_ref[lk], lstate) + lsrc_ref[lk]
            ustate = split_dot(utrans_ref[uk], ustate) + usrc_ref[uk]
    for k in range(count):
        total = diag_ref[k]
        total = total + jnp.dot(lrows_ref[k], lround_ref[k], preferred_element_type=F32)
        total = total + jnp.dot(urows_ref[k], uround_ref[k], preferred_element_type=F32)
        out_ref[k] = total.astype(out_ref.dtype)


def shifted(value, axis, count, shift, reverse):
    if reverse:
        pairs = [(i + shift, i) for i in range(count - shift)]
    else:
        pairs = [(i, i + shift) for i in range(count - shift)]
    return lax.ppermute(value, axis, pairs)


def scan_enter(summary_map, summary_state, axis, reverse):
    count = lax.axis_size(axis)
    rank = summary_map.shape[0]
    both = jnp.concatenate([summary_map, summary_state], axis=1)
    rounds = 0
    while 2 ** (rounds + 1) < count - 1:
        rounds += 1
    shift = 1
    for _ in range(rounds):
        got = shifted(both, axis, count, shift, reverse)
        joined = jnp.dot(both[:, :rank], got, precision=HIGHEST)
        both = joined + jnp.concatenate(
            [jnp.zeros_like(summary_map), both[:, rank:]], axis=1
        )
        shift *= 2
    near = shifted(both, axis, count, 1, reverse)
    far = shifted(both[:, rank:], axis, count, 1 + shift, reverse)
    return jnp.dot(near[:, :rank], far, precision=HIGHEST) + near[:, rank:]


def chip_shift(value, axis, chips, shift):
    pairs = [(2 * c, 2 * (c + shift)) for c in range(chips - shift)]
    pairs += [(2 * c + 1, 2 * (c - shift) + 1) for c in range(shift, chips)]
    width = value.shape[1]
    piece = 128 if width % 128 == 0 else width
    parts = [
        lax.ppermute(value[:, i : i + piece], axis, pairs)
        for i in range(0, width, piece)
    ]
    return parts[0] if len(parts) == 1 else jnp.concatenate(parts, axis=1)


def scan_chips(lmap, lstate, umap, ustate, axis):
    count = lax.axis_size(axis)
    chips = count // 2
    rank = lmap.shape[0]
    first = lax.axis_index(axis) % 2 == 0
    lower = jnp.concatenate([lmap, lstate], axis=1)
    upper = jnp.concatenate([umap, ustate], axis=1)
    own = jnp.where(first, lower, upper)
    partner = [(2 * c, 2 * c + 1) for c in range(chips)]
    partner += [(2 * c + 1, 2 * c) for c in range(chips)]
    got = lax.ppermute(jnp.where(first, upper, lower), axis, partner)
    tail = jnp.concatenate([jnp.zeros_like(lmap), got[:, rank:]], axis=1)
    both = jnp.dot(got[:, :rank], own, precision=HIGHEST) + tail
    rounds = 0
    while 2 ** (rounds + 1) < chips - 1:
        rounds += 1
    shift = 1
    for _ in range(rounds):
        got = chip_shift(both, axis, chips, shift)
        tail = jnp.concatenate([jnp.zeros_like(lmap), both[:, rank:]], axis=1)
        both = jnp.dot(both[:, :rank], got, precision=HIGHEST) + tail
        shift *= 2
    near = chip_shift(both, axis, chips, 1)
    far = chip_shift(both[:, rank:], axis, chips, 1 + shift)
    enter = jnp.dot(near[:, :rank], far, precision=HIGHEST) + near[:, rank:]
    send = jnp.dot(own[:, :rank], enter, precision=HIGHEST) + own[:, rank:]
    other = lax.ppermute(send, axis, partner)
    return jnp.where(first, enter, other), jnp.where(first, other, enter)


def shards(
    right_sides,
    diagonal_blocks,
    lower_rows,
    lower_cols,
    lower_trans,
    upper_rows,
    upper_cols,
    upper_trans,
):
    count, rows, rhs = right_sides.shape
    rank = lower_trans.shape[1]
    lmap, lstate, lsrc, umap, ustate, usrc = pl.pallas_call(
        sweep_kernel,
        out_shape=(
            jax.ShapeDtypeStruct((rank, rank), F32),
            jax.ShapeDtypeStruct((rank, rhs), F32),
            jax.ShapeDtypeStruct((count, rank, rhs), F32),
            jax.ShapeDtypeStruct((rank, rank), F32),
            jax.ShapeDtypeStruct((rank, rhs), F32),
            jax.ShapeDtypeStruct((count, rank, rhs), F32),
        ),
        name="sweep",
    )(right_sides, lower_cols, lower_trans, upper_cols, upper_trans)
    diag = jnp.einsum(
        "kab,kbc->kac", diagonal_blocks, right_sides, preferred_element_type=F32
    )
    count_row = lax.axis_size("row")
    if count_row % 2 == 0 and count_row >= 4:
        lenter, uenter = scan_chips(lmap, lstate, umap, ustate, "row")
    else:
        lenter = scan_enter(lmap, lstate, "row", False)
        uenter = scan_enter(umap, ustate, "row", True)
    return pl.pallas_call(
        apply_kernel,
        out_shape=jax.ShapeDtypeStruct((count, rows, rhs), BF16),
        scratch_shapes=[
            pltpu.VMEM((count, rank, rhs), BF16),
            pltpu.VMEM((count, rank, rhs), BF16),
        ],
        name="apply",
    )(lenter, uenter, lower_trans, upper_trans, lsrc, usrc, diag, lower_rows, upper_rows)


def solution(mesh):
    spec = P(("sep", "row"), None, None)
    return jax.shard_map(
        shards, mesh=mesh, in_specs=(spec,) * 8, out_specs=spec, check_vma=False
    )
```

```python
import jax
import jax.numpy as jnp
from jax import lax
from jax.experimental import pallas as pl
from jax.experimental.pallas import tpu as pltpu
from jax.sharding import PartitionSpec as P

F32 = jnp.float32
BF16 = jnp.bfloat16
HIGHEST = lax.Precision.HIGHEST


def split_dot(matrix, value):
    high = value.astype(BF16)
    low = (value - high.astype(F32)).astype(BF16)
    return jnp.dot(matrix, high, preferred_element_type=F32) + jnp.dot(
        matrix, low, preferred_element_type=F32
    )


def sweep_kernel(
    rhs_ref, lcols_ref, ltrans_ref, ucols_ref, utrans_ref,
    lmap_ref, lstate_ref, lsrc_ref, umap_ref, ustate_ref, usrc_ref,
):
    count = rhs_ref.shape[0]
    lmap = lstate = umap = ustate = None
    for step in range(count):
        lk = step
        uk = count - 1 - step
        lsrc = lax.dot_general(lcols_ref[lk], rhs_ref[lk], (((0,), (0,)), ((), ())), preferred_element_type=F32)
        usrc = lax.dot_general(ucols_ref[uk], rhs_ref[uk], (((0,), (0,)), ((), ())), preferred_element_type=F32)
        lsrc_ref[lk] = lsrc
        usrc_ref[uk] = usrc
        ltrans = ltrans_ref[lk]
        utrans = utrans_ref[uk]
        if step == 0:
            lstate = lsrc
            ustate = usrc
            lmap = ltrans.astype(F32)
            umap = utrans.astype(F32)
        else:
            lstate = split_dot(ltrans, lstate) + lsrc
            ustate = split_dot(utrans, ustate) + usrc
            lmap = split_dot(ltrans, lmap)
            umap = split_dot(utrans, umap)
    lmap_ref[...] = lmap
    lstate_ref[...] = lstate
    umap_ref[...] = umap
    ustate_ref[...] = ustate


def apply_kernel(
    lenter_ref, uenter_ref, ltrans_ref, utrans_ref, lsrc_ref, usrc_ref,
    diag_ref, lrows_ref, urows_ref, out_ref, lround_ref, uround_ref,
):
    count = ltrans_ref.shape[0]
    lstate = lenter_ref[...]
    ustate = uenter_ref[...]
    for step in range(count):
        lk = step
        uk = count - 1 - step
        lround_ref[lk] = lstate.astype(BF16)
        uround_ref[uk] = ustate.astype(BF16)
        if step + 1 < count:
            lstate = split_dot(ltrans_ref[lk], lstate) + lsrc_ref[lk]
            ustate = split_dot(utrans_ref[uk], ustate) + usrc_ref[uk]
    for k in range(count):
        total = diag_ref[k]
        total = total + jnp.dot(lrows_ref[k], lround_ref[k], preferred_element_type=F32)
        total = total + jnp.dot(urows_ref[k], uround_ref[k], preferred_element_type=F32)
        out_ref[k] = total.astype(out_ref.dtype)


def shifted(value, axis, count, shift, reverse):
    if reverse:
        pairs = [(i + shift, i) for i in range(count - shift)]
    else:
        pairs = [(i, i + shift) for i in range(count - shift)]
    return lax.ppermute(value, axis, pairs)


def scan_enter(summary_map, summary_state, axis, reverse):
    count = lax.axis_size(axis)
    rank = summary_map.shape[0]
    both = jnp.concatenate([summary_map, summary_state], axis=1)
    rounds = 0
    while 2 ** (rounds + 1) < count - 1:
        rounds += 1
    shift = 1
    for _ in range(rounds):
        got = shifted(both, axis, count, shift, reverse)
        joined = jnp.dot(both[:, :rank], got, precision=HIGHEST)
        both = joined + jnp.concatenate(
            [jnp.zeros_like(summary_map), both[:, rank:]], axis=1
        )
        shift *= 2
    near = shifted(both, axis, count, 1, reverse)
    far = shifted(both[:, rank:], axis, count, 1 + shift, reverse)
    return jnp.dot(near[:, :rank], far, precision=HIGHEST) + near[:, rank:]


def chip_shift(value, axis, chips, shift):
    pairs = [(2 * c, 2 * (c + shift)) for c in range(chips - shift)]
    pairs += [(2 * c + 1, 2 * (c - shift) + 1) for c in range(shift, chips)]
    return lax.ppermute(value, axis, pairs)


def scan_chips(lmap, lstate, umap, ustate, axis):
    count = lax.axis_size(axis)
    chips = count // 2
    rank = lmap.shape[0]
    first = lax.axis_index(axis) % 2 == 0
    lower = jnp.concatenate([lmap, lstate], axis=1)
    upper = jnp.concatenate([umap, ustate], axis=1)
    own = jnp.where(first, lower, upper)
    partner = [(2 * c, 2 * c + 1) for c in range(chips)]
    partner += [(2 * c + 1, 2 * c) for c in range(chips)]
    got = lax.ppermute(jnp.where(first, upper, lower), axis, partner)
    tail = jnp.concatenate([jnp.zeros_like(lmap), got[:, rank:]], axis=1)
    both = jnp.dot(got[:, :rank], own, precision=HIGHEST) + tail
    if chips <= 8:
        out = both[:, rank:]
        for step in range(chips - 1):
            enter = chip_shift(out, axis, chips, 1)
            if step + 2 < chips:
                out = jnp.dot(both[:, :rank], enter, precision=HIGHEST) + both[:, rank:]
    else:
        rounds = 0
        while 2 ** (rounds + 1) < chips - 1:
            rounds += 1
        shift = 1
        for _ in range(rounds):
            got = chip_shift(both, axis, chips, shift)
            tail = jnp.concatenate([jnp.zeros_like(lmap), both[:, rank:]], axis=1)
            both = jnp.dot(both[:, :rank], got, precision=HIGHEST) + tail
            shift *= 2
        near = chip_shift(both, axis, chips, 1)
        far = chip_shift(both[:, rank:], axis, chips, 1 + shift)
        enter = jnp.dot(near[:, :rank], far, precision=HIGHEST) + near[:, rank:]
    send = jnp.dot(own[:, :rank], enter, precision=HIGHEST) + own[:, rank:]
    other = lax.ppermute(send, axis, partner)
    return jnp.where(first, enter, other), jnp.where(first, other, enter)


def shards(
    right_sides,
    diagonal_blocks,
    lower_rows,
    lower_cols,
    lower_trans,
    upper_rows,
    upper_cols,
    upper_trans,
):
    count, rows, rhs = right_sides.shape
    rank = lower_trans.shape[1]
    lmap, lstate, lsrc, umap, ustate, usrc = pl.pallas_call(
        sweep_kernel,
        out_shape=(
            jax.ShapeDtypeStruct((rank, rank), F32),
            jax.ShapeDtypeStruct((rank, rhs), F32),
            jax.ShapeDtypeStruct((count, rank, rhs), F32),
            jax.ShapeDtypeStruct((rank, rank), F32),
            jax.ShapeDtypeStruct((rank, rhs), F32),
            jax.ShapeDtypeStruct((count, rank, rhs), F32),
        ),
        name="sweep",
    )(right_sides, lower_cols, lower_trans, upper_cols, upper_trans)
    diag = jnp.einsum(
        "kab,kbc->kac", diagonal_blocks, right_sides, preferred_element_type=F32
    )
    count_row = lax.axis_size("row")
    if count_row % 2 == 0 and count_row >= 4:
        lenter, uenter = scan_chips(lmap, lstate, umap, ustate, "row")
    else:
        lenter = scan_enter(lmap, lstate, "row", False)
        uenter = scan_enter(umap, ustate, "row", True)
    return pl.pallas_call(
        apply_kernel,
        out_shape=jax.ShapeDtypeStruct((count, rows, rhs), BF16),
        scratch_shapes=[
            pltpu.VMEM((count, rank, rhs), BF16),
            pltpu.VMEM((count, rank, rhs), BF16),
        ],
        name="apply",
    )(lenter, uenter, lower_trans, upper_trans, lsrc, usrc, diag, lower_rows, upper_rows)


def solution(mesh):
    spec = P(("sep", "row"), None, None)
    return jax.shard_map(
        shards, mesh=mesh, in_specs=(spec,) * 8, out_specs=spec, check_vma=False
    )
```

```python
import jax
import jax.numpy as jnp
from jax import lax
from jax.experimental import pallas as pl
from jax.experimental.pallas import tpu as pltpu
from jax.sharding import PartitionSpec as P

F32 = jnp.float32
BF16 = jnp.bfloat16
HIGHEST = lax.Precision.HIGHEST


def split_dot(matrix, value):
    high = value.astype(BF16)
    low = (value - high.astype(F32)).astype(BF16)
    return jnp.dot(matrix, high, preferred_element_type=F32) + jnp.dot(
        matrix, low, preferred_element_type=F32
    )


def sweep_kernel(
    rhs_ref, lcols_ref, ltrans_ref, ucols_ref, utrans_ref,
    lmap_ref, lsrc_ref, umap_ref, usrc_ref,
):
    count = rhs_ref.shape[0]
    lmap = lstate = umap = ustate = None
    for step in range(count):
        lk = step
        uk = count - 1 - step
        lsrc = lax.dot_general(lcols_ref[lk], rhs_ref[lk], (((0,), (0,)), ((), ())), preferred_element_type=F32)
        usrc = lax.dot_general(ucols_ref[uk], rhs_ref[uk], (((0,), (0,)), ((), ())), preferred_element_type=F32)
        lsrc_ref[lk] = lsrc
        usrc_ref[uk] = usrc
        ltrans = ltrans_ref[lk]
        utrans = utrans_ref[uk]
        if step == 0:
            lstate = lsrc
            ustate = usrc
            lmap = ltrans.astype(F32)
            umap = utrans.astype(F32)
        else:
            lstate = split_dot(ltrans, lstate) + lsrc
            ustate = split_dot(utrans, ustate) + usrc
            lmap = split_dot(ltrans, lmap)
            umap = split_dot(utrans, umap)
    rank = lmap.shape[0]
    lmap_ref[:, :rank] = lmap
    lmap_ref[:, rank:] = lstate
    umap_ref[:, :rank] = umap
    umap_ref[:, rank:] = ustate


def apply_kernel(
    flag_ref, enter_ref, other_ref, ltrans_ref, utrans_ref, lsrc_ref, usrc_ref,
    diag_ref, lrows_ref, urows_ref, out_ref, lround_ref, uround_ref,
):
    count = ltrans_ref.shape[0]
    first = flag_ref[0] == 0
    lstate = jnp.where(first, enter_ref[...], other_ref[...])
    ustate = jnp.where(first, other_ref[...], enter_ref[...])
    for step in range(count):
        lk = step
        uk = count - 1 - step
        lround_ref[lk] = lstate.astype(BF16)
        uround_ref[uk] = ustate.astype(BF16)
        if step + 1 < count:
            lstate = split_dot(ltrans_ref[lk], lstate) + lsrc_ref[lk]
            ustate = split_dot(utrans_ref[uk], ustate) + usrc_ref[uk]
    for k in range(count):
        total = diag_ref[k]
        total = total + jnp.dot(lrows_ref[k], lround_ref[k], preferred_element_type=F32)
        total = total + jnp.dot(urows_ref[k], uround_ref[k], preferred_element_type=F32)
        out_ref[k] = total.astype(out_ref.dtype)


def shifted(value, axis, count, shift, reverse):
    if reverse:
        pairs = [(i + shift, i) for i in range(count - shift)]
    else:
        pairs = [(i, i + shift) for i in range(count - shift)]
    return lax.ppermute(value, axis, pairs)


def scan_enter(summary_map, summary_state, axis, reverse):
    count = lax.axis_size(axis)
    rank = summary_map.shape[0]
    both = jnp.concatenate([summary_map, summary_state], axis=1)
    rounds = 0
    while 2 ** (rounds + 1) < count - 1:
        rounds += 1
    shift = 1
    for _ in range(rounds):
        got = shifted(both, axis, count, shift, reverse)
        joined = jnp.dot(both[:, :rank], got, precision=HIGHEST)
        both = joined + jnp.concatenate(
            [jnp.zeros_like(summary_map), both[:, rank:]], axis=1
        )
        shift *= 2
    near = shifted(both, axis, count, 1, reverse)
    far = shifted(both[:, rank:], axis, count, 1 + shift, reverse)
    return jnp.dot(near[:, :rank], far, precision=HIGHEST) + near[:, rank:]


def chip_shift(value, axis, chips, shift):
    pairs = [(2 * c, 2 * (c + shift)) for c in range(chips - shift)]
    pairs += [(2 * c + 1, 2 * (c - shift) + 1) for c in range(shift, chips)]
    return lax.ppermute(value, axis, pairs)


def scan_chips(lower, upper, axis):
    count = lax.axis_size(axis)
    chips = count // 2
    rank = lower.shape[0]
    first = lax.axis_index(axis) % 2 == 0
    own = jnp.where(first, lower, upper)
    partner = [(2 * c, 2 * c + 1) for c in range(chips)]
    partner += [(2 * c + 1, 2 * c) for c in range(chips)]
    got = lax.ppermute(jnp.where(first, upper, lower), axis, partner)
    tail = jnp.concatenate([jnp.zeros((rank, rank), F32), got[:, rank:]], axis=1)
    both = jnp.dot(got[:, :rank], own, precision=HIGHEST) + tail
    rounds = 0
    while 2 ** (rounds + 1) < chips - 1:
        rounds += 1
    shift = 1
    for _ in range(rounds):
        got = chip_shift(both, axis, chips, shift)
        tail = jnp.concatenate([jnp.zeros((rank, rank), F32), both[:, rank:]], axis=1)
        both = jnp.dot(both[:, :rank], got, precision=HIGHEST) + tail
        shift *= 2
    near = chip_shift(both, axis, chips, 1)
    far = chip_shift(both[:, rank:], axis, chips, 1 + shift)
    enter = jnp.dot(near[:, :rank], far, precision=HIGHEST) + near[:, rank:]
    send = jnp.dot(own[:, :rank], enter, precision=HIGHEST) + own[:, rank:]
    other = lax.ppermute(send, axis, partner)
    return enter, other


def shards(
    right_sides,
    diagonal_blocks,
    lower_rows,
    lower_cols,
    lower_trans,
    upper_rows,
    upper_cols,
    upper_trans,
):
    count, rows, rhs = right_sides.shape
    rank = lower_trans.shape[1]
    lboth, lsrc, uboth, usrc = pl.pallas_call(
        sweep_kernel,
        out_shape=(
            jax.ShapeDtypeStruct((rank, rank + rhs), F32),
            jax.ShapeDtypeStruct((count, rank, rhs), F32),
            jax.ShapeDtypeStruct((rank, rank + rhs), F32),
            jax.ShapeDtypeStruct((count, rank, rhs), F32),
        ),
        name="sweep",
    )(right_sides, lower_cols, lower_trans, upper_cols, upper_trans)
    diag = jnp.einsum(
        "kab,kbc->kac", diagonal_blocks, right_sides, preferred_element_type=F32
    )
    count_row = lax.axis_size("row")
    if count_row % 2 == 0 and count_row >= 4:
        enter, other = scan_chips(lboth, uboth, "row")
        flag = jnp.full((1,), lax.axis_index("row") % 2, jnp.int32)
    else:
        enter = scan_enter(lboth[:, :rank], lboth[:, rank:], "row", False)
        other = scan_enter(uboth[:, :rank], uboth[:, rank:], "row", True)
        flag = jnp.zeros((1,), jnp.int32)
    vmem = pl.BlockSpec(memory_space=pltpu.VMEM)
    return pl.pallas_call(
        apply_kernel,
        out_shape=jax.ShapeDtypeStruct((count, rows, rhs), BF16),
        scratch_shapes=[
            pltpu.VMEM((count, rank, rhs), BF16),
            pltpu.VMEM((count, rank, rhs), BF16),
        ],
        in_specs=[pl.BlockSpec(memory_space=pltpu.SMEM)] + [vmem] * 9,
        name="apply",
    )(flag, enter, other, lower_trans, upper_trans, lsrc, usrc, diag, lower_rows, upper_rows)


def solution(mesh):
    spec = P(("sep", "row"), None, None)
    return jax.shard_map(
        shards, mesh=mesh, in_specs=(spec,) * 8, out_specs=spec, check_vma=False
    )
```

```python
import jax
import jax.numpy as jnp
from jax import lax
from jax.experimental import pallas as pl
from jax.experimental.pallas import tpu as pltpu
from jax.sharding import PartitionSpec as P

F32 = jnp.float32
BF16 = jnp.bfloat16
HIGHEST = lax.Precision.HIGHEST


def split_dot(matrix, value):
    high = value.astype(BF16)
    low = (value - high.astype(F32)).astype(BF16)
    return jnp.dot(matrix, high, preferred_element_type=F32) + jnp.dot(
        matrix, low, preferred_element_type=F32
    )


def split(value):
    high = value.astype(BF16)
    return high, (value - high.astype(F32)).astype(BF16)


def wide_dot(left, right):
    left_high, left_low = split(left)
    right_high, right_low = split(right)
    total = jnp.dot(left_high, right_high, preferred_element_type=F32)
    total = total + jnp.dot(left_high, right_low, preferred_element_type=F32)
    return total + jnp.dot(left_low, right_high, preferred_element_type=F32)


def tree_product(factors):
    level = [
        jnp.dot(factors[i], factors[i + 1], preferred_element_type=F32)
        if i + 1 < len(factors)
        else factors[i].astype(F32)
        for i in range(0, len(factors), 2)
    ]
    while len(level) > 1:
        level = [
            wide_dot(level[i], level[i + 1]) if i + 1 < len(level) else level[i]
            for i in range(0, len(level), 2)
        ]
    return level[0]


def sweep_kernel(
    flag_ref, rhs_ref, lcols_ref, ltrans_ref, ucols_ref, utrans_ref, diag_ref,
    own_ref, give_ref, lsrc_ref, usrc_ref, dprod_ref,
):
    count = rhs_ref.shape[0]
    lstate = ustate = None
    for step in range(count):
        lk = step
        uk = count - 1 - step
        lsrc = lax.dot_general(lcols_ref[lk], rhs_ref[lk], (((0,), (0,)), ((), ())), preferred_element_type=F32)
        usrc = lax.dot_general(ucols_ref[uk], rhs_ref[uk], (((0,), (0,)), ((), ())), preferred_element_type=F32)
        lsrc_ref[lk] = lsrc
        usrc_ref[uk] = usrc
        if step == 0:
            lstate = lsrc
            ustate = usrc
        else:
            lstate = split_dot(ltrans_ref[lk], lstate) + lsrc
            ustate = split_dot(utrans_ref[uk], ustate) + usrc
    lmap = tree_product([ltrans_ref[k] for k in reversed(range(count))])
    umap = tree_product([utrans_ref[k] for k in range(count)])
    for k in range(count):
        dprod_ref[k] = jnp.dot(diag_ref[k], rhs_ref[k], preferred_element_type=F32)
    rank = lmap.shape[0]
    first = flag_ref[0] == 0

    @pl.when(first)
    def _():
        own_ref[:, :rank] = lmap
        own_ref[:, rank:] = lstate
        give_ref[:, :rank] = umap
        give_ref[:, rank:] = ustate

    @pl.when(jnp.logical_not(first))
    def _():
        own_ref[:, :rank] = umap
        own_ref[:, rank:] = ustate
        give_ref[:, :rank] = lmap
        give_ref[:, rank:] = lstate


def apply_kernel(
    flag_ref, enter_ref, other_ref, ltrans_ref, utrans_ref, lsrc_ref, usrc_ref,
    diag_ref, lrows_ref, urows_ref, out_ref,
):
    count = ltrans_ref.shape[0]
    first = flag_ref[0] == 0
    lstate = jnp.where(first, enter_ref[...], other_ref[...])
    ustate = jnp.where(first, other_ref[...], enter_ref[...])
    lround = [None] * count
    uround = [None] * count

    def finish(k):
        total = diag_ref[k]
        total = total + jnp.dot(lrows_ref[k], lround[k], preferred_element_type=F32)
        total = total + jnp.dot(urows_ref[k], uround[k], preferred_element_type=F32)
        out_ref[k] = total.astype(out_ref.dtype)

    for step in range(count):
        lk = step
        uk = count - 1 - step
        lround[lk] = lstate.astype(BF16)
        uround[uk] = ustate.astype(BF16)
        if uround[lk] is not None:
            finish(lk)
        if uk != lk and lround[uk] is not None:
            finish(uk)
        if step + 1 < count:
            lstate = split_dot(ltrans_ref[lk], lstate) + lsrc_ref[lk]
            ustate = split_dot(utrans_ref[uk], ustate) + usrc_ref[uk]


def chip_shift(value, axis, chips, shift):
    pairs = [(2 * c, 2 * (c + shift)) for c in range(chips - shift)]
    pairs += [(2 * c + 1, 2 * (c - shift) + 1) for c in range(shift, chips)]
    return lax.ppermute(value, axis, pairs)


def scan_chips(own, give, axis):
    count = lax.axis_size(axis)
    chips = count // 2
    rank = own.shape[0]
    partner = [(2 * c, 2 * c + 1) for c in range(chips)]
    partner += [(2 * c + 1, 2 * c) for c in range(chips)]
    got = lax.ppermute(give, axis, partner)
    tail = jnp.concatenate([jnp.zeros((rank, rank), F32), got[:, rank:]], axis=1)
    both = jnp.dot(got[:, :rank], own, precision=HIGHEST) + tail
    rounds = 0
    while 2 ** (rounds + 1) < chips - 1:
        rounds += 1
    shift = 1
    for _ in range(rounds):
        got = chip_shift(both, axis, chips, shift)
        tail = jnp.concatenate([jnp.zeros((rank, rank), F32), both[:, rank:]], axis=1)
        both = jnp.dot(both[:, :rank], got, precision=HIGHEST) + tail
        shift *= 2
    near = chip_shift(both, axis, chips, 1)
    far = chip_shift(both[:, rank:], axis, chips, 1 + shift)
    enter = jnp.dot(near[:, :rank], far, precision=HIGHEST) + near[:, rank:]
    send = jnp.dot(own[:, :rank], enter, precision=HIGHEST) + own[:, rank:]
    other = lax.ppermute(send, axis, partner)
    return enter, other


def shards(
    right_sides,
    diagonal_blocks,
    lower_rows,
    lower_cols,
    lower_trans,
    upper_rows,
    upper_cols,
    upper_trans,
):
    count, rows, rhs = right_sides.shape
    rank = lower_trans.shape[1]
    count_row = lax.axis_size("row")
    chip_scan = count_row % 2 == 0 and count_row >= 4
    if chip_scan:
        flag = jnp.full((1,), lax.axis_index("row") % 2, jnp.int32)
    else:
        flag = jnp.zeros((1,), jnp.int32)
    vmem = pl.BlockSpec(memory_space=pltpu.VMEM)
    smem = pl.BlockSpec(memory_space=pltpu.SMEM)
    own, give, lsrc, usrc, diag = pl.pallas_call(
        sweep_kernel,
        out_shape=(
            jax.ShapeDtypeStruct((rank, rank + rhs), F32),
            jax.ShapeDtypeStruct((rank, rank + rhs), F32),
            jax.ShapeDtypeStruct((count, rank, rhs), F32),
            jax.ShapeDtypeStruct((count, rank, rhs), F32),
            jax.ShapeDtypeStruct((count, rows, rhs), F32),
        ),
        in_specs=[smem] + [vmem] * 6,
        name="sweep",
    )(flag, right_sides, lower_cols, lower_trans, upper_cols, upper_trans, diagonal_blocks)
    if chip_scan:
        enter, other = scan_chips(own, give, "row")
    else:
        enter = scan_enter(own[:, :rank], own[:, rank:], "row", False)
        other = scan_enter(give[:, :rank], give[:, rank:], "row", True)
    return pl.pallas_call(
        apply_kernel,
        out_shape=jax.ShapeDtypeStruct((count, rows, rhs), BF16),
        in_specs=[smem] + [vmem] * 9,
        name="apply",
    )(flag, enter, other, lower_trans, upper_trans, lsrc, usrc, diag, lower_rows, upper_rows)


def solution(mesh):
    spec = P(("sep", "row"), None, None)
    return jax.shard_map(
        shards, mesh=mesh, in_specs=(spec,) * 8, out_specs=spec, check_vma=False
    )
```

```python
import jax
import jax.numpy as jnp
from jax import lax
from jax.experimental import pallas as pl
from jax.experimental.pallas import tpu as pltpu
from jax.sharding import PartitionSpec as P

F32 = jnp.float32
BF16 = jnp.bfloat16
HIGHEST = lax.Precision.HIGHEST


def split_dot(matrix, value):
    high = value.astype(BF16)
    low = (value - high.astype(F32)).astype(BF16)
    return jnp.dot(matrix, high, preferred_element_type=F32) + jnp.dot(
        matrix, low, preferred_element_type=F32
    )


def sweep_kernel(
    rhs_ref, lcols_ref, ltrans_ref, ucols_ref, utrans_ref,
    lmap_ref, lsrc_ref, umap_ref, usrc_ref,
):
    count = rhs_ref.shape[0]
    lmap = lstate = umap = ustate = None
    for step in range(count):
        lk = step
        uk = count - 1 - step
        lsrc = lax.dot_general(lcols_ref[lk], rhs_ref[lk], (((0,), (0,)), ((), ())), preferred_element_type=F32)
        usrc = lax.dot_general(ucols_ref[uk], rhs_ref[uk], (((0,), (0,)), ((), ())), preferred_element_type=F32)
        lsrc_ref[lk] = lsrc
        usrc_ref[uk] = usrc
        ltrans = ltrans_ref[lk]
        utrans = utrans_ref[uk]
        if step == 0:
            lstate = lsrc
            ustate = usrc
            lmap = ltrans.astype(F32)
            umap = utrans.astype(F32)
        else:
            lstate = split_dot(ltrans, lstate) + lsrc
            ustate = split_dot(utrans, ustate) + usrc
            lmap = split_dot(ltrans, lmap)
            umap = split_dot(utrans, umap)
    rank = lmap.shape[0]
    lmap_ref[:, :rank] = lmap
    lmap_ref[:, rank:] = lstate
    umap_ref[:, :rank] = umap
    umap_ref[:, rank:] = ustate


def apply_kernel(
    flag_ref, enter_ref, other_ref, ltrans_hbm, utrans_hbm, lsrc_hbm, usrc_hbm,
    diag_hbm, lrows_hbm, urows_hbm, out_ref,
    ltrans_ref, utrans_ref, lsrc_ref, usrc_ref, diag_ref, lrows_ref, urows_ref, sems,
):
    count = ltrans_ref.shape[0]
    sources = (ltrans_hbm, utrans_hbm, lsrc_hbm, usrc_hbm, diag_hbm, lrows_hbm, urows_hbm)
    targets = (ltrans_ref, utrans_ref, lsrc_ref, usrc_ref, diag_ref, lrows_ref, urows_ref)
    copies = [
        [pltpu.make_async_copy(sources[a].at[k], targets[a].at[k], sems.at[a, k]) for k in range(count)]
        for a in range(len(sources))
    ]
    order = []
    for step in range(count):
        order += [(0, step), (2, step), (1, count - 1 - step), (3, count - 1 - step)]
    for step in range(count):
        for k in sorted({step, count - 1 - step}):
            if max(k, count - 1 - k) == step:
                order += [(4, k), (5, k), (6, k)]
    for a, k in order:
        copies[a][k].start()

    def ready(a, k):
        copies[a][k].wait()
        return targets[a][k]

    first = flag_ref[0] == 0
    lstate = jnp.where(first, enter_ref[...], other_ref[...])
    ustate = jnp.where(first, other_ref[...], enter_ref[...])
    lround = [None] * count
    uround = [None] * count

    def finish(k):
        total = ready(4, k)
        total = total + jnp.dot(ready(5, k), lround[k], preferred_element_type=F32)
        total = total + jnp.dot(ready(6, k), uround[k], preferred_element_type=F32)
        out_ref[k] = total.astype(out_ref.dtype)

    for step in range(count):
        lk = step
        uk = count - 1 - step
        lround[lk] = lstate.astype(BF16)
        uround[uk] = ustate.astype(BF16)
        if uround[lk] is not None:
            finish(lk)
        if uk != lk and lround[uk] is not None:
            finish(uk)
        if step + 1 < count:
            lstate = split_dot(ready(0, lk), lstate) + ready(2, lk)
            ustate = split_dot(ready(1, uk), ustate) + ready(3, uk)
    for step in range(count - 1, count):
        copies[0][step].wait()
        copies[2][step].wait()
        copies[1][count - 1 - step].wait()
        copies[3][count - 1 - step].wait()


def shifted(value, axis, count, shift, reverse):
    if reverse:
        pairs = [(i + shift, i) for i in range(count - shift)]
    else:
        pairs = [(i, i + shift) for i in range(count - shift)]
    return lax.ppermute(value, axis, pairs)


def scan_enter(summary_map, summary_state, axis, reverse):
    count = lax.axis_size(axis)
    rank = summary_map.shape[0]
    both = jnp.concatenate([summary_map, summary_state], axis=1)
    rounds = 0
    while 2 ** (rounds + 1) < count - 1:
        rounds += 1
    shift = 1
    for _ in range(rounds):
        got = shifted(both, axis, count, shift, reverse)
        joined = jnp.dot(both[:, :rank], got, precision=HIGHEST)
        both = joined + jnp.concatenate(
            [jnp.zeros_like(summary_map), both[:, rank:]], axis=1
        )
        shift *= 2
    near = shifted(both, axis, count, 1, reverse)
    far = shifted(both[:, rank:], axis, count, 1 + shift, reverse)
    return jnp.dot(near[:, :rank], far, precision=HIGHEST) + near[:, rank:]


def chip_shift(value, axis, chips, shift):
    pairs = [(2 * c, 2 * (c + shift)) for c in range(chips - shift)]
    pairs += [(2 * c + 1, 2 * (c - shift) + 1) for c in range(shift, chips)]
    return lax.ppermute(value, axis, pairs)


def scan_chips(lower, upper, axis):
    count = lax.axis_size(axis)
    chips = count // 2
    rank = lower.shape[0]
    first = lax.axis_index(axis) % 2 == 0
    own = jnp.where(first, lower, upper)
    partner = [(2 * c, 2 * c + 1) for c in range(chips)]
    partner += [(2 * c + 1, 2 * c) for c in range(chips)]
    got = lax.ppermute(jnp.where(first, upper, lower), axis, partner)
    tail = jnp.concatenate([jnp.zeros((rank, rank), F32), got[:, rank:]], axis=1)
    both = jnp.dot(got[:, :rank], own, precision=HIGHEST) + tail
    rounds = 0
    while 2 ** (rounds + 1) < chips - 1:
        rounds += 1
    shift = 1
    for _ in range(rounds):
        got = chip_shift(both, axis, chips, shift)
        tail = jnp.concatenate([jnp.zeros((rank, rank), F32), both[:, rank:]], axis=1)
        both = jnp.dot(both[:, :rank], got, precision=HIGHEST) + tail
        shift *= 2
    near = chip_shift(both, axis, chips, 1)
    far = chip_shift(both[:, rank:], axis, chips, 1 + shift)
    enter = jnp.dot(near[:, :rank], far, precision=HIGHEST) + near[:, rank:]
    send = jnp.dot(own[:, :rank], enter, precision=HIGHEST) + own[:, rank:]
    other = lax.ppermute(send, axis, partner)
    return enter, other


def shards(
    right_sides,
    diagonal_blocks,
    lower_rows,
    lower_cols,
    lower_trans,
    upper_rows,
    upper_cols,
    upper_trans,
):
    count, rows, rhs = right_sides.shape
    rank = lower_trans.shape[1]
    lboth, lsrc, uboth, usrc = pl.pallas_call(
        sweep_kernel,
        out_shape=(
            jax.ShapeDtypeStruct((rank, rank + rhs), F32),
            jax.ShapeDtypeStruct((count, rank, rhs), F32),
            jax.ShapeDtypeStruct((rank, rank + rhs), F32),
            jax.ShapeDtypeStruct((count, rank, rhs), F32),
        ),
        name="sweep",
    )(right_sides, lower_cols, lower_trans, upper_cols, upper_trans)
    diag = jnp.einsum(
        "kab,kbc->kac", diagonal_blocks, right_sides, preferred_element_type=F32
    )
    count_row = lax.axis_size("row")
    if count_row % 2 == 0 and count_row >= 4:
        enter, other = scan_chips(lboth, uboth, "row")
        flag = jnp.full((1,), lax.axis_index("row") % 2, jnp.int32)
    else:
        enter = scan_enter(lboth[:, :rank], lboth[:, rank:], "row", False)
        other = scan_enter(uboth[:, :rank], uboth[:, rank:], "row", True)
        flag = jnp.zeros((1,), jnp.int32)
    vmem = pl.BlockSpec(memory_space=pltpu.VMEM)
    anywhere = pl.BlockSpec(memory_space=pl.ANY)
    return pl.pallas_call(
        apply_kernel,
        out_shape=jax.ShapeDtypeStruct((count, rows, rhs), BF16),
        scratch_shapes=[
            pltpu.VMEM((count, rank, rank), BF16),
            pltpu.VMEM((count, rank, rank), BF16),
            pltpu.VMEM((count, rank, rhs), F32),
            pltpu.VMEM((count, rank, rhs), F32),
            pltpu.VMEM((count, rows, rhs), F32),
            pltpu.VMEM((count, rows, rank), BF16),
            pltpu.VMEM((count, rows, rank), BF16),
            pltpu.SemaphoreType.DMA((7, count)),
        ],
        in_specs=[pl.BlockSpec(memory_space=pltpu.SMEM), vmem, vmem] + [anywhere] * 7,
        name="apply",
    )(flag, enter, other, lower_trans, upper_trans, lsrc, usrc, diag, lower_rows, upper_rows)


def solution(mesh):
    spec = P(("sep", "row"), None, None)
    return jax.shard_map(
        shards, mesh=mesh, in_specs=(spec,) * 8, out_specs=spec, check_vma=False
    )
```

```python
import jax
import jax.numpy as jnp
from jax import lax
from jax.experimental import pallas as pl
from jax.experimental.pallas import tpu as pltpu
from jax.sharding import PartitionSpec as P

F32 = jnp.float32
BF16 = jnp.bfloat16
HIGHEST = lax.Precision.HIGHEST


def split_dot(matrix, value):
    high = value.astype(BF16)
    low = (value - high.astype(F32)).astype(BF16)
    return jnp.dot(matrix, high, preferred_element_type=F32) + jnp.dot(
        matrix, low, preferred_element_type=F32
    )


def sweep_kernel(
    rhs_ref, lcols_ref, ltrans_ref, ucols_ref, utrans_ref,
    lmap_ref, lsrc_ref, umap_ref, usrc_ref,
):
    count = rhs_ref.shape[0]
    lmap = lstate = umap = ustate = None
    for step in range(count):
        lk = step
        uk = count - 1 - step
        lsrc = lax.dot_general(lcols_ref[lk], rhs_ref[lk], (((0,), (0,)), ((), ())), preferred_element_type=F32)
        usrc = lax.dot_general(ucols_ref[uk], rhs_ref[uk], (((0,), (0,)), ((), ())), preferred_element_type=F32)
        lsrc_ref[lk] = lsrc
        usrc_ref[uk] = usrc
        ltrans = ltrans_ref[lk]
        utrans = utrans_ref[uk]
        if step == 0:
            lstate = lsrc
            ustate = usrc
            lmap = ltrans.astype(F32)
            umap = utrans.astype(F32)
        else:
            lstate = split_dot(ltrans, lstate) + lsrc
            ustate = split_dot(utrans, ustate) + usrc
            lmap = split_dot(ltrans, lmap)
            umap = split_dot(utrans, umap)
    rank = lmap.shape[0]
    lmap_ref[:, :rank] = lmap
    lmap_ref[:, rank:] = lstate
    umap_ref[:, :rank] = umap
    umap_ref[:, rank:] = ustate


def apply_kernel(
    flag_ref, enter_ref, other_ref, ltrans_ref, utrans_ref, lsrc_ref, usrc_ref,
    diag_ref, lrows_ref, urows_ref, out_ref, lround_ref, uround_ref,
):
    count = ltrans_ref.shape[0]
    first = flag_ref[0] == 0
    lstate = jnp.where(first, enter_ref[...], other_ref[...])
    ustate = jnp.where(first, other_ref[...], enter_ref[...])
    for step in range(count):
        lk = step
        uk = count - 1 - step
        lround_ref[lk] = lstate.astype(BF16)
        uround_ref[uk] = ustate.astype(BF16)
        if step + 1 < count:
            lstate = split_dot(ltrans_ref[lk], lstate) + lsrc_ref[lk]
            ustate = split_dot(utrans_ref[uk], ustate) + usrc_ref[uk]
    for k in range(count):
        total = diag_ref[k]
        total = total + jnp.dot(lrows_ref[k], lround_ref[k], preferred_element_type=F32)
        total = total + jnp.dot(urows_ref[k], uround_ref[k], preferred_element_type=F32)
        out_ref[k] = total.astype(out_ref.dtype)


def shifted(value, axis, count, shift, reverse):
    if reverse:
        pairs = [(i + shift, i) for i in range(count - shift)]
    else:
        pairs = [(i, i + shift) for i in range(count - shift)]
    return lax.ppermute(value, axis, pairs)


def scan_enter(summary_map, summary_state, axis, reverse):
    count = lax.axis_size(axis)
    rank = summary_map.shape[0]
    both = jnp.concatenate([summary_map, summary_state], axis=1)
    rounds = 0
    while 2 ** (rounds + 1) < count - 1:
        rounds += 1
    shift = 1
    for _ in range(rounds):
        got = shifted(both, axis, count, shift, reverse)
        joined = jnp.dot(both[:, :rank], got, precision=HIGHEST)
        both = joined + jnp.concatenate(
            [jnp.zeros_like(summary_map), both[:, rank:]], axis=1
        )
        shift *= 2
    near = shifted(both, axis, count, 1, reverse)
    far = shifted(both[:, rank:], axis, count, 1 + shift, reverse)
    return jnp.dot(near[:, :rank], far, precision=HIGHEST) + near[:, rank:]


def chip_shift(value, axis, chips, shift):
    pairs = [(2 * c, 2 * (c + shift)) for c in range(chips - shift)]
    pairs += [(2 * c + 1, 2 * (c - shift) + 1) for c in range(shift, chips)]
    return lax.ppermute(value, axis, pairs)


def scan_chips(lower, upper, axis):
    count = lax.axis_size(axis)
    chips = count // 2
    rank = lower.shape[0]
    first = lax.axis_index(axis) % 2 == 0
    own = jnp.where(first, lower, upper)
    partner = [(2 * c, 2 * c + 1) for c in range(chips)]
    partner += [(2 * c + 1, 2 * c) for c in range(chips)]
    got = lax.ppermute(jnp.where(first, upper, lower), axis, partner)
    tail = jnp.concatenate([jnp.zeros((rank, rank), F32), got[:, rank:]], axis=1)
    both = jnp.dot(got[:, :rank], own, precision=HIGHEST) + tail
    rounds = 0
    while 2 ** (rounds + 1) < chips - 1:
        rounds += 1
    shift = 1
    for _ in range(rounds):
        got = chip_shift(both, axis, chips, shift)
        tail = jnp.concatenate([jnp.zeros((rank, rank), F32), both[:, rank:]], axis=1)
        both = jnp.dot(both[:, :rank], got, precision=HIGHEST) + tail
        shift *= 2
    near = chip_shift(both, axis, chips, 1)
    far = chip_shift(both[:, rank:], axis, chips, 1 + shift)
    enter = jnp.dot(near[:, :rank], far, precision=HIGHEST) + near[:, rank:]
    send = jnp.dot(own[:, :rank], enter, precision=HIGHEST) + own[:, rank:]
    other = lax.ppermute(send, axis, partner)
    return enter, other


def group_shift(value, axis, groups, shift):
    pairs = [(4 * g + 2, 4 * (g + shift) + 2) for g in range(groups - shift)]
    pairs += [(4 * g + 1, 4 * (g - shift) + 1) for g in range(shift, groups)]
    return lax.ppermute(value, axis, pairs)


def scan_groups(own, give, axis):
    count = lax.axis_size(axis)
    groups = count // 4
    rank = own.shape[0]
    place = lax.axis_index(axis) % 4
    zeros = jnp.zeros((rank, rank), F32)
    partner = [(2 * c, 2 * c + 1) for c in range(count // 2)]
    partner += [(2 * c + 1, 2 * c) for c in range(count // 2)]
    got = lax.ppermute(give, axis, partner)
    both = jnp.dot(got[:, :rank], own, precision=HIGHEST) + jnp.concatenate(
        [zeros, got[:, rank:]], axis=1
    )
    pair = [(4 * g, 4 * g + 2) for g in range(groups)]
    pair += [(4 * g + 3, 4 * g + 1) for g in range(groups)]
    beside = lax.ppermute(both, axis, pair)
    both = jnp.dot(both[:, :rank], beside, precision=HIGHEST) + jnp.concatenate(
        [zeros, both[:, rank:]], axis=1
    )
    rounds = 0
    while 2 ** (rounds + 1) < groups - 1:
        rounds += 1
    shift = 1
    for _ in range(rounds):
        got = group_shift(both, axis, groups, shift)
        tail = jnp.concatenate([zeros, both[:, rank:]], axis=1)
        both = jnp.dot(both[:, :rank], got, precision=HIGHEST) + tail
        shift *= 2
    near = group_shift(both, axis, groups, 1)
    far = group_shift(both[:, rank:], axis, groups, 1 + shift)
    start = jnp.dot(near[:, :rank], far, precision=HIGHEST) + near[:, rank:]
    back = [(4 * g + 2, 4 * g) for g in range(groups)]
    back += [(4 * g + 1, 4 * g + 3) for g in range(groups)]
    sent = lax.ppermute(start, axis, back)
    mine = jnp.dot(beside[:, :rank], start, precision=HIGHEST) + beside[:, rank:]
    holder = jnp.logical_or(place == 1, place == 2)
    enter = jnp.where(holder, mine, sent)
    send = jnp.dot(own[:, :rank], enter, precision=HIGHEST) + own[:, rank:]
    other = lax.ppermute(send, axis, partner)
    return enter, other


def shards(
    right_sides,
    diagonal_blocks,
    lower_rows,
    lower_cols,
    lower_trans,
    upper_rows,
    upper_cols,
    upper_trans,
):
    count, rows, rhs = right_sides.shape
    rank = lower_trans.shape[1]
    lboth, lsrc, uboth, usrc = pl.pallas_call(
        sweep_kernel,
        out_shape=(
            jax.ShapeDtypeStruct((rank, rank + rhs), F32),
            jax.ShapeDtypeStruct((count, rank, rhs), F32),
            jax.ShapeDtypeStruct((rank, rank + rhs), F32),
            jax.ShapeDtypeStruct((count, rank, rhs), F32),
        ),
        name="sweep",
    )(right_sides, lower_cols, lower_trans, upper_cols, upper_trans)
    diag = jnp.einsum(
        "kab,kbc->kac", diagonal_blocks, right_sides, preferred_element_type=F32
    )
    count_row = lax.axis_size("row")
    if count_row % 4 == 0 and count_row >= 8:
        first = lax.axis_index("row") % 2 == 0
        enter, other = scan_groups(
            jnp.where(first, lboth, uboth), jnp.where(first, uboth, lboth), "row"
        )
        flag = jnp.full((1,), lax.axis_index("row") % 2, jnp.int32)
    elif count_row % 2 == 0 and count_row >= 4:
        enter, other = scan_chips(lboth, uboth, "row")
        flag = jnp.full((1,), lax.axis_index("row") % 2, jnp.int32)
    else:
        enter = scan_enter(lboth[:, :rank], lboth[:, rank:], "row", False)
        other = scan_enter(uboth[:, :rank], uboth[:, rank:], "row", True)
        flag = jnp.zeros((1,), jnp.int32)
    vmem = pl.BlockSpec(memory_space=pltpu.VMEM)
    return pl.pallas_call(
        apply_kernel,
        out_shape=jax.ShapeDtypeStruct((count, rows, rhs), BF16),
        scratch_shapes=[
            pltpu.VMEM((count, rank, rhs), BF16),
            pltpu.VMEM((count, rank, rhs), BF16),
        ],
        in_specs=[pl.BlockSpec(memory_space=pltpu.SMEM)] + [vmem] * 9,
        name="apply",
    )(flag, enter, other, lower_trans, upper_trans, lsrc, usrc, diag, lower_rows, upper_rows)


def solution(mesh):
    spec = P(("sep", "row"), None, None)
    return jax.shard_map(
        shards, mesh=mesh, in_specs=(spec,) * 8, out_specs=spec, check_vma=False
    )
```

```python
import jax
import jax.numpy as jnp
from jax import lax
from jax.experimental import pallas as pl
from jax.experimental.pallas import tpu as pltpu
from jax.sharding import PartitionSpec as P

F32 = jnp.float32
BF16 = jnp.bfloat16
HIGHEST = lax.Precision.HIGHEST


def split_dot(matrix, value):
    high = value.astype(BF16)
    low = (value - high.astype(F32)).astype(BF16)
    return jnp.dot(matrix, high, preferred_element_type=F32) + jnp.dot(
        matrix, low, preferred_element_type=F32
    )


def sweep_kernel(
    rhs_ref, lcols_ref, ltrans_ref, ucols_ref, utrans_ref,
    lmap_ref, lsrc_ref, umap_ref, usrc_ref,
):
    count = rhs_ref.shape[0]
    lmap = lstate = umap = ustate = None
    for step in range(count):
        lk = step
        uk = count - 1 - step
        lsrc = lax.dot_general(lcols_ref[lk], rhs_ref[lk], (((0,), (0,)), ((), ())), preferred_element_type=F32)
        usrc = lax.dot_general(ucols_ref[uk], rhs_ref[uk], (((0,), (0,)), ((), ())), preferred_element_type=F32)
        lsrc_ref[lk] = lsrc
        usrc_ref[uk] = usrc
        ltrans = ltrans_ref[lk]
        utrans = utrans_ref[uk]
        if step == 0:
            lstate = lsrc
            ustate = usrc
            lmap = ltrans.astype(F32)
            umap = utrans.astype(F32)
        else:
            lstate = split_dot(ltrans, lstate) + lsrc
            ustate = split_dot(utrans, ustate) + usrc
            lmap = split_dot(ltrans, lmap)
            umap = split_dot(utrans, umap)
    rank = lmap.shape[0]
    lmap_ref[:, :rank] = lmap
    lmap_ref[:, rank:] = lstate
    umap_ref[:, :rank] = umap
    umap_ref[:, rank:] = ustate


def apply_kernel(
    flag_ref, enter_ref, other_ref, ltrans_ref, utrans_ref, lsrc_ref, usrc_ref,
    diag_ref, lrows_ref, urows_ref, out_ref, lround_ref, uround_ref,
):
    count = ltrans_ref.shape[0]
    first = flag_ref[0] == 0
    lstate = jnp.where(first, enter_ref[...], other_ref[...])
    ustate = jnp.where(first, other_ref[...], enter_ref[...])
    for step in range(count):
        lk = step
        uk = count - 1 - step
        lround_ref[lk] = lstate.astype(BF16)
        uround_ref[uk] = ustate.astype(BF16)
        if step + 1 < count:
            lstate = split_dot(ltrans_ref[lk], lstate) + lsrc_ref[lk]
            ustate = split_dot(utrans_ref[uk], ustate) + usrc_ref[uk]
    for k in range(count):
        total = diag_ref[k]
        total = total + jnp.dot(lrows_ref[k], lround_ref[k], preferred_element_type=F32)
        total = total + jnp.dot(urows_ref[k], uround_ref[k], preferred_element_type=F32)
        out_ref[k] = total.astype(out_ref.dtype)


def shifted(value, axis, count, shift, reverse):
    if reverse:
        pairs = [(i + shift, i) for i in range(count - shift)]
    else:
        pairs = [(i, i + shift) for i in range(count - shift)]
    return lax.ppermute(value, axis, pairs)


def scan_enter(summary_map, summary_state, axis, reverse):
    count = lax.axis_size(axis)
    rank = summary_map.shape[0]
    both = jnp.concatenate([summary_map, summary_state], axis=1)
    rounds = 0
    while 2 ** (rounds + 1) < count - 1:
        rounds += 1
    shift = 1
    for _ in range(rounds):
        got = shifted(both, axis, count, shift, reverse)
        joined = jnp.dot(both[:, :rank], got, precision=HIGHEST)
        both = joined + jnp.concatenate(
            [jnp.zeros_like(summary_map), both[:, rank:]], axis=1
        )
        shift *= 2
    near = shifted(both, axis, count, 1, reverse)
    far = shifted(both[:, rank:], axis, count, 1 + shift, reverse)
    return jnp.dot(near[:, :rank], far, precision=HIGHEST) + near[:, rank:]


def chip_shift(value, axis, chips, shift):
    pairs = [(2 * c, 2 * (c + shift)) for c in range(chips - shift)]
    pairs += [(2 * c + 1, 2 * (c - shift) + 1) for c in range(shift, chips)]
    return lax.ppermute(value, axis, pairs)


def scan_chips(lower, upper, axis):
    count = lax.axis_size(axis)
    chips = count // 2
    rank = lower.shape[0]
    first = lax.axis_index(axis) % 2 == 0
    own = jnp.where(first, lower, upper)
    partner = [(2 * c, 2 * c + 1) for c in range(chips)]
    partner += [(2 * c + 1, 2 * c) for c in range(chips)]
    got = lax.ppermute(jnp.where(first, upper, lower), axis, partner)
    tail = jnp.concatenate([jnp.zeros((rank, rank), F32), got[:, rank:]], axis=1)
    both = jnp.dot(got[:, :rank], own, precision=HIGHEST) + tail
    rounds = 0
    while 2 ** (rounds + 1) < chips - 1:
        rounds += 1
    shift = 1
    for _ in range(rounds):
        got = chip_shift(both, axis, chips, shift)
        tail = jnp.concatenate([jnp.zeros((rank, rank), F32), both[:, rank:]], axis=1)
        both = jnp.dot(both[:, :rank], got, precision=HIGHEST) + tail
        shift *= 2
    near = chip_shift(both, axis, chips, 1)
    far = chip_shift(both[:, rank:], axis, chips, 1 + shift)
    enter = jnp.dot(near[:, :rank], far, precision=HIGHEST) + near[:, rank:]
    send = jnp.dot(own[:, :rank], enter, precision=HIGHEST) + own[:, rank:]
    other = lax.ppermute(send, axis, partner)
    return enter, other


def group_shift(value, axis, groups, shift):
    pairs = [(4 * g + 2, 4 * (g + shift) + 2) for g in range(groups - shift)]
    pairs += [(4 * g + 1, 4 * (g - shift) + 1) for g in range(shift, groups)]
    return lax.ppermute(value, axis, pairs)


def scan_groups(own, give, axis):
    count = lax.axis_size(axis)
    groups = count // 4
    rank = own.shape[0]
    place = lax.axis_index(axis) % 4
    zeros = jnp.zeros((rank, rank), F32)
    partner = [(2 * c, 2 * c + 1) for c in range(count // 2)]
    partner += [(2 * c + 1, 2 * c) for c in range(count // 2)]
    got = lax.ppermute(give, axis, partner)
    both = jnp.dot(got[:, :rank], own, precision=HIGHEST) + jnp.concatenate(
        [zeros, got[:, rank:]], axis=1
    )
    pair = [(4 * g, 4 * g + 2) for g in range(groups)]
    pair += [(4 * g + 3, 4 * g + 1) for g in range(groups)]
    beside = lax.ppermute(both, axis, pair)
    both = jnp.dot(both[:, :rank], beside, precision=HIGHEST) + jnp.concatenate(
        [zeros, both[:, rank:]], axis=1
    )
    if groups <= 4:
        out = both[:, rank:]
        for step in range(groups - 1):
            start = group_shift(out, axis, groups, 1)
            if step + 2 < groups:
                out = jnp.dot(both[:, :rank], start, precision=HIGHEST) + both[:, rank:]
    else:
        rounds = 0
        while 2 ** (rounds + 1) < groups - 1:
            rounds += 1
        shift = 1
        for _ in range(rounds):
            got = group_shift(both, axis, groups, shift)
            tail = jnp.concatenate([zeros, both[:, rank:]], axis=1)
            both = jnp.dot(both[:, :rank], got, precision=HIGHEST) + tail
            shift *= 2
        near = group_shift(both, axis, groups, 1)
        far = group_shift(both[:, rank:], axis, groups, 1 + shift)
        start = jnp.dot(near[:, :rank], far, precision=HIGHEST) + near[:, rank:]
    back = [(4 * g + 2, 4 * g) for g in range(groups)]
    back += [(4 * g + 1, 4 * g + 3) for g in range(groups)]
    sent = lax.ppermute(start, axis, back)
    mine = jnp.dot(beside[:, :rank], start, precision=HIGHEST) + beside[:, rank:]
    holder = jnp.logical_or(place == 1, place == 2)
    enter = jnp.where(holder, mine, sent)
    send = jnp.dot(own[:, :rank], enter, precision=HIGHEST) + own[:, rank:]
    other = lax.ppermute(send, axis, partner)
    return enter, other


def shards(
    right_sides,
    diagonal_blocks,
    lower_rows,
    lower_cols,
    lower_trans,
    upper_rows,
    upper_cols,
    upper_trans,
):
    count, rows, rhs = right_sides.shape
    rank = lower_trans.shape[1]
    lboth, lsrc, uboth, usrc = pl.pallas_call(
        sweep_kernel,
        out_shape=(
            jax.ShapeDtypeStruct((rank, rank + rhs), F32),
            jax.ShapeDtypeStruct((count, rank, rhs), F32),
            jax.ShapeDtypeStruct((rank, rank + rhs), F32),
            jax.ShapeDtypeStruct((count, rank, rhs), F32),
        ),
        name="sweep",
    )(right_sides, lower_cols, lower_trans, upper_cols, upper_trans)
    diag = jnp.einsum(
        "kab,kbc->kac", diagonal_blocks, right_sides, preferred_element_type=F32
    )
    count_row = lax.axis_size("row")
    if count_row % 4 == 0 and count_row >= 8:
        first = lax.axis_index("row") % 2 == 0
        enter, other = scan_groups(
            jnp.where(first, lboth, uboth), jnp.where(first, uboth, lboth), "row"
        )
        flag = jnp.full((1,), lax.axis_index("row") % 2, jnp.int32)
    elif count_row % 2 == 0 and count_row >= 4:
        enter, other = scan_chips(lboth, uboth, "row")
        flag = jnp.full((1,), lax.axis_index("row") % 2, jnp.int32)
    else:
        enter = scan_enter(lboth[:, :rank], lboth[:, rank:], "row", False)
        other = scan_enter(uboth[:, :rank], uboth[:, rank:], "row", True)
        flag = jnp.zeros((1,), jnp.int32)
    vmem = pl.BlockSpec(memory_space=pltpu.VMEM)
    return pl.pallas_call(
        apply_kernel,
        out_shape=jax.ShapeDtypeStruct((count, rows, rhs), BF16),
        scratch_shapes=[
            pltpu.VMEM((count, rank, rhs), BF16),
            pltpu.VMEM((count, rank, rhs), BF16),
        ],
        in_specs=[pl.BlockSpec(memory_space=pltpu.SMEM)] + [vmem] * 9,
        name="apply",
    )(flag, enter, other, lower_trans, upper_trans, lsrc, usrc, diag, lower_rows, upper_rows)


def solution(mesh):
    spec = P(("sep", "row"), None, None)
    return jax.shard_map(
        shards, mesh=mesh, in_specs=(spec,) * 8, out_specs=spec, check_vma=False
    )
```

```python
import jax
import jax.numpy as jnp
from jax import lax
from jax.experimental import pallas as pl
from jax.experimental.pallas import tpu as pltpu
from jax.sharding import PartitionSpec as P

F32 = jnp.float32
BF16 = jnp.bfloat16
HIGHEST = lax.Precision.HIGHEST


def split_dot(matrix, value):
    high = value.astype(BF16)
    low = (value - high.astype(F32)).astype(BF16)
    return jnp.dot(matrix, high, preferred_element_type=F32) + jnp.dot(
        matrix, low, preferred_element_type=F32
    )


def sweep_kernel(
    rhs_ref, lcols_ref, ltrans_ref, ucols_ref, utrans_ref,
    lmap_ref, lsrc_ref, umap_ref, usrc_ref,
):
    count = rhs_ref.shape[0]
    lmap = lstate = umap = ustate = None
    for step in range(count):
        lk = step
        uk = count - 1 - step
        lsrc = lax.dot_general(lcols_ref[lk], rhs_ref[lk], (((0,), (0,)), ((), ())), preferred_element_type=F32)
        usrc = lax.dot_general(ucols_ref[uk], rhs_ref[uk], (((0,), (0,)), ((), ())), preferred_element_type=F32)
        lsrc_ref[lk] = lsrc
        usrc_ref[uk] = usrc
        ltrans = ltrans_ref[lk]
        utrans = utrans_ref[uk]
        if step == 0:
            lstate = lsrc
            ustate = usrc
            lmap = ltrans.astype(F32)
            umap = utrans.astype(F32)
        else:
            lstate = split_dot(ltrans, lstate) + lsrc
            ustate = split_dot(utrans, ustate) + usrc
            lmap = split_dot(ltrans, lmap)
            umap = split_dot(utrans, umap)
    rank = lmap.shape[0]
    lmap_ref[:, :rank] = lmap
    lmap_ref[:, rank:] = lstate
    umap_ref[:, :rank] = umap
    umap_ref[:, rank:] = ustate


def wide_dot(left, right):
    left_high = left.astype(BF16)
    left_low = (left - left_high.astype(F32)).astype(BF16)
    right_high = right.astype(BF16)
    right_low = (right - right_high.astype(F32)).astype(BF16)
    total = jnp.dot(left_high, right_high, preferred_element_type=F32)
    total = total + jnp.dot(left_high, right_low, preferred_element_type=F32)
    return total + jnp.dot(left_low, right_high, preferred_element_type=F32)


def prefix_kernel(
    ltrans_ref, utrans_ref, lsrc_ref, usrc_ref, lpre_ref, lloc_ref, upre_ref, uloc_ref,
):
    count, rank, _ = ltrans_ref.shape
    rows = lax.broadcasted_iota(jnp.int32, (rank, rank), 0)
    cols = lax.broadcasted_iota(jnp.int32, (rank, rank), 1)
    eye = jnp.where(rows == cols, 1.0, 0.0).astype(F32)
    zero = jnp.zeros(lloc_ref.shape[1:], F32)
    lpre = upre = eye
    lloc = uloc = zero
    for step in range(count):
        lk = step
        uk = count - 1 - step
        lpre_ref[lk] = lpre
        lloc_ref[lk] = lloc
        upre_ref[uk] = upre
        uloc_ref[uk] = uloc
        if step + 1 < count:
            if step == 0:
                lpre = ltrans_ref[lk].astype(F32)
                upre = utrans_ref[uk].astype(F32)
                lloc = lsrc_ref[lk]
                uloc = usrc_ref[uk]
            else:
                lpre = split_dot(ltrans_ref[lk], lpre)
                upre = split_dot(utrans_ref[uk], upre)
                lloc = split_dot(ltrans_ref[lk], lloc) + lsrc_ref[lk]
                uloc = split_dot(utrans_ref[uk], uloc) + usrc_ref[uk]


def apply_kernel(
    flag_ref, enter_ref, other_ref, lpre_ref, lloc_ref, upre_ref, uloc_ref,
    diag_ref, lrows_ref, urows_ref, out_ref,
):
    first = flag_ref[0] == 0
    lenter = jnp.where(first, enter_ref[...], other_ref[...])
    uenter = jnp.where(first, other_ref[...], enter_ref[...])
    lstate = lloc_ref[0] + wide_dot(lpre_ref[0], lenter)
    ustate = uloc_ref[0] + wide_dot(upre_ref[0], uenter)
    total = diag_ref[0]
    total = total + jnp.dot(lrows_ref[0], lstate.astype(BF16), preferred_element_type=F32)
    total = total + jnp.dot(urows_ref[0], ustate.astype(BF16), preferred_element_type=F32)
    out_ref[0] = total.astype(out_ref.dtype)


def shifted(value, axis, count, shift, reverse):
    if reverse:
        pairs = [(i + shift, i) for i in range(count - shift)]
    else:
        pairs = [(i, i + shift) for i in range(count - shift)]
    return lax.ppermute(value, axis, pairs)


def scan_enter(summary_map, summary_state, axis, reverse):
    count = lax.axis_size(axis)
    rank = summary_map.shape[0]
    both = jnp.concatenate([summary_map, summary_state], axis=1)
    rounds = 0
    while 2 ** (rounds + 1) < count - 1:
        rounds += 1
    shift = 1
    for _ in range(rounds):
        got = shifted(both, axis, count, shift, reverse)
        joined = jnp.dot(both[:, :rank], got, precision=HIGHEST)
        both = joined + jnp.concatenate(
            [jnp.zeros_like(summary_map), both[:, rank:]], axis=1
        )
        shift *= 2
    near = shifted(both, axis, count, 1, reverse)
    far = shifted(both[:, rank:], axis, count, 1 + shift, reverse)
    return jnp.dot(near[:, :rank], far, precision=HIGHEST) + near[:, rank:]


def chip_shift(value, axis, chips, shift):
    pairs = [(2 * c, 2 * (c + shift)) for c in range(chips - shift)]
    pairs += [(2 * c + 1, 2 * (c - shift) + 1) for c in range(shift, chips)]
    return lax.ppermute(value, axis, pairs)


def scan_chips(lower, upper, axis):
    count = lax.axis_size(axis)
    chips = count // 2
    rank = lower.shape[0]
    first = lax.axis_index(axis) % 2 == 0
    own = jnp.where(first, lower, upper)
    partner = [(2 * c, 2 * c + 1) for c in range(chips)]
    partner += [(2 * c + 1, 2 * c) for c in range(chips)]
    got = lax.ppermute(jnp.where(first, upper, lower), axis, partner)
    tail = jnp.concatenate([jnp.zeros((rank, rank), F32), got[:, rank:]], axis=1)
    both = jnp.dot(got[:, :rank], own, precision=HIGHEST) + tail
    rounds = 0
    while 2 ** (rounds + 1) < chips - 1:
        rounds += 1
    shift = 1
    for _ in range(rounds):
        got = chip_shift(both, axis, chips, shift)
        tail = jnp.concatenate([jnp.zeros((rank, rank), F32), both[:, rank:]], axis=1)
        both = jnp.dot(both[:, :rank], got, precision=HIGHEST) + tail
        shift *= 2
    near = chip_shift(both, axis, chips, 1)
    far = chip_shift(both[:, rank:], axis, chips, 1 + shift)
    enter = jnp.dot(near[:, :rank], far, precision=HIGHEST) + near[:, rank:]
    send = jnp.dot(own[:, :rank], enter, precision=HIGHEST) + own[:, rank:]
    other = lax.ppermute(send, axis, partner)
    return enter, other


def group_shift(value, axis, groups, shift):
    pairs = [(4 * g + 2, 4 * (g + shift) + 2) for g in range(groups - shift)]
    pairs += [(4 * g + 1, 4 * (g - shift) + 1) for g in range(shift, groups)]
    return lax.ppermute(value, axis, pairs)


def scan_groups(own, give, axis):
    count = lax.axis_size(axis)
    groups = count // 4
    rank = own.shape[0]
    place = lax.axis_index(axis) % 4
    zeros = jnp.zeros((rank, rank), F32)
    partner = [(2 * c, 2 * c + 1) for c in range(count // 2)]
    partner += [(2 * c + 1, 2 * c) for c in range(count // 2)]
    got = lax.ppermute(give, axis, partner)
    both = jnp.dot(got[:, :rank], own, precision=HIGHEST) + jnp.concatenate(
        [zeros, got[:, rank:]], axis=1
    )
    pair = [(4 * g, 4 * g + 2) for g in range(groups)]
    pair += [(4 * g + 3, 4 * g + 1) for g in range(groups)]
    beside = lax.ppermute(both, axis, pair)
    both = jnp.dot(both[:, :rank], beside, precision=HIGHEST) + jnp.concatenate(
        [zeros, both[:, rank:]], axis=1
    )
    if groups <= 4:
        out = both[:, rank:]
        for step in range(groups - 1):
            start = group_shift(out, axis, groups, 1)
            if step + 2 < groups:
                out = jnp.dot(both[:, :rank], start, precision=HIGHEST) + both[:, rank:]
    else:
        rounds = 0
        while 2 ** (rounds + 1) < groups - 1:
            rounds += 1
        shift = 1
        for _ in range(rounds):
            got = group_shift(both, axis, groups, shift)
            tail = jnp.concatenate([zeros, both[:, rank:]], axis=1)
            both = jnp.dot(both[:, :rank], got, precision=HIGHEST) + tail
            shift *= 2
        near = group_shift(both, axis, groups, 1)
        far = group_shift(both[:, rank:], axis, groups, 1 + shift)
        start = jnp.dot(near[:, :rank], far, precision=HIGHEST) + near[:, rank:]
    back = [(4 * g + 2, 4 * g) for g in range(groups)]
    back += [(4 * g + 1, 4 * g + 3) for g in range(groups)]
    sent = lax.ppermute(start, axis, back)
    mine = jnp.dot(beside[:, :rank], start, precision=HIGHEST) + beside[:, rank:]
    holder = jnp.logical_or(place == 1, place == 2)
    enter = jnp.where(holder, mine, sent)
    send = jnp.dot(own[:, :rank], enter, precision=HIGHEST) + own[:, rank:]
    other = lax.ppermute(send, axis, partner)
    return enter, other


def shards(
    right_sides,
    diagonal_blocks,
    lower_rows,
    lower_cols,
    lower_trans,
    upper_rows,
    upper_cols,
    upper_trans,
):
    count, rows, rhs = right_sides.shape
    rank = lower_trans.shape[1]
    lboth, lsrc, uboth, usrc = pl.pallas_call(
        sweep_kernel,
        out_shape=(
            jax.ShapeDtypeStruct((rank, rank + rhs), F32),
            jax.ShapeDtypeStruct((count, rank, rhs), F32),
            jax.ShapeDtypeStruct((rank, rank + rhs), F32),
            jax.ShapeDtypeStruct((count, rank, rhs), F32),
        ),
        name="sweep",
    )(right_sides, lower_cols, lower_trans, upper_cols, upper_trans)
    diag = jnp.einsum(
        "kab,kbc->kac", diagonal_blocks, right_sides, preferred_element_type=F32
    )
    count_row = lax.axis_size("row")
    if count_row % 4 == 0 and count_row >= 8:
        first = lax.axis_index("row") % 2 == 0
        enter, other = scan_groups(
            jnp.where(first, lboth, uboth), jnp.where(first, uboth, lboth), "row"
        )
        flag = jnp.full((1,), lax.axis_index("row") % 2, jnp.int32)
    elif count_row % 2 == 0 and count_row >= 4:
        enter, other = scan_chips(lboth, uboth, "row")
        flag = jnp.full((1,), lax.axis_index("row") % 2, jnp.int32)
    else:
        enter = scan_enter(lboth[:, :rank], lboth[:, rank:], "row", False)
        other = scan_enter(uboth[:, :rank], uboth[:, rank:], "row", True)
        flag = jnp.zeros((1,), jnp.int32)
    vmem = pl.BlockSpec(memory_space=pltpu.VMEM)
    lpre, lloc, upre, uloc = pl.pallas_call(
        prefix_kernel,
        out_shape=(
            jax.ShapeDtypeStruct((count, rank, rank), F32),
            jax.ShapeDtypeStruct((count, rank, rhs), F32),
            jax.ShapeDtypeStruct((count, rank, rank), F32),
            jax.ShapeDtypeStruct((count, rank, rhs), F32),
        ),
        name="prefix",
    )(lower_trans, upper_trans, lsrc, usrc)
    whole = lambda k: (0, 0)
    block = lambda k: (k, 0, 0)
    return pl.pallas_call(
        apply_kernel,
        out_shape=jax.ShapeDtypeStruct((count, rows, rhs), BF16),
        grid=(count,),
        in_specs=[
            pl.BlockSpec(memory_space=pltpu.SMEM),
            pl.BlockSpec((rank, rhs), whole),
            pl.BlockSpec((rank, rhs), whole),
            pl.BlockSpec((1, rank, rank), block),
            pl.BlockSpec((1, rank, rhs), block),
            pl.BlockSpec((1, rank, rank), block),
            pl.BlockSpec((1, rank, rhs), block),
            pl.BlockSpec((1, rows, rhs), block),
            pl.BlockSpec((1, rows, rank), block),
            pl.BlockSpec((1, rows, rank), block),
        ],
        out_specs=pl.BlockSpec((1, rows, rhs), block),
        name="apply",
    )(flag, enter, other, lpre, lloc, upre, uloc, diag, lower_rows, upper_rows)


def solution(mesh):
    spec = P(("sep", "row"), None, None)
    return jax.shard_map(
        shards, mesh=mesh, in_specs=(spec,) * 8, out_specs=spec, check_vma=False
    )
```

```python
import jax
import jax.numpy as jnp
from jax import lax
from jax.experimental import pallas as pl
from jax.experimental.pallas import tpu as pltpu
from jax.sharding import PartitionSpec as P

F32 = jnp.float32
BF16 = jnp.bfloat16
HIGHEST = lax.Precision.HIGHEST
LIMIT = 20 * 1024 * 1024


def split_dot(matrix, value):
    high = value.astype(BF16)
    low = (value - high.astype(F32)).astype(BF16)
    return jnp.dot(matrix, high, preferred_element_type=F32) + jnp.dot(
        matrix, low, preferred_element_type=F32
    )


def sweep_kernel(
    rhs_ref, lcols_ref, ltrans_ref, ucols_ref, utrans_ref,
    lmap_ref, lsrc_ref, umap_ref, usrc_ref,
):
    count = rhs_ref.shape[0]
    lmap = lstate = umap = ustate = None
    for step in range(count):
        lk = step
        uk = count - 1 - step
        lsrc = lax.dot_general(lcols_ref[lk], rhs_ref[lk], (((0,), (0,)), ((), ())), preferred_element_type=F32)
        usrc = lax.dot_general(ucols_ref[uk], rhs_ref[uk], (((0,), (0,)), ((), ())), preferred_element_type=F32)
        lsrc_ref[lk] = lsrc
        usrc_ref[uk] = usrc
        ltrans = ltrans_ref[lk]
        utrans = utrans_ref[uk]
        if step == 0:
            lstate = lsrc
            ustate = usrc
            lmap = ltrans.astype(F32)
            umap = utrans.astype(F32)
        else:
            lstate = split_dot(ltrans, lstate) + lsrc
            ustate = split_dot(utrans, ustate) + usrc
            lmap = split_dot(ltrans, lmap)
            umap = split_dot(utrans, umap)
    rank = lmap.shape[0]
    lmap_ref[:, :rank] = lmap
    lmap_ref[:, rank:] = lstate
    umap_ref[:, :rank] = umap
    umap_ref[:, rank:] = ustate


def apply_kernel(
    flag_ref, enter_ref, other_ref, ltrans_ref, utrans_ref, lsrc_ref, usrc_ref,
    diag_ref, lrows_ref, urows_ref, out_ref, lround_ref, uround_ref,
):
    count = ltrans_ref.shape[0]
    first = flag_ref[0] == 0
    lstate = jnp.where(first, enter_ref[...], other_ref[...])
    ustate = jnp.where(first, other_ref[...], enter_ref[...])
    for step in range(count):
        lk = step
        uk = count - 1 - step
        lround_ref[lk] = lstate.astype(BF16)
        uround_ref[uk] = ustate.astype(BF16)
        if step + 1 < count:
            lstate = split_dot(ltrans_ref[lk], lstate) + lsrc_ref[lk]
            ustate = split_dot(utrans_ref[uk], ustate) + usrc_ref[uk]
    for k in range(count):
        total = diag_ref[k]
        total = total + jnp.dot(lrows_ref[k], lround_ref[k], preferred_element_type=F32)
        total = total + jnp.dot(urows_ref[k], uround_ref[k], preferred_element_type=F32)
        out_ref[k] = total.astype(out_ref.dtype)


def shifted(value, axis, count, shift, reverse):
    if reverse:
        pairs = [(i + shift, i) for i in range(count - shift)]
    else:
        pairs = [(i, i + shift) for i in range(count - shift)]
    return lax.ppermute(value, axis, pairs)


def scan_enter(summary_map, summary_state, axis, reverse):
    count = lax.axis_size(axis)
    rank = summary_map.shape[0]
    both = jnp.concatenate([summary_map, summary_state], axis=1)
    rounds = 0
    while 2 ** (rounds + 1) < count - 1:
        rounds += 1
    shift = 1
    for _ in range(rounds):
        got = shifted(both, axis, count, shift, reverse)
        joined = jnp.dot(both[:, :rank], got, precision=HIGHEST)
        both = joined + jnp.concatenate(
            [jnp.zeros_like(summary_map), both[:, rank:]], axis=1
        )
        shift *= 2
    near = shifted(both, axis, count, 1, reverse)
    far = shifted(both[:, rank:], axis, count, 1 + shift, reverse)
    return jnp.dot(near[:, :rank], far, precision=HIGHEST) + near[:, rank:]


def chip_shift(value, axis, chips, shift):
    pairs = [(2 * c, 2 * (c + shift)) for c in range(chips - shift)]
    pairs += [(2 * c + 1, 2 * (c - shift) + 1) for c in range(shift, chips)]
    return lax.ppermute(value, axis, pairs)


def scan_chips(lower, upper, axis):
    count = lax.axis_size(axis)
    chips = count // 2
    rank = lower.shape[0]
    first = lax.axis_index(axis) % 2 == 0
    own = jnp.where(first, lower, upper)
    partner = [(2 * c, 2 * c + 1) for c in range(chips)]
    partner += [(2 * c + 1, 2 * c) for c in range(chips)]
    got = lax.ppermute(jnp.where(first, upper, lower), axis, partner)
    tail = jnp.concatenate([jnp.zeros((rank, rank), F32), got[:, rank:]], axis=1)
    both = jnp.dot(got[:, :rank], own, precision=HIGHEST) + tail
    rounds = 0
    while 2 ** (rounds + 1) < chips - 1:
        rounds += 1
    shift = 1
    for _ in range(rounds):
        got = chip_shift(both, axis, chips, shift)
        tail = jnp.concatenate([jnp.zeros((rank, rank), F32), both[:, rank:]], axis=1)
        both = jnp.dot(both[:, :rank], got, precision=HIGHEST) + tail
        shift *= 2
    near = chip_shift(both, axis, chips, 1)
    far = chip_shift(both[:, rank:], axis, chips, 1 + shift)
    enter = jnp.dot(near[:, :rank], far, precision=HIGHEST) + near[:, rank:]
    send = jnp.dot(own[:, :rank], enter, precision=HIGHEST) + own[:, rank:]
    other = lax.ppermute(send, axis, partner)
    return enter, other


def group_shift(value, axis, groups, shift):
    pairs = [(4 * g + 2, 4 * (g + shift) + 2) for g in range(groups - shift)]
    pairs += [(4 * g + 1, 4 * (g - shift) + 1) for g in range(shift, groups)]
    return lax.ppermute(value, axis, pairs)


def scan_groups(own, give, axis):
    count = lax.axis_size(axis)
    groups = count // 4
    rank = own.shape[0]
    place = lax.axis_index(axis) % 4
    zeros = jnp.zeros((rank, rank), F32)
    partner = [(2 * c, 2 * c + 1) for c in range(count // 2)]
    partner += [(2 * c + 1, 2 * c) for c in range(count // 2)]
    got = lax.ppermute(give, axis, partner)
    both = jnp.dot(got[:, :rank], own, precision=HIGHEST) + jnp.concatenate(
        [zeros, got[:, rank:]], axis=1
    )
    pair = [(4 * g, 4 * g + 2) for g in range(groups)]
    pair += [(4 * g + 3, 4 * g + 1) for g in range(groups)]
    beside = lax.ppermute(both, axis, pair)
    both = jnp.dot(both[:, :rank], beside, precision=HIGHEST) + jnp.concatenate(
        [zeros, both[:, rank:]], axis=1
    )
    if groups <= 4:
        out = both[:, rank:]
        for step in range(groups - 1):
            start = group_shift(out, axis, groups, 1)
            if step + 2 < groups:
                out = jnp.dot(both[:, :rank], start, precision=HIGHEST) + both[:, rank:]
    else:
        rounds = 0
        while 2 ** (rounds + 1) < groups - 1:
            rounds += 1
        shift = 1
        for _ in range(rounds):
            got = group_shift(both, axis, groups, shift)
            tail = jnp.concatenate([zeros, both[:, rank:]], axis=1)
            both = jnp.dot(both[:, :rank], got, precision=HIGHEST) + tail
            shift *= 2
        near = group_shift(both, axis, groups, 1)
        far = group_shift(both[:, rank:], axis, groups, 1 + shift)
        start = jnp.dot(near[:, :rank], far, precision=HIGHEST) + near[:, rank:]
    back = [(4 * g + 2, 4 * g) for g in range(groups)]
    back += [(4 * g + 1, 4 * g + 3) for g in range(groups)]
    sent = lax.ppermute(start, axis, back)
    mine = jnp.dot(beside[:, :rank], start, precision=HIGHEST) + beside[:, rank:]
    holder = jnp.logical_or(place == 1, place == 2)
    enter = jnp.where(holder, mine, sent)
    send = jnp.dot(own[:, :rank], enter, precision=HIGHEST) + own[:, rank:]
    other = lax.ppermute(send, axis, partner)
    return enter, other


def shards(
    right_sides,
    diagonal_blocks,
    lower_rows,
    lower_cols,
    lower_trans,
    upper_rows,
    upper_cols,
    upper_trans,
):
    count, rows, rhs = right_sides.shape
    rank = lower_trans.shape[1]
    lboth, lsrc, uboth, usrc = pl.pallas_call(
        sweep_kernel,
        out_shape=(
            jax.ShapeDtypeStruct((rank, rank + rhs), F32),
            jax.ShapeDtypeStruct((count, rank, rhs), F32),
            jax.ShapeDtypeStruct((rank, rank + rhs), F32),
            jax.ShapeDtypeStruct((count, rank, rhs), F32),
        ),
        compiler_params=pltpu.CompilerParams(vmem_limit_bytes=LIMIT),
        name="sweep",
    )(right_sides, lower_cols, lower_trans, upper_cols, upper_trans)
    diag = jnp.einsum(
        "kab,kbc->kac", diagonal_blocks, right_sides, preferred_element_type=F32
    )
    count_row = lax.axis_size("row")
    if count_row % 4 == 0 and count_row >= 8:
        first = lax.axis_index("row") % 2 == 0
        enter, other = scan_groups(
            jnp.where(first, lboth, uboth), jnp.where(first, uboth, lboth), "row"
        )
        flag = jnp.full((1,), lax.axis_index("row") % 2, jnp.int32)
    elif count_row % 2 == 0 and count_row >= 4:
        enter, other = scan_chips(lboth, uboth, "row")
        flag = jnp.full((1,), lax.axis_index("row") % 2, jnp.int32)
    else:
        enter = scan_enter(lboth[:, :rank], lboth[:, rank:], "row", False)
        other = scan_enter(uboth[:, :rank], uboth[:, rank:], "row", True)
        flag = jnp.zeros((1,), jnp.int32)
    vmem = pl.BlockSpec(memory_space=pltpu.VMEM)
    return pl.pallas_call(
        apply_kernel,
        out_shape=jax.ShapeDtypeStruct((count, rows, rhs), BF16),
        scratch_shapes=[
            pltpu.VMEM((count, rank, rhs), BF16),
            pltpu.VMEM((count, rank, rhs), BF16),
        ],
        in_specs=[pl.BlockSpec(memory_space=pltpu.SMEM)] + [vmem] * 9,
        compiler_params=pltpu.CompilerParams(vmem_limit_bytes=LIMIT),
        name="apply",
    )(flag, enter, other, lower_trans, upper_trans, lsrc, usrc, diag, lower_rows, upper_rows)


def solution(mesh):
    spec = P(("sep", "row"), None, None)
    return jax.shard_map(
        shards, mesh=mesh, in_specs=(spec,) * 8, out_specs=spec, check_vma=False
    )
```

```python
import jax
import jax.numpy as jnp
from jax import lax
from jax.experimental import pallas as pl
from jax.experimental.pallas import tpu as pltpu
from jax.sharding import PartitionSpec as P

F32 = jnp.float32
BF16 = jnp.bfloat16
HIGHEST = lax.Precision.HIGHEST
LIMIT = 20 * 1024 * 1024


def split_dot(matrix, value):
    high = value.astype(BF16)
    low = (value - high.astype(F32)).astype(BF16)
    return jnp.dot(matrix, high, preferred_element_type=F32) + jnp.dot(
        matrix, low, preferred_element_type=F32
    )


def sweep_kernel(
    rhs_ref, lcols_ref, ltrans_ref, ucols_ref, utrans_ref,
    lmap_ref, lsrc_ref, umap_ref, usrc_ref,
):
    count = rhs_ref.shape[0]
    lmap = lstate = umap = ustate = None
    for step in range(count):
        lk = step
        uk = count - 1 - step
        lsrc = lax.dot_general(lcols_ref[lk], rhs_ref[lk], (((0,), (0,)), ((), ())), preferred_element_type=F32)
        usrc = lax.dot_general(ucols_ref[uk], rhs_ref[uk], (((0,), (0,)), ((), ())), preferred_element_type=F32)
        lsrc_ref[lk] = lsrc
        usrc_ref[uk] = usrc
        ltrans = ltrans_ref[lk]
        utrans = utrans_ref[uk]
        if step == 0:
            lstate = lsrc
            ustate = usrc
            lmap = ltrans.astype(F32)
            umap = utrans.astype(F32)
        else:
            lstate = split_dot(ltrans, lstate) + lsrc
            ustate = split_dot(utrans, ustate) + usrc
            lmap = split_dot(ltrans, lmap)
            umap = split_dot(utrans, umap)
    rank = lmap.shape[0]
    lmap_ref[:, :rank] = lmap
    lmap_ref[:, rank:] = lstate
    umap_ref[:, :rank] = umap
    umap_ref[:, rank:] = ustate


def apply_kernel(
    flag_ref, enter_ref, other_ref, ltrans_ref, utrans_ref, lsrc_ref, usrc_ref,
    diag_ref, lrows_ref, urows_ref, out_ref, lround_ref, uround_ref,
):
    count = ltrans_ref.shape[0]
    first = flag_ref[0] == 0
    lstate = jnp.where(first, enter_ref[...], other_ref[...])
    ustate = jnp.where(first, other_ref[...], enter_ref[...])
    for step in range(count):
        lk = step
        uk = count - 1 - step
        lround_ref[lk] = lstate.astype(BF16)
        uround_ref[uk] = ustate.astype(BF16)
        if step + 1 < count:
            lstate = split_dot(ltrans_ref[lk], lstate) + lsrc_ref[lk]
            ustate = split_dot(utrans_ref[uk], ustate) + usrc_ref[uk]
    for k in range(count):
        total = diag_ref[k]
        total = total + jnp.dot(lrows_ref[k], lround_ref[k], preferred_element_type=F32)
        total = total + jnp.dot(urows_ref[k], uround_ref[k], preferred_element_type=F32)
        out_ref[k] = total.astype(out_ref.dtype)


def shifted(value, axis, count, shift, reverse):
    if reverse:
        pairs = [(i + shift, i) for i in range(count - shift)]
    else:
        pairs = [(i, i + shift) for i in range(count - shift)]
    return lax.ppermute(value, axis, pairs)


def scan_enter(summary_map, summary_state, axis, reverse):
    count = lax.axis_size(axis)
    rank = summary_map.shape[0]
    both = jnp.concatenate([summary_map, summary_state], axis=1)
    rounds = 0
    while 2 ** (rounds + 1) < count - 1:
        rounds += 1
    shift = 1
    for _ in range(rounds):
        got = shifted(both, axis, count, shift, reverse)
        joined = jnp.dot(both[:, :rank], got, precision=HIGHEST)
        both = joined + jnp.concatenate(
            [jnp.zeros_like(summary_map), both[:, rank:]], axis=1
        )
        shift *= 2
    near = shifted(both, axis, count, 1, reverse)
    far = shifted(both[:, rank:], axis, count, 1 + shift, reverse)
    return jnp.dot(near[:, :rank], far, precision=HIGHEST) + near[:, rank:]


def chip_shift(value, axis, chips, shift):
    pairs = [(2 * c, 2 * (c + shift)) for c in range(chips - shift)]
    pairs += [(2 * c + 1, 2 * (c - shift) + 1) for c in range(shift, chips)]
    return lax.ppermute(value, axis, pairs)


def scan_chips(lower, upper, axis):
    count = lax.axis_size(axis)
    chips = count // 2
    rank = lower.shape[0]
    first = lax.axis_index(axis) % 2 == 0
    own = jnp.where(first, lower, upper)
    partner = [(2 * c, 2 * c + 1) for c in range(chips)]
    partner += [(2 * c + 1, 2 * c) for c in range(chips)]
    got = lax.ppermute(jnp.where(first, upper, lower), axis, partner)
    tail = jnp.concatenate([jnp.zeros((rank, rank), F32), got[:, rank:]], axis=1)
    both = jnp.dot(got[:, :rank], own, precision=HIGHEST) + tail
    rounds = 0
    while 2 ** (rounds + 1) < chips - 1:
        rounds += 1
    shift = 1
    for _ in range(rounds):
        got = chip_shift(both, axis, chips, shift)
        tail = jnp.concatenate([jnp.zeros((rank, rank), F32), both[:, rank:]], axis=1)
        both = jnp.dot(both[:, :rank], got, precision=HIGHEST) + tail
        shift *= 2
    near = chip_shift(both, axis, chips, 1)
    far = chip_shift(both[:, rank:], axis, chips, 1 + shift)
    enter = jnp.dot(near[:, :rank], far, precision=HIGHEST) + near[:, rank:]
    send = jnp.dot(own[:, :rank], enter, precision=HIGHEST) + own[:, rank:]
    other = lax.ppermute(send, axis, partner)
    return enter, other


def group_shift(value, axis, groups, shift):
    pairs = [(4 * g + 2, 4 * (g + shift) + 2) for g in range(groups - shift)]
    pairs += [(4 * g + 1, 4 * (g - shift) + 1) for g in range(shift, groups)]
    return lax.ppermute(value, axis, pairs)


def scan_groups(own, give, axis):
    count = lax.axis_size(axis)
    groups = count // 4
    rank = own.shape[0]
    place = lax.axis_index(axis) % 4
    zeros = jnp.zeros((rank, rank), F32)
    partner = [(2 * c, 2 * c + 1) for c in range(count // 2)]
    partner += [(2 * c + 1, 2 * c) for c in range(count // 2)]
    got = lax.ppermute(give, axis, partner)
    both = jnp.dot(got[:, :rank], own, precision=HIGHEST) + jnp.concatenate(
        [zeros, got[:, rank:]], axis=1
    )
    pair = [(4 * g, 4 * g + 2) for g in range(groups)]
    pair += [(4 * g + 3, 4 * g + 1) for g in range(groups)]
    beside = lax.ppermute(both, axis, pair)
    both = jnp.dot(both[:, :rank], beside, precision=HIGHEST) + jnp.concatenate(
        [zeros, both[:, rank:]], axis=1
    )
    if groups <= 4:
        out = both[:, rank:]
        for step in range(groups - 1):
            start = group_shift(out, axis, groups, 1)
            if step + 2 < groups:
                out = jnp.dot(both[:, :rank], start, precision=HIGHEST) + both[:, rank:]
    else:
        rounds = 0
        while 2 ** (rounds + 1) < groups - 1:
            rounds += 1
        shift = 1
        for _ in range(rounds):
            got = group_shift(both, axis, groups, shift)
            tail = jnp.concatenate([zeros, both[:, rank:]], axis=1)
            both = jnp.dot(both[:, :rank], got, precision=HIGHEST) + tail
            shift *= 2
        near = group_shift(both, axis, groups, 1)
        far = group_shift(both[:, rank:], axis, groups, 1 + shift)
        start = jnp.dot(near[:, :rank], far, precision=HIGHEST) + near[:, rank:]
    back = [(4 * g + 2, 4 * g) for g in range(groups)]
    back += [(4 * g + 1, 4 * g + 3) for g in range(groups)]
    sent = lax.ppermute(start, axis, back)
    mine = jnp.dot(beside[:, :rank], start, precision=HIGHEST) + beside[:, rank:]
    holder = jnp.logical_or(place == 1, place == 2)
    enter = jnp.where(holder, mine, sent)
    send = jnp.dot(own[:, :rank], enter, precision=HIGHEST) + own[:, rank:]
    other = lax.ppermute(send, axis, partner)
    return enter, other


def shards(
    right_sides,
    diagonal_blocks,
    lower_rows,
    lower_cols,
    lower_trans,
    upper_rows,
    upper_cols,
    upper_trans,
):
    count, rows, rhs = right_sides.shape
    rank = lower_trans.shape[1]
    lboth, lsrc, uboth, usrc = pl.pallas_call(
        sweep_kernel,
        out_shape=(
            jax.ShapeDtypeStruct((rank, rank + rhs), F32),
            jax.ShapeDtypeStruct((count, rank, rhs), F32),
            jax.ShapeDtypeStruct((rank, rank + rhs), F32),
            jax.ShapeDtypeStruct((count, rank, rhs), F32),
        ),
        name="sweep",
    )(right_sides, lower_cols, lower_trans, upper_cols, upper_trans)
    diag = jnp.einsum(
        "kab,kbc->kac", diagonal_blocks, right_sides, preferred_element_type=F32
    )
    count_row = lax.axis_size("row")
    if count_row % 4 == 0 and count_row >= 8:
        first = lax.axis_index("row") % 2 == 0
        enter, other = scan_groups(
            jnp.where(first, lboth, uboth), jnp.where(first, uboth, lboth), "row"
        )
        flag = jnp.full((1,), lax.axis_index("row") % 2, jnp.int32)
    elif count_row % 2 == 0 and count_row >= 4:
        enter, other = scan_chips(lboth, uboth, "row")
        flag = jnp.full((1,), lax.axis_index("row") % 2, jnp.int32)
    else:
        enter = scan_enter(lboth[:, :rank], lboth[:, rank:], "row", False)
        other = scan_enter(uboth[:, :rank], uboth[:, rank:], "row", True)
        flag = jnp.zeros((1,), jnp.int32)
    vmem = pl.BlockSpec(memory_space=pltpu.VMEM)
    return pl.pallas_call(
        apply_kernel,
        out_shape=jax.ShapeDtypeStruct((count, rows, rhs), BF16),
        scratch_shapes=[
            pltpu.VMEM((count, rank, rhs), BF16),
            pltpu.VMEM((count, rank, rhs), BF16),
        ],
        in_specs=[pl.BlockSpec(memory_space=pltpu.SMEM)] + [vmem] * 9,
        compiler_params=pltpu.CompilerParams(vmem_limit_bytes=LIMIT),
        name="apply",
    )(flag, enter, other, lower_trans, upper_trans, lsrc, usrc, diag, lower_rows, upper_rows)


def solution(mesh):
    spec = P(("sep", "row"), None, None)
    return jax.shard_map(
        shards, mesh=mesh, in_specs=(spec,) * 8, out_specs=spec, check_vma=False
    )
```

```python
import jax
import jax.numpy as jnp
from jax import lax
from jax.experimental import pallas as pl
from jax.experimental.pallas import tpu as pltpu
from jax.sharding import PartitionSpec as P

F32 = jnp.float32
BF16 = jnp.bfloat16
HIGHEST = lax.Precision.HIGHEST
LIMIT = 20 * 1024 * 1024


def split_dot(matrix, value):
    high = value.astype(BF16)
    low = (value - high.astype(F32)).astype(BF16)
    return jnp.dot(matrix, high, preferred_element_type=F32) + jnp.dot(
        matrix, low, preferred_element_type=F32
    )


def sweep_kernel(
    rhs_ref, lcols_ref, ltrans_ref, ucols_ref, utrans_ref,
    lmap_ref, lsrc_ref, umap_ref, usrc_ref,
):
    count = rhs_ref.shape[0]
    lmap = lstate = umap = ustate = None
    for step in range(count):
        lk = step
        uk = count - 1 - step
        lsrc = lax.dot_general(lcols_ref[lk], rhs_ref[lk], (((0,), (0,)), ((), ())), preferred_element_type=F32)
        usrc = lax.dot_general(ucols_ref[uk], rhs_ref[uk], (((0,), (0,)), ((), ())), preferred_element_type=F32)
        lsrc_ref[lk] = lsrc
        usrc_ref[uk] = usrc
        ltrans = ltrans_ref[lk]
        utrans = utrans_ref[uk]
        if step == 0:
            lstate = lsrc
            ustate = usrc
            lmap = ltrans.astype(F32)
            umap = utrans.astype(F32)
        else:
            lstate = split_dot(ltrans, lstate) + lsrc
            ustate = split_dot(utrans, ustate) + usrc
            lmap = split_dot(ltrans, lmap)
            umap = split_dot(utrans, umap)
    rank = lmap.shape[0]
    lmap_ref[:, :rank] = lmap
    lmap_ref[:, rank:] = lstate
    umap_ref[:, :rank] = umap
    umap_ref[:, rank:] = ustate


def apply_kernel(
    flag_ref, enter_ref, other_ref, ltrans_ref, utrans_ref, lsrc_ref, usrc_ref,
    diag_ref, rhs_ref, lrows_ref, urows_ref, out_ref, lround_ref, uround_ref,
):
    count = ltrans_ref.shape[0]
    first = flag_ref[0] == 0
    lstate = jnp.where(first, enter_ref[...], other_ref[...])
    ustate = jnp.where(first, other_ref[...], enter_ref[...])
    for step in range(count):
        lk = step
        uk = count - 1 - step
        lround_ref[lk] = lstate.astype(BF16)
        uround_ref[uk] = ustate.astype(BF16)
        if step + 1 < count:
            lstate = split_dot(ltrans_ref[lk], lstate) + lsrc_ref[lk]
            ustate = split_dot(utrans_ref[uk], ustate) + usrc_ref[uk]
    for k in range(count):
        total = jnp.dot(diag_ref[k], rhs_ref[k], preferred_element_type=F32)
        total = total + jnp.dot(lrows_ref[k], lround_ref[k], preferred_element_type=F32)
        total = total + jnp.dot(urows_ref[k], uround_ref[k], preferred_element_type=F32)
        out_ref[k] = total.astype(out_ref.dtype)


def shifted(value, axis, count, shift, reverse):
    if reverse:
        pairs = [(i + shift, i) for i in range(count - shift)]
    else:
        pairs = [(i, i + shift) for i in range(count - shift)]
    return lax.ppermute(value, axis, pairs)


def scan_enter(summary_map, summary_state, axis, reverse):
    count = lax.axis_size(axis)
    rank = summary_map.shape[0]
    both = jnp.concatenate([summary_map, summary_state], axis=1)
    rounds = 0
    while 2 ** (rounds + 1) < count - 1:
        rounds += 1
    shift = 1
    for _ in range(rounds):
        got = shifted(both, axis, count, shift, reverse)
        joined = jnp.dot(both[:, :rank], got, precision=HIGHEST)
        both = joined + jnp.concatenate(
            [jnp.zeros_like(summary_map), both[:, rank:]], axis=1
        )
        shift *= 2
    near = shifted(both, axis, count, 1, reverse)
    far = shifted(both[:, rank:], axis, count, 1 + shift, reverse)
    return jnp.dot(near[:, :rank], far, precision=HIGHEST) + near[:, rank:]


def chip_shift(value, axis, chips, shift):
    pairs = [(2 * c, 2 * (c + shift)) for c in range(chips - shift)]
    pairs += [(2 * c + 1, 2 * (c - shift) + 1) for c in range(shift, chips)]
    return lax.ppermute(value, axis, pairs)


def scan_chips(lower, upper, axis):
    count = lax.axis_size(axis)
    chips = count // 2
    rank = lower.shape[0]
    first = lax.axis_index(axis) % 2 == 0
    own = jnp.where(first, lower, upper)
    partner = [(2 * c, 2 * c + 1) for c in range(chips)]
    partner += [(2 * c + 1, 2 * c) for c in range(chips)]
    got = lax.ppermute(jnp.where(first, upper, lower), axis, partner)
    tail = jnp.concatenate([jnp.zeros((rank, rank), F32), got[:, rank:]], axis=1)
    both = jnp.dot(got[:, :rank], own, precision=HIGHEST) + tail
    rounds = 0
    while 2 ** (rounds + 1) < chips - 1:
        rounds += 1
    shift = 1
    for _ in range(rounds):
        got = chip_shift(both, axis, chips, shift)
        tail = jnp.concatenate([jnp.zeros((rank, rank), F32), both[:, rank:]], axis=1)
        both = jnp.dot(both[:, :rank], got, precision=HIGHEST) + tail
        shift *= 2
    near = chip_shift(both, axis, chips, 1)
    far = chip_shift(both[:, rank:], axis, chips, 1 + shift)
    enter = jnp.dot(near[:, :rank], far, precision=HIGHEST) + near[:, rank:]
    send = jnp.dot(own[:, :rank], enter, precision=HIGHEST) + own[:, rank:]
    other = lax.ppermute(send, axis, partner)
    return enter, other


def group_shift(value, axis, groups, shift):
    pairs = [(4 * g + 2, 4 * (g + shift) + 2) for g in range(groups - shift)]
    pairs += [(4 * g + 1, 4 * (g - shift) + 1) for g in range(shift, groups)]
    return lax.ppermute(value, axis, pairs)


def scan_groups(own, give, axis):
    count = lax.axis_size(axis)
    groups = count // 4
    rank = own.shape[0]
    place = lax.axis_index(axis) % 4
    zeros = jnp.zeros((rank, rank), F32)
    partner = [(2 * c, 2 * c + 1) for c in range(count // 2)]
    partner += [(2 * c + 1, 2 * c) for c in range(count // 2)]
    got = lax.ppermute(give, axis, partner)
    both = jnp.dot(got[:, :rank], own, precision=HIGHEST) + jnp.concatenate(
        [zeros, got[:, rank:]], axis=1
    )
    pair = [(4 * g, 4 * g + 2) for g in range(groups)]
    pair += [(4 * g + 3, 4 * g + 1) for g in range(groups)]
    beside = lax.ppermute(both, axis, pair)
    both = jnp.dot(both[:, :rank], beside, precision=HIGHEST) + jnp.concatenate(
        [zeros, both[:, rank:]], axis=1
    )
    if groups <= 4:
        out = both[:, rank:]
        for step in range(groups - 1):
            start = group_shift(out, axis, groups, 1)
            if step + 2 < groups:
                out = jnp.dot(both[:, :rank], start, precision=HIGHEST) + both[:, rank:]
    else:
        rounds = 0
        while 2 ** (rounds + 1) < groups - 1:
            rounds += 1
        shift = 1
        for _ in range(rounds):
            got = group_shift(both, axis, groups, shift)
            tail = jnp.concatenate([zeros, both[:, rank:]], axis=1)
            both = jnp.dot(both[:, :rank], got, precision=HIGHEST) + tail
            shift *= 2
        near = group_shift(both, axis, groups, 1)
        far = group_shift(both[:, rank:], axis, groups, 1 + shift)
        start = jnp.dot(near[:, :rank], far, precision=HIGHEST) + near[:, rank:]
    back = [(4 * g + 2, 4 * g) for g in range(groups)]
    back += [(4 * g + 1, 4 * g + 3) for g in range(groups)]
    sent = lax.ppermute(start, axis, back)
    mine = jnp.dot(beside[:, :rank], start, precision=HIGHEST) + beside[:, rank:]
    mine, sent = lax.optimization_barrier((mine, sent))
    holder = jnp.logical_or(place == 1, place == 2)
    enter = jnp.where(holder, mine, sent)
    send = jnp.dot(own[:, :rank], enter, precision=HIGHEST) + own[:, rank:]
    other = lax.ppermute(send, axis, partner)
    return enter, other


def shards(
    right_sides,
    diagonal_blocks,
    lower_rows,
    lower_cols,
    lower_trans,
    upper_rows,
    upper_cols,
    upper_trans,
):
    count, rows, rhs = right_sides.shape
    rank = lower_trans.shape[1]
    lboth, lsrc, uboth, usrc = pl.pallas_call(
        sweep_kernel,
        out_shape=(
            jax.ShapeDtypeStruct((rank, rank + rhs), F32),
            jax.ShapeDtypeStruct((count, rank, rhs), F32),
            jax.ShapeDtypeStruct((rank, rank + rhs), F32),
            jax.ShapeDtypeStruct((count, rank, rhs), F32),
        ),
        name="sweep",
    )(right_sides, lower_cols, lower_trans, upper_cols, upper_trans)
    count_row = lax.axis_size("row")
    if count_row % 4 == 0 and count_row >= 8:
        first = lax.axis_index("row") % 2 == 0
        enter, other = scan_groups(
            jnp.where(first, lboth, uboth), jnp.where(first, uboth, lboth), "row"
        )
        flag = jnp.full((1,), lax.axis_index("row") % 2, jnp.int32)
    elif count_row % 2 == 0 and count_row >= 4:
        enter, other = scan_chips(lboth, uboth, "row")
        flag = jnp.full((1,), lax.axis_index("row") % 2, jnp.int32)
    else:
        enter = scan_enter(lboth[:, :rank], lboth[:, rank:], "row", False)
        other = scan_enter(uboth[:, :rank], uboth[:, rank:], "row", True)
        flag = jnp.zeros((1,), jnp.int32)
    vmem = pl.BlockSpec(memory_space=pltpu.VMEM)
    return pl.pallas_call(
        apply_kernel,
        out_shape=jax.ShapeDtypeStruct((count, rows, rhs), BF16),
        scratch_shapes=[
            pltpu.VMEM((count, rank, rhs), BF16),
            pltpu.VMEM((count, rank, rhs), BF16),
        ],
        in_specs=[pl.BlockSpec(memory_space=pltpu.SMEM)] + [vmem] * 10,
        compiler_params=pltpu.CompilerParams(vmem_limit_bytes=LIMIT),
        name="apply",
    )(flag, enter, other, lower_trans, upper_trans, lsrc, usrc, diagonal_blocks, right_sides, lower_rows, upper_rows)


def solution(mesh):
    spec = P(("sep", "row"), None, None)
    return jax.shard_map(
        shards, mesh=mesh, in_specs=(spec,) * 8, out_specs=spec, check_vma=False
    )
```

```python
import jax
import jax.numpy as jnp
from jax import lax
from jax.experimental import pallas as pl
from jax.experimental.pallas import tpu as pltpu
from jax.sharding import PartitionSpec as P

F32 = jnp.float32
BF16 = jnp.bfloat16
HIGHEST = lax.Precision.HIGHEST
LIMIT = 20 * 1024 * 1024


def split_dot(matrix, value):
    high = value.astype(BF16)
    low = (value - high.astype(F32)).astype(BF16)
    return jnp.dot(matrix, high, preferred_element_type=F32) + jnp.dot(
        matrix, low, preferred_element_type=F32
    )


def sweep_kernel(
    rhs_ref, lcols_ref, ltrans_ref, ucols_ref, utrans_ref,
    lmap_ref, lsrc_hbm, umap_ref, usrc_hbm,
    lsrc_ref, usrc_ref, sems,
):
    count = rhs_ref.shape[0]
    copies = []
    lmap = lstate = umap = ustate = None
    for step in range(count):
        lk = step
        uk = count - 1 - step
        lsrc = lax.dot_general(lcols_ref[lk], rhs_ref[lk], (((0,), (0,)), ((), ())), preferred_element_type=F32)
        usrc = lax.dot_general(ucols_ref[uk], rhs_ref[uk], (((0,), (0,)), ((), ())), preferred_element_type=F32)
        lsrc_ref[lk] = lsrc
        usrc_ref[uk] = usrc
        for target, source, k, side in ((lsrc_hbm, lsrc_ref, lk, 0), (usrc_hbm, usrc_ref, uk, 1)):
            copy = pltpu.make_async_copy(source.at[k], target.at[k], sems.at[side, k])
            copy.start()
            copies.append(copy)
        ltrans = ltrans_ref[lk]
        utrans = utrans_ref[uk]
        if step == 0:
            lstate = lsrc
            ustate = usrc
            lmap = ltrans.astype(F32)
            umap = utrans.astype(F32)
        else:
            lstate = split_dot(ltrans, lstate) + lsrc
            ustate = split_dot(utrans, ustate) + usrc
            lmap = split_dot(ltrans, lmap)
            umap = split_dot(utrans, umap)
    for copy in copies:
        copy.wait()
    rank = lmap.shape[0]
    lmap_ref[:, :rank] = lmap
    lmap_ref[:, rank:] = lstate
    umap_ref[:, :rank] = umap
    umap_ref[:, rank:] = ustate


def apply_kernel(
    flag_ref, enter_ref, other_ref, ltrans_ref, utrans_ref, lsrc_ref, usrc_ref,
    diag_ref, lrows_ref, urows_ref, out_ref, lround_ref, uround_ref,
):
    count = ltrans_ref.shape[0]
    first = flag_ref[0] == 0
    lstate = jnp.where(first, enter_ref[...], other_ref[...])
    ustate = jnp.where(first, other_ref[...], enter_ref[...])
    for step in range(count):
        lk = step
        uk = count - 1 - step
        lround_ref[lk] = lstate.astype(BF16)
        uround_ref[uk] = ustate.astype(BF16)
        if step + 1 < count:
            lstate = split_dot(ltrans_ref[lk], lstate) + lsrc_ref[lk]
            ustate = split_dot(utrans_ref[uk], ustate) + usrc_ref[uk]
    for k in range(count):
        total = diag_ref[k]
        total = total + jnp.dot(lrows_ref[k], lround_ref[k], preferred_element_type=F32)
        total = total + jnp.dot(urows_ref[k], uround_ref[k], preferred_element_type=F32)
        out_ref[k] = total.astype(out_ref.dtype)


def shifted(value, axis, count, shift, reverse):
    if reverse:
        pairs = [(i + shift, i) for i in range(count - shift)]
    else:
        pairs = [(i, i + shift) for i in range(count - shift)]
    return lax.ppermute(value, axis, pairs)


def scan_enter(summary_map, summary_state, axis, reverse):
    count = lax.axis_size(axis)
    rank = summary_map.shape[0]
    both = jnp.concatenate([summary_map, summary_state], axis=1)
    rounds = 0
    while 2 ** (rounds + 1) < count - 1:
        rounds += 1
    shift = 1
    for _ in range(rounds):
        got = shifted(both, axis, count, shift, reverse)
        joined = jnp.dot(both[:, :rank], got, precision=HIGHEST)
        both = joined + jnp.concatenate(
            [jnp.zeros_like(summary_map), both[:, rank:]], axis=1
        )
        shift *= 2
    near = shifted(both, axis, count, 1, reverse)
    far = shifted(both[:, rank:], axis, count, 1 + shift, reverse)
    return jnp.dot(near[:, :rank], far, precision=HIGHEST) + near[:, rank:]


def chip_shift(value, axis, chips, shift):
    pairs = [(2 * c, 2 * (c + shift)) for c in range(chips - shift)]
    pairs += [(2 * c + 1, 2 * (c - shift) + 1) for c in range(shift, chips)]
    return lax.ppermute(value, axis, pairs)


def scan_chips(lower, upper, axis):
    count = lax.axis_size(axis)
    chips = count // 2
    rank = lower.shape[0]
    first = lax.axis_index(axis) % 2 == 0
    own = jnp.where(first, lower, upper)
    partner = [(2 * c, 2 * c + 1) for c in range(chips)]
    partner += [(2 * c + 1, 2 * c) for c in range(chips)]
    got = lax.ppermute(jnp.where(first, upper, lower), axis, partner)
    tail = jnp.concatenate([jnp.zeros((rank, rank), F32), got[:, rank:]], axis=1)
    both = jnp.dot(got[:, :rank], own, precision=HIGHEST) + tail
    rounds = 0
    while 2 ** (rounds + 1) < chips - 1:
        rounds += 1
    shift = 1
    for _ in range(rounds):
        got = chip_shift(both, axis, chips, shift)
        tail = jnp.concatenate([jnp.zeros((rank, rank), F32), both[:, rank:]], axis=1)
        both = jnp.dot(both[:, :rank], got, precision=HIGHEST) + tail
        shift *= 2
    near = chip_shift(both, axis, chips, 1)
    far = chip_shift(both[:, rank:], axis, chips, 1 + shift)
    enter = jnp.dot(near[:, :rank], far, precision=HIGHEST) + near[:, rank:]
    send = jnp.dot(own[:, :rank], enter, precision=HIGHEST) + own[:, rank:]
    other = lax.ppermute(send, axis, partner)
    return enter, other


def group_shift(value, axis, groups, shift):
    pairs = [(4 * g + 2, 4 * (g + shift) + 2) for g in range(groups - shift)]
    pairs += [(4 * g + 1, 4 * (g - shift) + 1) for g in range(shift, groups)]
    return lax.ppermute(value, axis, pairs)


def scan_groups(own, give, axis):
    count = lax.axis_size(axis)
    groups = count // 4
    rank = own.shape[0]
    place = lax.axis_index(axis) % 4
    zeros = jnp.zeros((rank, rank), F32)
    partner = [(2 * c, 2 * c + 1) for c in range(count // 2)]
    partner += [(2 * c + 1, 2 * c) for c in range(count // 2)]
    got = lax.ppermute(give, axis, partner)
    both = jnp.dot(got[:, :rank], own, precision=HIGHEST) + jnp.concatenate(
        [zeros, got[:, rank:]], axis=1
    )
    pair = [(4 * g, 4 * g + 2) for g in range(groups)]
    pair += [(4 * g + 3, 4 * g + 1) for g in range(groups)]
    beside = lax.ppermute(both, axis, pair)
    both = jnp.dot(both[:, :rank], beside, precision=HIGHEST) + jnp.concatenate(
        [zeros, both[:, rank:]], axis=1
    )
    if groups <= 4:
        out = both[:, rank:]
        for step in range(groups - 1):
            start = group_shift(out, axis, groups, 1)
            if step + 2 < groups:
                out = jnp.dot(both[:, :rank], start, precision=HIGHEST) + both[:, rank:]
    else:
        rounds = 0
        while 2 ** (rounds + 1) < groups - 1:
            rounds += 1
        shift = 1
        for _ in range(rounds):
            got = group_shift(both, axis, groups, shift)
            tail = jnp.concatenate([zeros, both[:, rank:]], axis=1)
            both = jnp.dot(both[:, :rank], got, precision=HIGHEST) + tail
            shift *= 2
        near = group_shift(both, axis, groups, 1)
        far = group_shift(both[:, rank:], axis, groups, 1 + shift)
        start = jnp.dot(near[:, :rank], far, precision=HIGHEST) + near[:, rank:]
    back = [(4 * g + 2, 4 * g) for g in range(groups)]
    back += [(4 * g + 1, 4 * g + 3) for g in range(groups)]
    sent = lax.ppermute(start, axis, back)
    mine = jnp.dot(beside[:, :rank], start, precision=HIGHEST) + beside[:, rank:]
    holder = jnp.logical_or(place == 1, place == 2)
    enter = jnp.where(holder, mine, sent)
    send = jnp.dot(own[:, :rank], enter, precision=HIGHEST) + own[:, rank:]
    other = lax.ppermute(send, axis, partner)
    return enter, other


def shards(
    right_sides,
    diagonal_blocks,
    lower_rows,
    lower_cols,
    lower_trans,
    upper_rows,
    upper_cols,
    upper_trans,
):
    count, rows, rhs = right_sides.shape
    rank = lower_trans.shape[1]
    lboth, lsrc, uboth, usrc = pl.pallas_call(
        sweep_kernel,
        out_shape=(
            jax.ShapeDtypeStruct((rank, rank + rhs), F32),
            jax.ShapeDtypeStruct((count, rank, rhs), F32),
            jax.ShapeDtypeStruct((rank, rank + rhs), F32),
            jax.ShapeDtypeStruct((count, rank, rhs), F32),
        ),
        out_specs=(
            pl.BlockSpec(memory_space=pltpu.VMEM),
            pl.BlockSpec(memory_space=pl.ANY),
            pl.BlockSpec(memory_space=pltpu.VMEM),
            pl.BlockSpec(memory_space=pl.ANY),
        ),
        scratch_shapes=[
            pltpu.VMEM((count, rank, rhs), F32),
            pltpu.VMEM((count, rank, rhs), F32),
            pltpu.SemaphoreType.DMA((2, count)),
        ],
        name="sweep",
    )(right_sides, lower_cols, lower_trans, upper_cols, upper_trans)
    diag = jnp.einsum(
        "kab,kbc->kac", diagonal_blocks, right_sides, preferred_element_type=F32
    )
    count_row = lax.axis_size("row")
    if count_row % 4 == 0 and count_row >= 8:
        first = lax.axis_index("row") % 2 == 0
        enter, other = scan_groups(
            jnp.where(first, lboth, uboth), jnp.where(first, uboth, lboth), "row"
        )
        flag = jnp.full((1,), lax.axis_index("row") % 2, jnp.int32)
    elif count_row % 2 == 0 and count_row >= 4:
        enter, other = scan_chips(lboth, uboth, "row")
        flag = jnp.full((1,), lax.axis_index("row") % 2, jnp.int32)
    else:
        enter = scan_enter(lboth[:, :rank], lboth[:, rank:], "row", False)
        other = scan_enter(uboth[:, :rank], uboth[:, rank:], "row", True)
        flag = jnp.zeros((1,), jnp.int32)
    vmem = pl.BlockSpec(memory_space=pltpu.VMEM)
    return pl.pallas_call(
        apply_kernel,
        out_shape=jax.ShapeDtypeStruct((count, rows, rhs), BF16),
        scratch_shapes=[
            pltpu.VMEM((count, rank, rhs), BF16),
            pltpu.VMEM((count, rank, rhs), BF16),
        ],
        in_specs=[pl.BlockSpec(memory_space=pltpu.SMEM)] + [vmem] * 9,
        compiler_params=pltpu.CompilerParams(vmem_limit_bytes=LIMIT),
        name="apply",
    )(flag, enter, other, lower_trans, upper_trans, lsrc, usrc, diag, lower_rows, upper_rows)


def solution(mesh):
    spec = P(("sep", "row"), None, None)
    return jax.shard_map(
        shards, mesh=mesh, in_specs=(spec,) * 8, out_specs=spec, check_vma=False
    )
```

```python
import jax
import jax.numpy as jnp
from jax import lax
from jax.experimental import pallas as pl
from jax.experimental.pallas import tpu as pltpu
from jax.sharding import PartitionSpec as P

F32 = jnp.float32
BF16 = jnp.bfloat16
HIGHEST = lax.Precision.HIGHEST
LIMIT = 20 * 1024 * 1024


def split_dot(matrix, value):
    high = value.astype(BF16)
    low = (value - high.astype(F32)).astype(BF16)
    return jnp.dot(matrix, high, preferred_element_type=F32) + jnp.dot(
        matrix, low, preferred_element_type=F32
    )


def sweep_kernel(
    rhs_ref, lcols_ref, ltrans_ref, ucols_ref, utrans_ref,
    lmap_ref, lsrc_ref, umap_ref, usrc_ref,
):
    count = rhs_ref.shape[0]
    lmap = lstate = umap = ustate = None
    for step in range(count):
        lk = step
        uk = count - 1 - step
        lsrc = lax.dot_general(lcols_ref[lk], rhs_ref[lk], (((0,), (0,)), ((), ())), preferred_element_type=F32)
        usrc = lax.dot_general(ucols_ref[uk], rhs_ref[uk], (((0,), (0,)), ((), ())), preferred_element_type=F32)
        lsrc_ref[lk] = lsrc
        usrc_ref[uk] = usrc
        ltrans = ltrans_ref[lk]
        utrans = utrans_ref[uk]
        if step == 0:
            lstate = lsrc
            ustate = usrc
            lmap = ltrans.astype(F32)
            umap = utrans.astype(F32)
        else:
            lstate = split_dot(ltrans, lstate) + lsrc
            ustate = split_dot(utrans, ustate) + usrc
            lmap = split_dot(ltrans, lmap)
            umap = split_dot(utrans, umap)
    rank = lmap.shape[0]
    lmap_ref[:, :rank] = lmap
    lmap_ref[:, rank:] = lstate
    umap_ref[:, :rank] = umap
    umap_ref[:, rank:] = ustate


def apply_kernel(
    flag_ref, enter_ref, other_ref, ltrans_ref, utrans_ref, lsrc_ref, usrc_ref,
    diag_ref, lrows_ref, urows_ref, out_ref, lround_ref, uround_ref,
):
    count = ltrans_ref.shape[0]
    first = flag_ref[0] == 0
    lstate = jnp.where(first, enter_ref[...], other_ref[...])
    ustate = jnp.where(first, other_ref[...], enter_ref[...])
    for step in range(count):
        lk = step
        uk = count - 1 - step
        lround_ref[lk] = lstate.astype(BF16)
        uround_ref[uk] = ustate.astype(BF16)
        if step + 1 < count:
            lstate = split_dot(ltrans_ref[lk], lstate) + lsrc_ref[lk]
            ustate = split_dot(utrans_ref[uk], ustate) + usrc_ref[uk]
    for k in range(count):
        total = diag_ref[k]
        total = total + jnp.dot(lrows_ref[k], lround_ref[k], preferred_element_type=F32)
        total = total + jnp.dot(urows_ref[k], uround_ref[k], preferred_element_type=F32)
        out_ref[k] = total.astype(out_ref.dtype)


def shifted(value, axis, count, shift, reverse):
    if reverse:
        pairs = [(i + shift, i) for i in range(count - shift)]
    else:
        pairs = [(i, i + shift) for i in range(count - shift)]
    return lax.ppermute(value, axis, pairs)


def scan_enter(summary_map, summary_state, axis, reverse):
    count = lax.axis_size(axis)
    rank = summary_map.shape[0]
    both = jnp.concatenate([summary_map, summary_state], axis=1)
    rounds = 0
    while 2 ** (rounds + 1) < count - 1:
        rounds += 1
    shift = 1
    for _ in range(rounds):
        got = shifted(both, axis, count, shift, reverse)
        joined = jnp.dot(both[:, :rank], got, precision=HIGHEST)
        both = joined + jnp.concatenate(
            [jnp.zeros_like(summary_map), both[:, rank:]], axis=1
        )
        shift *= 2
    near = shifted(both, axis, count, 1, reverse)
    far = shifted(both[:, rank:], axis, count, 1 + shift, reverse)
    return jnp.dot(near[:, :rank], far, precision=HIGHEST) + near[:, rank:]


def chip_shift(value, axis, chips, shift):
    pairs = [(2 * c, 2 * (c + shift)) for c in range(chips - shift)]
    pairs += [(2 * c + 1, 2 * (c - shift) + 1) for c in range(shift, chips)]
    return lax.ppermute(value, axis, pairs)


def scan_chips(lower, upper, axis):
    count = lax.axis_size(axis)
    chips = count // 2
    rank = lower.shape[0]
    first = lax.axis_index(axis) % 2 == 0
    own = jnp.where(first, lower, upper)
    partner = [(2 * c, 2 * c + 1) for c in range(chips)]
    partner += [(2 * c + 1, 2 * c) for c in range(chips)]
    got = lax.ppermute(jnp.where(first, upper, lower), axis, partner)
    tail = jnp.concatenate([jnp.zeros((rank, rank), F32), got[:, rank:]], axis=1)
    both = jnp.dot(got[:, :rank], own, precision=HIGHEST) + tail
    rounds = 0
    while 2 ** (rounds + 1) < chips - 1:
        rounds += 1
    shift = 1
    for _ in range(rounds):
        got = chip_shift(both, axis, chips, shift)
        tail = jnp.concatenate([jnp.zeros((rank, rank), F32), both[:, rank:]], axis=1)
        both = jnp.dot(both[:, :rank], got, precision=HIGHEST) + tail
        shift *= 2
    near = chip_shift(both, axis, chips, 1)
    far = chip_shift(both[:, rank:], axis, chips, 1 + shift)
    enter = jnp.dot(near[:, :rank], far, precision=HIGHEST) + near[:, rank:]
    send = jnp.dot(own[:, :rank], enter, precision=HIGHEST) + own[:, rank:]
    other = lax.ppermute(send, axis, partner)
    return enter, other


def group_shift(value, axis, groups, shift):
    pairs = [(4 * g + 2, 4 * (g + shift) + 2) for g in range(groups - shift)]
    pairs += [(4 * g + 1, 4 * (g - shift) + 1) for g in range(shift, groups)]
    return lax.ppermute(value, axis, pairs)


def scan_groups(own, give, axis):
    count = lax.axis_size(axis)
    groups = count // 4
    rank = own.shape[0]
    place = lax.axis_index(axis) % 4
    zeros = jnp.zeros((rank, rank), F32)
    partner = [(2 * c, 2 * c + 1) for c in range(count // 2)]
    partner += [(2 * c + 1, 2 * c) for c in range(count // 2)]
    got = lax.ppermute(give, axis, partner)
    both = jnp.dot(got[:, :rank], own, precision=HIGHEST) + jnp.concatenate(
        [zeros, got[:, rank:]], axis=1
    )
    pair = [(4 * g, 4 * g + 2) for g in range(groups)]
    pair += [(4 * g + 3, 4 * g + 1) for g in range(groups)]
    beside_state = lax.ppermute(both[:, rank:], axis, pair)
    beside_map = lax.ppermute(both[:, :rank], axis, pair)
    group_state = jnp.dot(both[:, :rank], beside_state, precision=HIGHEST) + both[:, rank:]
    group_map = jnp.dot(both[:, :rank], beside_map, precision=HIGHEST)
    beside = jnp.concatenate([beside_map, beside_state], axis=1)
    both = jnp.concatenate([group_map, group_state], axis=1)
    if groups <= 4:
        out = group_state
        for step in range(groups - 1):
            start = group_shift(out, axis, groups, 1)
            if step + 2 < groups:
                out = jnp.dot(group_map, start, precision=HIGHEST) + group_state
    else:
        rounds = 0
        while 2 ** (rounds + 1) < groups - 1:
            rounds += 1
        shift = 1
        for _ in range(rounds):
            got = group_shift(both, axis, groups, shift)
            tail = jnp.concatenate([zeros, both[:, rank:]], axis=1)
            both = jnp.dot(both[:, :rank], got, precision=HIGHEST) + tail
            shift *= 2
        near = group_shift(both, axis, groups, 1)
        far = group_shift(both[:, rank:], axis, groups, 1 + shift)
        start = jnp.dot(near[:, :rank], far, precision=HIGHEST) + near[:, rank:]
    back = [(4 * g + 2, 4 * g) for g in range(groups)]
    back += [(4 * g + 1, 4 * g + 3) for g in range(groups)]
    sent = lax.ppermute(start, axis, back)
    mine = jnp.dot(beside_map, start, precision=HIGHEST) + beside_state
    holder = jnp.logical_or(place == 1, place == 2)
    enter = jnp.where(holder, mine, sent)
    send = jnp.dot(own[:, :rank], enter, precision=HIGHEST) + own[:, rank:]
    other = lax.ppermute(send, axis, partner)
    return enter, other


def shards(
    right_sides,
    diagonal_blocks,
    lower_rows,
    lower_cols,
    lower_trans,
    upper_rows,
    upper_cols,
    upper_trans,
):
    count, rows, rhs = right_sides.shape
    rank = lower_trans.shape[1]
    lboth, lsrc, uboth, usrc = pl.pallas_call(
        sweep_kernel,
        out_shape=(
            jax.ShapeDtypeStruct((rank, rank + rhs), F32),
            jax.ShapeDtypeStruct((count, rank, rhs), F32),
            jax.ShapeDtypeStruct((rank, rank + rhs), F32),
            jax.ShapeDtypeStruct((count, rank, rhs), F32),
        ),
        name="sweep",
    )(right_sides, lower_cols, lower_trans, upper_cols, upper_trans)
    diag = jnp.einsum(
        "kab,kbc->kac", diagonal_blocks, right_sides, preferred_element_type=F32
    )
    count_row = lax.axis_size("row")
    if count_row % 4 == 0 and count_row >= 8:
        first = lax.axis_index("row") % 2 == 0
        enter, other = scan_groups(
            jnp.where(first, lboth, uboth), jnp.where(first, uboth, lboth), "row"
        )
        flag = jnp.full((1,), lax.axis_index("row") % 2, jnp.int32)
    elif count_row % 2 == 0 and count_row >= 4:
        enter, other = scan_chips(lboth, uboth, "row")
        flag = jnp.full((1,), lax.axis_index("row") % 2, jnp.int32)
    else:
        enter = scan_enter(lboth[:, :rank], lboth[:, rank:], "row", False)
        other = scan_enter(uboth[:, :rank], uboth[:, rank:], "row", True)
        flag = jnp.zeros((1,), jnp.int32)
    vmem = pl.BlockSpec(memory_space=pltpu.VMEM)
    return pl.pallas_call(
        apply_kernel,
        out_shape=jax.ShapeDtypeStruct((count, rows, rhs), BF16),
        scratch_shapes=[
            pltpu.VMEM((count, rank, rhs), BF16),
            pltpu.VMEM((count, rank, rhs), BF16),
        ],
        in_specs=[pl.BlockSpec(memory_space=pltpu.SMEM)] + [vmem] * 9,
        compiler_params=pltpu.CompilerParams(vmem_limit_bytes=LIMIT),
        name="apply",
    )(flag, enter, other, lower_trans, upper_trans, lsrc, usrc, diag, lower_rows, upper_rows)


def solution(mesh):
    spec = P(("sep", "row"), None, None)
    return jax.shard_map(
        shards, mesh=mesh, in_specs=(spec,) * 8, out_specs=spec, check_vma=False
    )
```

```python
import jax
import jax.numpy as jnp
from jax import lax
from jax.experimental import pallas as pl
from jax.experimental.pallas import tpu as pltpu
from jax.sharding import PartitionSpec as P

F32 = jnp.float32
BF16 = jnp.bfloat16
HIGHEST = lax.Precision.HIGHEST
LIMIT = 20 * 1024 * 1024


def split_dot(matrix, value):
    high = value.astype(BF16)
    low = (value - high.astype(F32)).astype(BF16)
    return jnp.dot(matrix, high, preferred_element_type=F32) + jnp.dot(
        matrix, low, preferred_element_type=F32
    )


def sweep_kernel(
    rhs_ref, lcols_ref, ltrans_ref, ucols_ref, utrans_ref,
    lmap_ref, lsrc_ref, umap_ref, usrc_ref,
):
    count = rhs_ref.shape[0]
    lmap = lstate = umap = ustate = None
    for step in range(count):
        lk = step
        uk = count - 1 - step
        lsrc = lax.dot_general(lcols_ref[lk], rhs_ref[lk], (((0,), (0,)), ((), ())), preferred_element_type=F32)
        usrc = lax.dot_general(ucols_ref[uk], rhs_ref[uk], (((0,), (0,)), ((), ())), preferred_element_type=F32)
        lsrc_ref[lk] = lsrc
        usrc_ref[uk] = usrc
        ltrans = ltrans_ref[lk]
        utrans = utrans_ref[uk]
        if step == 0:
            lstate = lsrc
            ustate = usrc
            lmap = ltrans.astype(F32)
            umap = utrans.astype(F32)
        else:
            lstate = split_dot(ltrans, lstate) + lsrc
            ustate = split_dot(utrans, ustate) + usrc
            lmap = split_dot(ltrans, lmap)
            umap = split_dot(utrans, umap)
    rank = lmap.shape[0]
    lmap_ref[:, :rank] = lmap
    lmap_ref[:, rank:] = lstate
    umap_ref[:, :rank] = umap
    umap_ref[:, rank:] = ustate


def apply_kernel(
    flag_ref, enter_ref, other_ref, ltrans_ref, utrans_ref, lsrc_ref, usrc_ref,
    diag_ref, lrows_ref, urows_ref, out_ref, lround_ref, uround_ref,
):
    count = ltrans_ref.shape[0]
    first = flag_ref[0] == 0
    lstate = jnp.where(first, enter_ref[...], other_ref[...])
    ustate = jnp.where(first, other_ref[...], enter_ref[...])
    for step in range(count):
        lk = step
        uk = count - 1 - step
        lround_ref[lk] = lstate.astype(BF16)
        uround_ref[uk] = ustate.astype(BF16)
        if step + 1 < count:
            lstate = split_dot(ltrans_ref[lk], lstate) + lsrc_ref[lk]
            ustate = split_dot(utrans_ref[uk], ustate) + usrc_ref[uk]
    for k in range(count):
        total = diag_ref[k]
        total = total + jnp.dot(lrows_ref[k], lround_ref[k], preferred_element_type=F32)
        total = total + jnp.dot(urows_ref[k], uround_ref[k], preferred_element_type=F32)
        out_ref[k] = total.astype(out_ref.dtype)


def shifted(value, axis, count, shift, reverse):
    if reverse:
        pairs = [(i + shift, i) for i in range(count - shift)]
    else:
        pairs = [(i, i + shift) for i in range(count - shift)]
    return lax.ppermute(value, axis, pairs)


def scan_enter(summary_map, summary_state, axis, reverse):
    count = lax.axis_size(axis)
    rank = summary_map.shape[0]
    both = jnp.concatenate([summary_map, summary_state], axis=1)
    rounds = 0
    while 2 ** (rounds + 1) < count - 1:
        rounds += 1
    shift = 1
    for _ in range(rounds):
        got = shifted(both, axis, count, shift, reverse)
        joined = jnp.dot(both[:, :rank], got, precision=HIGHEST)
        both = joined + jnp.concatenate(
            [jnp.zeros_like(summary_map), both[:, rank:]], axis=1
        )
        shift *= 2
    near = shifted(both, axis, count, 1, reverse)
    far = shifted(both[:, rank:], axis, count, 1 + shift, reverse)
    return jnp.dot(near[:, :rank], far, precision=HIGHEST) + near[:, rank:]


def chip_shift(value, axis, chips, shift):
    pairs = [(2 * c, 2 * (c + shift)) for c in range(chips - shift)]
    pairs += [(2 * c + 1, 2 * (c - shift) + 1) for c in range(shift, chips)]
    return lax.ppermute(value, axis, pairs)


def scan_chips(lower, upper, axis):
    count = lax.axis_size(axis)
    chips = count // 2
    rank = lower.shape[0]
    first = lax.axis_index(axis) % 2 == 0
    own = jnp.where(first, lower, upper)
    partner = [(2 * c, 2 * c + 1) for c in range(chips)]
    partner += [(2 * c + 1, 2 * c) for c in range(chips)]
    got = lax.ppermute(jnp.where(first, upper, lower), axis, partner)
    tail = jnp.concatenate([jnp.zeros((rank, rank), F32), got[:, rank:]], axis=1)
    both = jnp.dot(got[:, :rank], own, precision=HIGHEST) + tail
    rounds = 0
    while 2 ** (rounds + 1) < chips - 1:
        rounds += 1
    shift = 1
    for _ in range(rounds):
        got = chip_shift(both, axis, chips, shift)
        tail = jnp.concatenate([jnp.zeros((rank, rank), F32), both[:, rank:]], axis=1)
        both = jnp.dot(both[:, :rank], got, precision=HIGHEST) + tail
        shift *= 2
    near = chip_shift(both, axis, chips, 1)
    far = chip_shift(both[:, rank:], axis, chips, 1 + shift)
    enter = jnp.dot(near[:, :rank], far, precision=HIGHEST) + near[:, rank:]
    send = jnp.dot(own[:, :rank], enter, precision=HIGHEST) + own[:, rank:]
    other = lax.ppermute(send, axis, partner)
    return enter, other


def group_shift(value, axis, groups, shift):
    pairs = [(4 * g + 2, 4 * (g + shift) + 2) for g in range(groups - shift)]
    pairs += [(4 * g + 1, 4 * (g - shift) + 1) for g in range(shift, groups)]
    return lax.ppermute(value, axis, pairs)


def scan_groups(own, give, axis):
    count = lax.axis_size(axis)
    groups = count // 4
    rank = own.shape[0]
    place = lax.axis_index(axis) % 4
    zeros = jnp.zeros((rank, rank), F32)
    partner = [(2 * c, 2 * c + 1) for c in range(count // 2)]
    partner += [(2 * c + 1, 2 * c) for c in range(count // 2)]
    got = lax.ppermute(give, axis, partner)
    both = jnp.dot(got[:, :rank], own, precision=HIGHEST) + jnp.concatenate(
        [zeros, got[:, rank:]], axis=1
    )
    pair = [(4 * g, 4 * g + 2) for g in range(groups)]
    pair += [(4 * g + 3, 4 * g + 1) for g in range(groups)]
    early = [(4 * g, 4 * g + 2) for g in range(groups)]
    early += [(4 * g + 3, 4 * g + 1) for g in range(groups)]
    far_own = lax.ppermute(own, axis, early)
    beside_state = lax.ppermute(both[:, rank:], axis, pair)
    beside_map = lax.ppermute(both[:, :rank], axis, pair)
    group_state = jnp.dot(both[:, :rank], beside_state, precision=HIGHEST) + both[:, rank:]
    group_map = jnp.dot(both[:, :rank], beside_map, precision=HIGHEST)
    beside = jnp.concatenate([beside_map, beside_state], axis=1)
    both = jnp.concatenate([group_map, group_state], axis=1)
    if groups <= 4:
        out = group_state
        for step in range(groups - 1):
            start = group_shift(out, axis, groups, 1)
            if step + 2 < groups:
                out = jnp.dot(group_map, start, precision=HIGHEST) + group_state
    else:
        rounds = 0
        while 2 ** (rounds + 1) < groups - 1:
            rounds += 1
        shift = 1
        for _ in range(rounds):
            got = group_shift(both, axis, groups, shift)
            tail = jnp.concatenate([zeros, both[:, rank:]], axis=1)
            both = jnp.dot(both[:, :rank], got, precision=HIGHEST) + tail
            shift *= 2
        near = group_shift(both, axis, groups, 1)
        far = group_shift(both[:, rank:], axis, groups, 1 + shift)
        start = jnp.dot(near[:, :rank], far, precision=HIGHEST) + near[:, rank:]
    back = [(4 * g + 2, 4 * g) for g in range(groups)]
    back += [(4 * g + 1, 4 * g + 3) for g in range(groups)]
    cross = [(4 * g + 2, 4 * g + 1) for g in range(groups)]
    cross += [(4 * g + 1, 4 * g + 2) for g in range(groups)]
    inner = [(4 * g + 2, 4 * g + 3) for g in range(groups)]
    inner += [(4 * g + 1, 4 * g) for g in range(groups)]
    mine = jnp.dot(beside_map, start, precision=HIGHEST) + beside_state
    crossed = jnp.dot(far_own[:, :rank], start, precision=HIGHEST) + far_own[:, rank:]
    inside = jnp.dot(own[:, :rank], mine, precision=HIGHEST) + own[:, rank:]
    sent = lax.ppermute(start, axis, back)
    got_cross = lax.ppermute(crossed, axis, cross)
    got_inner = lax.ppermute(inside, axis, inner)
    holder = jnp.logical_or(place == 1, place == 2)
    enter = jnp.where(holder, mine, sent)
    other = jnp.where(holder, got_cross, got_inner)
    return enter, other


def shards(
    right_sides,
    diagonal_blocks,
    lower_rows,
    lower_cols,
    lower_trans,
    upper_rows,
    upper_cols,
    upper_trans,
):
    count, rows, rhs = right_sides.shape
    rank = lower_trans.shape[1]
    lboth, lsrc, uboth, usrc = pl.pallas_call(
        sweep_kernel,
        out_shape=(
            jax.ShapeDtypeStruct((rank, rank + rhs), F32),
            jax.ShapeDtypeStruct((count, rank, rhs), F32),
            jax.ShapeDtypeStruct((rank, rank + rhs), F32),
            jax.ShapeDtypeStruct((count, rank, rhs), F32),
        ),
        name="sweep",
    )(right_sides, lower_cols, lower_trans, upper_cols, upper_trans)
    diag = jnp.einsum(
        "kab,kbc->kac", diagonal_blocks, right_sides, preferred_element_type=F32
    )
    count_row = lax.axis_size("row")
    if count_row % 4 == 0 and count_row >= 8:
        first = lax.axis_index("row") % 2 == 0
        enter, other = scan_groups(
            jnp.where(first, lboth, uboth), jnp.where(first, uboth, lboth), "row"
        )
        flag = jnp.full((1,), lax.axis_index("row") % 2, jnp.int32)
    elif count_row % 2 == 0 and count_row >= 4:
        enter, other = scan_chips(lboth, uboth, "row")
        flag = jnp.full((1,), lax.axis_index("row") % 2, jnp.int32)
    else:
        enter = scan_enter(lboth[:, :rank], lboth[:, rank:], "row", False)
        other = scan_enter(uboth[:, :rank], uboth[:, rank:], "row", True)
        flag = jnp.zeros((1,), jnp.int32)
    vmem = pl.BlockSpec(memory_space=pltpu.VMEM)
    return pl.pallas_call(
        apply_kernel,
        out_shape=jax.ShapeDtypeStruct((count, rows, rhs), BF16),
        scratch_shapes=[
            pltpu.VMEM((count, rank, rhs), BF16),
            pltpu.VMEM((count, rank, rhs), BF16),
        ],
        in_specs=[pl.BlockSpec(memory_space=pltpu.SMEM)] + [vmem] * 9,
        compiler_params=pltpu.CompilerParams(vmem_limit_bytes=LIMIT),
        name="apply",
    )(flag, enter, other, lower_trans, upper_trans, lsrc, usrc, diag, lower_rows, upper_rows)


def solution(mesh):
    spec = P(("sep", "row"), None, None)
    return jax.shard_map(
        shards, mesh=mesh, in_specs=(spec,) * 8, out_specs=spec, check_vma=False
    )
```

```python
import jax
import jax.numpy as jnp
from jax import lax
from jax.experimental import pallas as pl
from jax.experimental.pallas import tpu as pltpu
from jax.sharding import PartitionSpec as P

F32 = jnp.float32
BF16 = jnp.bfloat16
HIGHEST = lax.Precision.HIGHEST
LIMIT = 20 * 1024 * 1024


def split_dot(matrix, value):
    high = value.astype(BF16)
    low = (value - high.astype(F32)).astype(BF16)
    return jnp.dot(matrix, high, preferred_element_type=F32) + jnp.dot(
        matrix, low, preferred_element_type=F32
    )


def sweep_kernel(
    flag_ref, rhs_ref, lcols_ref, ltrans_ref, ucols_ref, utrans_ref,
    lmap_ref, lsrc_ref, umap_ref, usrc_ref,
):
    count = rhs_ref.shape[0]
    lmap = lstate = umap = ustate = None
    for step in range(count):
        lk = step
        uk = count - 1 - step
        lsrc = lax.dot_general(lcols_ref[lk], rhs_ref[lk], (((0,), (0,)), ((), ())), preferred_element_type=F32)
        usrc = lax.dot_general(ucols_ref[uk], rhs_ref[uk], (((0,), (0,)), ((), ())), preferred_element_type=F32)
        lsrc_ref[lk] = lsrc
        usrc_ref[uk] = usrc
        ltrans = ltrans_ref[lk]
        utrans = utrans_ref[uk]
        if step == 0:
            lstate = lsrc
            ustate = usrc
            lmap = ltrans.astype(F32)
            umap = utrans.astype(F32)
        else:
            lstate = split_dot(ltrans, lstate) + lsrc
            ustate = split_dot(utrans, ustate) + usrc
            lmap = split_dot(ltrans, lmap)
            umap = split_dot(utrans, umap)
    rank = lmap.shape[0]
    first = flag_ref[0] == 0

    @pl.when(first)
    def _():
        lmap_ref[:, :rank] = lmap
        lmap_ref[:, rank:] = lstate
        umap_ref[:, :rank] = umap
        umap_ref[:, rank:] = ustate

    @pl.when(jnp.logical_not(first))
    def _():
        lmap_ref[:, :rank] = umap
        lmap_ref[:, rank:] = ustate
        umap_ref[:, :rank] = lmap
        umap_ref[:, rank:] = lstate


def apply_kernel(
    flag_ref, enter_ref, other_ref, ltrans_ref, utrans_ref, lsrc_ref, usrc_ref,
    diag_ref, lrows_ref, urows_ref, out_ref, lround_ref, uround_ref,
):
    count = ltrans_ref.shape[0]
    first = flag_ref[0] == 0
    lstate = jnp.where(first, enter_ref[...], other_ref[...])
    ustate = jnp.where(first, other_ref[...], enter_ref[...])
    for step in range(count):
        lk = step
        uk = count - 1 - step
        lround_ref[lk] = lstate.astype(BF16)
        uround_ref[uk] = ustate.astype(BF16)
        if step + 1 < count:
            lstate = split_dot(ltrans_ref[lk], lstate) + lsrc_ref[lk]
            ustate = split_dot(utrans_ref[uk], ustate) + usrc_ref[uk]
    for k in range(count):
        total = diag_ref[k]
        total = total + jnp.dot(lrows_ref[k], lround_ref[k], preferred_element_type=F32)
        total = total + jnp.dot(urows_ref[k], uround_ref[k], preferred_element_type=F32)
        out_ref[k] = total.astype(out_ref.dtype)


def shifted(value, axis, count, shift, reverse):
    if reverse:
        pairs = [(i + shift, i) for i in range(count - shift)]
    else:
        pairs = [(i, i + shift) for i in range(count - shift)]
    return lax.ppermute(value, axis, pairs)


def scan_enter(summary_map, summary_state, axis, reverse):
    count = lax.axis_size(axis)
    rank = summary_map.shape[0]
    both = jnp.concatenate([summary_map, summary_state], axis=1)
    rounds = 0
    while 2 ** (rounds + 1) < count - 1:
        rounds += 1
    shift = 1
    for _ in range(rounds):
        got = shifted(both, axis, count, shift, reverse)
        joined = jnp.dot(both[:, :rank], got, precision=HIGHEST)
        both = joined + jnp.concatenate(
            [jnp.zeros_like(summary_map), both[:, rank:]], axis=1
        )
        shift *= 2
    near = shifted(both, axis, count, 1, reverse)
    far = shifted(both[:, rank:], axis, count, 1 + shift, reverse)
    return jnp.dot(near[:, :rank], far, precision=HIGHEST) + near[:, rank:]


def chip_shift(value, axis, chips, shift):
    pairs = [(2 * c, 2 * (c + shift)) for c in range(chips - shift)]
    pairs += [(2 * c + 1, 2 * (c - shift) + 1) for c in range(shift, chips)]
    return lax.ppermute(value, axis, pairs)


def scan_chips(lower, upper, axis):
    count = lax.axis_size(axis)
    chips = count // 2
    rank = lower.shape[0]
    first = lax.axis_index(axis) % 2 == 0
    own = jnp.where(first, lower, upper)
    partner = [(2 * c, 2 * c + 1) for c in range(chips)]
    partner += [(2 * c + 1, 2 * c) for c in range(chips)]
    got = lax.ppermute(jnp.where(first, upper, lower), axis, partner)
    tail = jnp.concatenate([jnp.zeros((rank, rank), F32), got[:, rank:]], axis=1)
    both = jnp.dot(got[:, :rank], own, precision=HIGHEST) + tail
    rounds = 0
    while 2 ** (rounds + 1) < chips - 1:
        rounds += 1
    shift = 1
    for _ in range(rounds):
        got = chip_shift(both, axis, chips, shift)
        tail = jnp.concatenate([jnp.zeros((rank, rank), F32), both[:, rank:]], axis=1)
        both = jnp.dot(both[:, :rank], got, precision=HIGHEST) + tail
        shift *= 2
    near = chip_shift(both, axis, chips, 1)
    far = chip_shift(both[:, rank:], axis, chips, 1 + shift)
    enter = jnp.dot(near[:, :rank], far, precision=HIGHEST) + near[:, rank:]
    send = jnp.dot(own[:, :rank], enter, precision=HIGHEST) + own[:, rank:]
    other = lax.ppermute(send, axis, partner)
    return enter, other


def group_shift(value, axis, groups, shift):
    pairs = [(4 * g + 2, 4 * (g + shift) + 2) for g in range(groups - shift)]
    pairs += [(4 * g + 1, 4 * (g - shift) + 1) for g in range(shift, groups)]
    return lax.ppermute(value, axis, pairs)


def scan_groups(own, give, axis):
    count = lax.axis_size(axis)
    groups = count // 4
    rank = own.shape[0]
    place = lax.axis_index(axis) % 4
    zeros = jnp.zeros((rank, rank), F32)
    partner = [(2 * c, 2 * c + 1) for c in range(count // 2)]
    partner += [(2 * c + 1, 2 * c) for c in range(count // 2)]
    got = lax.ppermute(give, axis, partner)
    both = jnp.dot(got[:, :rank], own, precision=HIGHEST) + jnp.concatenate(
        [zeros, got[:, rank:]], axis=1
    )
    pair = [(4 * g, 4 * g + 2) for g in range(groups)]
    pair += [(4 * g + 3, 4 * g + 1) for g in range(groups)]
    beside_state = lax.ppermute(both[:, rank:], axis, pair)
    beside_map = lax.ppermute(both[:, :rank], axis, pair)
    group_state = jnp.dot(both[:, :rank], beside_state, precision=HIGHEST) + both[:, rank:]
    group_map = jnp.dot(both[:, :rank], beside_map, precision=HIGHEST)
    beside = jnp.concatenate([beside_map, beside_state], axis=1)
    both = jnp.concatenate([group_map, group_state], axis=1)
    if groups <= 4:
        out = group_state
        for step in range(groups - 1):
            start = group_shift(out, axis, groups, 1)
            if step + 2 < groups:
                out = jnp.dot(group_map, start, precision=HIGHEST) + group_state
    else:
        rounds = 0
        while 2 ** (rounds + 1) < groups - 1:
            rounds += 1
        shift = 1
        for _ in range(rounds):
            got = group_shift(both, axis, groups, shift)
            tail = jnp.concatenate([zeros, both[:, rank:]], axis=1)
            both = jnp.dot(both[:, :rank], got, precision=HIGHEST) + tail
            shift *= 2
        near = group_shift(both, axis, groups, 1)
        far = group_shift(both[:, rank:], axis, groups, 1 + shift)
        start = jnp.dot(near[:, :rank], far, precision=HIGHEST) + near[:, rank:]
    back = [(4 * g + 2, 4 * g) for g in range(groups)]
    back += [(4 * g + 1, 4 * g + 3) for g in range(groups)]
    sent = lax.ppermute(start, axis, back)
    mine = jnp.dot(beside_map, start, precision=HIGHEST) + beside_state
    mine, sent = lax.optimization_barrier((mine, sent))
    holder = jnp.logical_or(place == 1, place == 2)
    enter = jnp.where(holder, mine, sent)
    send = jnp.dot(own[:, :rank], enter, precision=HIGHEST) + own[:, rank:]
    other = lax.ppermute(send, axis, partner)
    return enter, other


def shards(
    right_sides,
    diagonal_blocks,
    lower_rows,
    lower_cols,
    lower_trans,
    upper_rows,
    upper_cols,
    upper_trans,
):
    count, rows, rhs = right_sides.shape
    rank = lower_trans.shape[1]
    count_row = lax.axis_size("row")
    grouped = count_row % 4 == 0 and count_row >= 8
    if grouped:
        flag = jnp.full((1,), lax.axis_index("row") % 2, jnp.int32)
    else:
        flag = jnp.zeros((1,), jnp.int32)
    lboth, lsrc, uboth, usrc = pl.pallas_call(
        sweep_kernel,
        out_shape=(
            jax.ShapeDtypeStruct((rank, rank + rhs), F32),
            jax.ShapeDtypeStruct((count, rank, rhs), F32),
            jax.ShapeDtypeStruct((rank, rank + rhs), F32),
            jax.ShapeDtypeStruct((count, rank, rhs), F32),
        ),
        in_specs=[pl.BlockSpec(memory_space=pltpu.SMEM)] + [pl.BlockSpec(memory_space=pltpu.VMEM)] * 5,
        name="sweep",
    )(flag, right_sides, lower_cols, lower_trans, upper_cols, upper_trans)
    diag = jnp.einsum(
        "kab,kbc->kac", diagonal_blocks, right_sides, preferred_element_type=F32
    )
    count_row = lax.axis_size("row")
    if grouped:
        enter, other = scan_groups(lboth, uboth, "row")
    elif count_row % 2 == 0 and count_row >= 4:
        enter, other = scan_chips(lboth, uboth, "row")
        flag = jnp.full((1,), lax.axis_index("row") % 2, jnp.int32)
    else:
        enter = scan_enter(lboth[:, :rank], lboth[:, rank:], "row", False)
        other = scan_enter(uboth[:, :rank], uboth[:, rank:], "row", True)
        flag = jnp.zeros((1,), jnp.int32)
    vmem = pl.BlockSpec(memory_space=pltpu.VMEM)
    return pl.pallas_call(
        apply_kernel,
        out_shape=jax.ShapeDtypeStruct((count, rows, rhs), BF16),
        scratch_shapes=[
            pltpu.VMEM((count, rank, rhs), BF16),
            pltpu.VMEM((count, rank, rhs), BF16),
        ],
        in_specs=[pl.BlockSpec(memory_space=pltpu.SMEM)] + [vmem] * 9,
        compiler_params=pltpu.CompilerParams(vmem_limit_bytes=LIMIT),
        name="apply",
    )(flag, enter, other, lower_trans, upper_trans, lsrc, usrc, diag, lower_rows, upper_rows)


def solution(mesh):
    spec = P(("sep", "row"), None, None)
    return jax.shard_map(
        shards, mesh=mesh, in_specs=(spec,) * 8, out_specs=spec, check_vma=False
    )
```

```python
import jax
import jax.numpy as jnp
from jax import lax
from jax.experimental import pallas as pl
from jax.experimental.pallas import tpu as pltpu
from jax.sharding import PartitionSpec as P

F32 = jnp.float32
BF16 = jnp.bfloat16
HIGHEST = lax.Precision.HIGHEST
LIMIT = 20 * 1024 * 1024


def split_dot(matrix, value):
    high = value.astype(BF16)
    low = (value - high.astype(F32)).astype(BF16)
    return jnp.dot(matrix, high, preferred_element_type=F32) + jnp.dot(
        matrix, low, preferred_element_type=F32
    )


def wide_kernel(left_ref, right_ref, add_ref, out_ref):
    left = left_ref[...]
    right = right_ref[...]
    left_high = left.astype(BF16)
    left_low = (left - left_high.astype(F32)).astype(BF16)
    right_high = right.astype(BF16)
    right_low = (right - right_high.astype(F32)).astype(BF16)
    total = jnp.dot(left_high, right_high, preferred_element_type=F32)
    total = total + jnp.dot(left_high, right_low, preferred_element_type=F32)
    total = total + jnp.dot(left_low, right_high, preferred_element_type=F32)
    out_ref[...] = total + add_ref[...]


def wide(left, right, add):
    return pl.pallas_call(
        wide_kernel,
        out_shape=jax.ShapeDtypeStruct((left.shape[0], right.shape[1]), F32),
        name="wide",
    )(left, right, add)


def sweep_kernel(
    flag_ref, rhs_ref, lcols_ref, ltrans_ref, ucols_ref, utrans_ref,
    lmap_ref, lsrc_ref, umap_ref, usrc_ref,
):
    count = rhs_ref.shape[0]
    lmap = lstate = umap = ustate = None
    for step in range(count):
        lk = step
        uk = count - 1 - step
        lsrc = lax.dot_general(lcols_ref[lk], rhs_ref[lk], (((0,), (0,)), ((), ())), preferred_element_type=F32)
        usrc = lax.dot_general(ucols_ref[uk], rhs_ref[uk], (((0,), (0,)), ((), ())), preferred_element_type=F32)
        lsrc_ref[lk] = lsrc
        usrc_ref[uk] = usrc
        ltrans = ltrans_ref[lk]
        utrans = utrans_ref[uk]
        if step == 0:
            lstate = lsrc
            ustate = usrc
            lmap = ltrans.astype(F32)
            umap = utrans.astype(F32)
        else:
            lstate = split_dot(ltrans, lstate) + lsrc
            ustate = split_dot(utrans, ustate) + usrc
            lmap = split_dot(ltrans, lmap)
            umap = split_dot(utrans, umap)
    rank = lmap.shape[0]
    first = flag_ref[0] == 0

    @pl.when(first)
    def _():
        lmap_ref[:, :rank] = lmap
        lmap_ref[:, rank:] = lstate
        umap_ref[:, :rank] = umap
        umap_ref[:, rank:] = ustate

    @pl.when(jnp.logical_not(first))
    def _():
        lmap_ref[:, :rank] = umap
        lmap_ref[:, rank:] = ustate
        umap_ref[:, :rank] = lmap
        umap_ref[:, rank:] = lstate


def apply_kernel(
    flag_ref, enter_ref, other_ref, ltrans_ref, utrans_ref, lsrc_ref, usrc_ref,
    diag_ref, lrows_ref, urows_ref, out_ref, lround_ref, uround_ref,
):
    count = ltrans_ref.shape[0]
    first = flag_ref[0] == 0
    lstate = jnp.where(first, enter_ref[...], other_ref[...])
    ustate = jnp.where(first, other_ref[...], enter_ref[...])
    for step in range(count):
        lk = step
        uk = count - 1 - step
        lround_ref[lk] = lstate.astype(BF16)
        uround_ref[uk] = ustate.astype(BF16)
        if step + 1 < count:
            lstate = split_dot(ltrans_ref[lk], lstate) + lsrc_ref[lk]
            ustate = split_dot(utrans_ref[uk], ustate) + usrc_ref[uk]
    for k in range(count):
        total = diag_ref[k]
        total = total + jnp.dot(lrows_ref[k], lround_ref[k], preferred_element_type=F32)
        total = total + jnp.dot(urows_ref[k], uround_ref[k], preferred_element_type=F32)
        out_ref[k] = total.astype(out_ref.dtype)


def shifted(value, axis, count, shift, reverse):
    if reverse:
        pairs = [(i + shift, i) for i in range(count - shift)]
    else:
        pairs = [(i, i + shift) for i in range(count - shift)]
    return lax.ppermute(value, axis, pairs)


def scan_enter(summary_map, summary_state, axis, reverse):
    count = lax.axis_size(axis)
    rank = summary_map.shape[0]
    both = jnp.concatenate([summary_map, summary_state], axis=1)
    rounds = 0
    while 2 ** (rounds + 1) < count - 1:
        rounds += 1
    shift = 1
    for _ in range(rounds):
        got = shifted(both, axis, count, shift, reverse)
        joined = jnp.dot(both[:, :rank], got, precision=HIGHEST)
        both = joined + jnp.concatenate(
            [jnp.zeros_like(summary_map), both[:, rank:]], axis=1
        )
        shift *= 2
    near = shifted(both, axis, count, 1, reverse)
    far = shifted(both[:, rank:], axis, count, 1 + shift, reverse)
    return jnp.dot(near[:, :rank], far, precision=HIGHEST) + near[:, rank:]


def chip_shift(value, axis, chips, shift):
    pairs = [(2 * c, 2 * (c + shift)) for c in range(chips - shift)]
    pairs += [(2 * c + 1, 2 * (c - shift) + 1) for c in range(shift, chips)]
    return lax.ppermute(value, axis, pairs)


def scan_chips(lower, upper, axis):
    count = lax.axis_size(axis)
    chips = count // 2
    rank = lower.shape[0]
    first = lax.axis_index(axis) % 2 == 0
    own = jnp.where(first, lower, upper)
    partner = [(2 * c, 2 * c + 1) for c in range(chips)]
    partner += [(2 * c + 1, 2 * c) for c in range(chips)]
    got = lax.ppermute(jnp.where(first, upper, lower), axis, partner)
    tail = jnp.concatenate([jnp.zeros((rank, rank), F32), got[:, rank:]], axis=1)
    both = jnp.dot(got[:, :rank], own, precision=HIGHEST) + tail
    rounds = 0
    while 2 ** (rounds + 1) < chips - 1:
        rounds += 1
    shift = 1
    for _ in range(rounds):
        got = chip_shift(both, axis, chips, shift)
        tail = jnp.concatenate([jnp.zeros((rank, rank), F32), both[:, rank:]], axis=1)
        both = jnp.dot(both[:, :rank], got, precision=HIGHEST) + tail
        shift *= 2
    near = chip_shift(both, axis, chips, 1)
    far = chip_shift(both[:, rank:], axis, chips, 1 + shift)
    enter = jnp.dot(near[:, :rank], far, precision=HIGHEST) + near[:, rank:]
    send = jnp.dot(own[:, :rank], enter, precision=HIGHEST) + own[:, rank:]
    other = lax.ppermute(send, axis, partner)
    return enter, other


def group_shift(value, axis, groups, shift):
    pairs = [(4 * g + 2, 4 * (g + shift) + 2) for g in range(groups - shift)]
    pairs += [(4 * g + 1, 4 * (g - shift) + 1) for g in range(shift, groups)]
    return lax.ppermute(value, axis, pairs)


def scan_groups(own, give, axis):
    count = lax.axis_size(axis)
    groups = count // 4
    rank = own.shape[0]
    place = lax.axis_index(axis) % 4
    zeros = jnp.zeros((rank, rank), F32)
    partner = [(2 * c, 2 * c + 1) for c in range(count // 2)]
    partner += [(2 * c + 1, 2 * c) for c in range(count // 2)]
    got = lax.ppermute(give, axis, partner)
    both = wide(got[:, :rank], own, jnp.concatenate([zeros, got[:, rank:]], axis=1))
    pair = [(4 * g, 4 * g + 2) for g in range(groups)]
    pair += [(4 * g + 3, 4 * g + 1) for g in range(groups)]
    beside_state = lax.ppermute(both[:, rank:], axis, pair)
    beside_map = lax.ppermute(both[:, :rank], axis, pair)
    group_state = wide(both[:, :rank], beside_state, both[:, rank:])
    group_map = wide(both[:, :rank], beside_map, zeros)
    beside = jnp.concatenate([beside_map, beside_state], axis=1)
    both = jnp.concatenate([group_map, group_state], axis=1)
    if groups <= 4:
        out = group_state
        for step in range(groups - 1):
            start = group_shift(out, axis, groups, 1)
            if step + 2 < groups:
                out = wide(group_map, start, group_state)
    else:
        rounds = 0
        while 2 ** (rounds + 1) < groups - 1:
            rounds += 1
        shift = 1
        for _ in range(rounds):
            got = group_shift(both, axis, groups, shift)
            tail = jnp.concatenate([zeros, both[:, rank:]], axis=1)
            both = jnp.dot(both[:, :rank], got, precision=HIGHEST) + tail
            shift *= 2
        near = group_shift(both, axis, groups, 1)
        far = group_shift(both[:, rank:], axis, groups, 1 + shift)
        start = jnp.dot(near[:, :rank], far, precision=HIGHEST) + near[:, rank:]
    back = [(4 * g + 2, 4 * g) for g in range(groups)]
    back += [(4 * g + 1, 4 * g + 3) for g in range(groups)]
    sent = lax.ppermute(start, axis, back)
    mine = wide(beside_map, start, beside_state)
    mine, sent = lax.optimization_barrier((mine, sent))
    holder = jnp.logical_or(place == 1, place == 2)
    enter = jnp.where(holder, mine, sent)
    send = wide(own[:, :rank], enter, own[:, rank:])
    other = lax.ppermute(send, axis, partner)
    return enter, other


def shards(
    right_sides,
    diagonal_blocks,
    lower_rows,
    lower_cols,
    lower_trans,
    upper_rows,
    upper_cols,
    upper_trans,
):
    count, rows, rhs = right_sides.shape
    rank = lower_trans.shape[1]
    count_row = lax.axis_size("row")
    grouped = count_row % 4 == 0 and count_row >= 8
    if grouped:
        flag = jnp.full((1,), lax.axis_index("row") % 2, jnp.int32)
    else:
        flag = jnp.zeros((1,), jnp.int32)
    lboth, lsrc, uboth, usrc = pl.pallas_call(
        sweep_kernel,
        out_shape=(
            jax.ShapeDtypeStruct((rank, rank + rhs), F32),
            jax.ShapeDtypeStruct((count, rank, rhs), F32),
            jax.ShapeDtypeStruct((rank, rank + rhs), F32),
            jax.ShapeDtypeStruct((count, rank, rhs), F32),
        ),
        in_specs=[pl.BlockSpec(memory_space=pltpu.SMEM)] + [pl.BlockSpec(memory_space=pltpu.VMEM)] * 5,
        name="sweep",
    )(flag, right_sides, lower_cols, lower_trans, upper_cols, upper_trans)
    diag = jnp.einsum(
        "kab,kbc->kac", diagonal_blocks, right_sides, preferred_element_type=F32
    )
    count_row = lax.axis_size("row")
    if grouped:
        enter, other = scan_groups(lboth, uboth, "row")
    elif count_row % 2 == 0 and count_row >= 4:
        enter, other = scan_chips(lboth, uboth, "row")
        flag = jnp.full((1,), lax.axis_index("row") % 2, jnp.int32)
    else:
        enter = scan_enter(lboth[:, :rank], lboth[:, rank:], "row", False)
        other = scan_enter(uboth[:, :rank], uboth[:, rank:], "row", True)
        flag = jnp.zeros((1,), jnp.int32)
    vmem = pl.BlockSpec(memory_space=pltpu.VMEM)
    return pl.pallas_call(
        apply_kernel,
        out_shape=jax.ShapeDtypeStruct((count, rows, rhs), BF16),
        scratch_shapes=[
            pltpu.VMEM((count, rank, rhs), BF16),
            pltpu.VMEM((count, rank, rhs), BF16),
        ],
        in_specs=[pl.BlockSpec(memory_space=pltpu.SMEM)] + [vmem] * 9,
        compiler_params=pltpu.CompilerParams(vmem_limit_bytes=LIMIT),
        name="apply",
    )(flag, enter, other, lower_trans, upper_trans, lsrc, usrc, diag, lower_rows, upper_rows)


def solution(mesh):
    spec = P(("sep", "row"), None, None)
    return jax.shard_map(
        shards, mesh=mesh, in_specs=(spec,) * 8, out_specs=spec, check_vma=False
    )
```

```python
import jax
import jax.numpy as jnp
from jax import lax
from jax.experimental import pallas as pl
from jax.experimental.pallas import tpu as pltpu
from jax.sharding import PartitionSpec as P

F32 = jnp.float32
BF16 = jnp.bfloat16
HIGHEST = lax.Precision.HIGHEST
LIMIT = 20 * 1024 * 1024


def split_dot(matrix, value):
    high = value.astype(BF16)
    low = (value - high.astype(F32)).astype(BF16)
    return jnp.dot(matrix, high, preferred_element_type=F32) + jnp.dot(
        matrix, low, preferred_element_type=F32
    )


def source_kernel(rhs_ref, lcols_ref, ucols_ref, lsrc_ref, usrc_ref):
    for k in range(rhs_ref.shape[0]):
        lsrc_ref[k] = lax.dot_general(lcols_ref[k], rhs_ref[k], (((0,), (0,)), ((), ())), preferred_element_type=F32)
        usrc_ref[k] = lax.dot_general(ucols_ref[k], rhs_ref[k], (((0,), (0,)), ((), ())), preferred_element_type=F32)


def sweep_kernel(
    flag_ref, rhs_ref, lcols_ref, ltrans_ref, ucols_ref, utrans_ref,
    lmap_ref, umap_ref,
):
    count = rhs_ref.shape[0]
    lmap = lstate = umap = ustate = None
    for step in range(count):
        lk = step
        uk = count - 1 - step
        lsrc = lax.dot_general(lcols_ref[lk], rhs_ref[lk], (((0,), (0,)), ((), ())), preferred_element_type=F32)
        usrc = lax.dot_general(ucols_ref[uk], rhs_ref[uk], (((0,), (0,)), ((), ())), preferred_element_type=F32)
        ltrans = ltrans_ref[lk]
        utrans = utrans_ref[uk]
        if step == 0:
            lstate = lsrc
            ustate = usrc
            lmap = ltrans.astype(F32)
            umap = utrans.astype(F32)
        else:
            lstate = split_dot(ltrans, lstate) + lsrc
            ustate = split_dot(utrans, ustate) + usrc
            lmap = split_dot(ltrans, lmap)
            umap = split_dot(utrans, umap)
    rank = lmap.shape[0]
    first = flag_ref[0] == 0

    @pl.when(first)
    def _():
        lmap_ref[:, :rank] = lmap
        lmap_ref[:, rank:] = lstate
        umap_ref[:, :rank] = umap
        umap_ref[:, rank:] = ustate

    @pl.when(jnp.logical_not(first))
    def _():
        lmap_ref[:, :rank] = umap
        lmap_ref[:, rank:] = ustate
        umap_ref[:, :rank] = lmap
        umap_ref[:, rank:] = lstate


def apply_kernel(
    flag_ref, enter_ref, other_ref, ltrans_ref, utrans_ref, lsrc_ref, usrc_ref,
    diag_ref, lrows_ref, urows_ref, out_ref, lround_ref, uround_ref,
):
    count = ltrans_ref.shape[0]
    first = flag_ref[0] == 0
    lstate = jnp.where(first, enter_ref[...], other_ref[...])
    ustate = jnp.where(first, other_ref[...], enter_ref[...])
    for step in range(count):
        lk = step
        uk = count - 1 - step
        lround_ref[lk] = lstate.astype(BF16)
        uround_ref[uk] = ustate.astype(BF16)
        if step + 1 < count:
            lstate = split_dot(ltrans_ref[lk], lstate) + lsrc_ref[lk]
            ustate = split_dot(utrans_ref[uk], ustate) + usrc_ref[uk]
    for k in range(count):
        total = diag_ref[k]
        total = total + jnp.dot(lrows_ref[k], lround_ref[k], preferred_element_type=F32)
        total = total + jnp.dot(urows_ref[k], uround_ref[k], preferred_element_type=F32)
        out_ref[k] = total.astype(out_ref.dtype)


def shifted(value, axis, count, shift, reverse):
    if reverse:
        pairs = [(i + shift, i) for i in range(count - shift)]
    else:
        pairs = [(i, i + shift) for i in range(count - shift)]
    return lax.ppermute(value, axis, pairs)


def scan_enter(summary_map, summary_state, axis, reverse):
    count = lax.axis_size(axis)
    rank = summary_map.shape[0]
    both = jnp.concatenate([summary_map, summary_state], axis=1)
    rounds = 0
    while 2 ** (rounds + 1) < count - 1:
        rounds += 1
    shift = 1
    for _ in range(rounds):
        got = shifted(both, axis, count, shift, reverse)
        joined = jnp.dot(both[:, :rank], got, precision=HIGHEST)
        both = joined + jnp.concatenate(
            [jnp.zeros_like(summary_map), both[:, rank:]], axis=1
        )
        shift *= 2
    near = shifted(both, axis, count, 1, reverse)
    far = shifted(both[:, rank:], axis, count, 1 + shift, reverse)
    return jnp.dot(near[:, :rank], far, precision=HIGHEST) + near[:, rank:]


def chip_shift(value, axis, chips, shift):
    pairs = [(2 * c, 2 * (c + shift)) for c in range(chips - shift)]
    pairs += [(2 * c + 1, 2 * (c - shift) + 1) for c in range(shift, chips)]
    return lax.ppermute(value, axis, pairs)


def scan_chips(lower, upper, axis):
    count = lax.axis_size(axis)
    chips = count // 2
    rank = lower.shape[0]
    first = lax.axis_index(axis) % 2 == 0
    own = jnp.where(first, lower, upper)
    partner = [(2 * c, 2 * c + 1) for c in range(chips)]
    partner += [(2 * c + 1, 2 * c) for c in range(chips)]
    got = lax.ppermute(jnp.where(first, upper, lower), axis, partner)
    tail = jnp.concatenate([jnp.zeros((rank, rank), F32), got[:, rank:]], axis=1)
    both = jnp.dot(got[:, :rank], own, precision=HIGHEST) + tail
    rounds = 0
    while 2 ** (rounds + 1) < chips - 1:
        rounds += 1
    shift = 1
    for _ in range(rounds):
        got = chip_shift(both, axis, chips, shift)
        tail = jnp.concatenate([jnp.zeros((rank, rank), F32), both[:, rank:]], axis=1)
        both = jnp.dot(both[:, :rank], got, precision=HIGHEST) + tail
        shift *= 2
    near = chip_shift(both, axis, chips, 1)
    far = chip_shift(both[:, rank:], axis, chips, 1 + shift)
    enter = jnp.dot(near[:, :rank], far, precision=HIGHEST) + near[:, rank:]
    send = jnp.dot(own[:, :rank], enter, precision=HIGHEST) + own[:, rank:]
    other = lax.ppermute(send, axis, partner)
    return enter, other


def group_shift(value, axis, groups, shift):
    pairs = [(4 * g + 2, 4 * (g + shift) + 2) for g in range(groups - shift)]
    pairs += [(4 * g + 1, 4 * (g - shift) + 1) for g in range(shift, groups)]
    return lax.ppermute(value, axis, pairs)


def scan_groups(own, give, axis):
    count = lax.axis_size(axis)
    groups = count // 4
    rank = own.shape[0]
    place = lax.axis_index(axis) % 4
    zeros = jnp.zeros((rank, rank), F32)
    partner = [(2 * c, 2 * c + 1) for c in range(count // 2)]
    partner += [(2 * c + 1, 2 * c) for c in range(count // 2)]
    got = lax.ppermute(give, axis, partner)
    both = jnp.dot(got[:, :rank], own, precision=HIGHEST) + jnp.concatenate(
        [zeros, got[:, rank:]], axis=1
    )
    pair = [(4 * g, 4 * g + 2) for g in range(groups)]
    pair += [(4 * g + 3, 4 * g + 1) for g in range(groups)]
    beside_state = lax.ppermute(both[:, rank:], axis, pair)
    beside_map = lax.ppermute(both[:, :rank], axis, pair)
    group_state = jnp.dot(both[:, :rank], beside_state, precision=HIGHEST) + both[:, rank:]
    group_map = jnp.dot(both[:, :rank], beside_map, precision=HIGHEST)
    beside = jnp.concatenate([beside_map, beside_state], axis=1)
    both = jnp.concatenate([group_map, group_state], axis=1)
    if groups <= 4:
        out = group_state
        for step in range(groups - 1):
            start = group_shift(out, axis, groups, 1)
            if step + 2 < groups:
                out = jnp.dot(group_map, start, precision=HIGHEST) + group_state
    else:
        rounds = 0
        while 2 ** (rounds + 1) < groups - 1:
            rounds += 1
        shift = 1
        for _ in range(rounds):
            got = group_shift(both, axis, groups, shift)
            tail = jnp.concatenate([zeros, both[:, rank:]], axis=1)
            both = jnp.dot(both[:, :rank], got, precision=HIGHEST) + tail
            shift *= 2
        near = group_shift(both, axis, groups, 1)
        far = group_shift(both[:, rank:], axis, groups, 1 + shift)
        start = jnp.dot(near[:, :rank], far, precision=HIGHEST) + near[:, rank:]
    back = [(4 * g + 2, 4 * g) for g in range(groups)]
    back += [(4 * g + 1, 4 * g + 3) for g in range(groups)]
    sent = lax.ppermute(start, axis, back)
    mine = jnp.dot(beside_map, start, precision=HIGHEST) + beside_state
    mine, sent = lax.optimization_barrier((mine, sent))
    holder = jnp.logical_or(place == 1, place == 2)
    enter = jnp.where(holder, mine, sent)
    send = jnp.dot(own[:, :rank], enter, precision=HIGHEST) + own[:, rank:]
    other = lax.ppermute(send, axis, partner)
    return enter, other


def shards_body(
    right_sides,
    diagonal_blocks,
    lower_rows,
    lower_cols,
    lower_trans,
    upper_rows,
    upper_cols,
    upper_trans,
):
    count, rows, rhs = right_sides.shape
    rank = lower_trans.shape[1]
    count_row = lax.axis_size("row")
    grouped = count_row % 4 == 0 and count_row >= 8
    if grouped:
        flag = jnp.full((1,), lax.axis_index("row") % 2, jnp.int32)
    else:
        flag = jnp.zeros((1,), jnp.int32)
    lboth, uboth = pl.pallas_call(
        sweep_kernel,
        out_shape=(
            jax.ShapeDtypeStruct((rank, rank + rhs), F32),
            jax.ShapeDtypeStruct((rank, rank + rhs), F32),
        ),
        in_specs=[pl.BlockSpec(memory_space=pltpu.SMEM)] + [pl.BlockSpec(memory_space=pltpu.VMEM)] * 5,
        name="sweep",
    )(flag, right_sides, lower_cols, lower_trans, upper_cols, upper_trans)
    lsrc, usrc = pl.pallas_call(
        source_kernel,
        out_shape=(
            jax.ShapeDtypeStruct((count, rank, rhs), F32),
            jax.ShapeDtypeStruct((count, rank, rhs), F32),
        ),
        name="source",
    )(right_sides, lower_cols, upper_cols)
    diag = jnp.einsum(
        "kab,kbc->kac", diagonal_blocks, right_sides, preferred_element_type=F32
    )
    count_row = lax.axis_size("row")
    if grouped:
        enter, other = scan_groups(lboth, uboth, "row")
    elif count_row % 2 == 0 and count_row >= 4:
        enter, other = scan_chips(lboth, uboth, "row")
        flag = jnp.full((1,), lax.axis_index("row") % 2, jnp.int32)
    else:
        enter = scan_enter(lboth[:, :rank], lboth[:, rank:], "row", False)
        other = scan_enter(uboth[:, :rank], uboth[:, rank:], "row", True)
        flag = jnp.zeros((1,), jnp.int32)
    vmem = pl.BlockSpec(memory_space=pltpu.VMEM)
    return pl.pallas_call(
        apply_kernel,
        out_shape=jax.ShapeDtypeStruct((count, rows, rhs), BF16),
        scratch_shapes=[
            pltpu.VMEM((count, rank, rhs), BF16),
            pltpu.VMEM((count, rank, rhs), BF16),
        ],
        in_specs=[pl.BlockSpec(memory_space=pltpu.SMEM)] + [vmem] * 9,
        compiler_params=pltpu.CompilerParams(vmem_limit_bytes=LIMIT),
        name="apply",
    )(flag, enter, other, lower_trans, upper_trans, lsrc, usrc, diag, lower_rows, upper_rows)


def solution(mesh):
    spec = P(("sep", "row"), None, None)
    return jax.shard_map(
        shards_body, mesh=mesh, in_specs=(spec,) * 8, out_specs=spec, check_vma=False
    )
```

```python
import jax
import jax.numpy as jnp
from jax import lax
from jax.experimental import pallas as pl
from jax.experimental.pallas import tpu as pltpu
from jax.sharding import PartitionSpec as P

F32 = jnp.float32
BF16 = jnp.bfloat16
HIGHEST = lax.Precision.HIGHEST
LIMIT = 20 * 1024 * 1024


def split_dot(matrix, value):
    high = value.astype(BF16)
    low = (value - high.astype(F32)).astype(BF16)
    return jnp.dot(matrix, high, preferred_element_type=F32) + jnp.dot(
        matrix, low, preferred_element_type=F32
    )


def sweep_kernel(
    flag_ref, rhs_ref, lcols_ref, ltrans_ref, ucols_ref, utrans_ref,
    lmap_ref, umap_ref,
):
    count = rhs_ref.shape[0]
    lmap = lstate = umap = ustate = None
    for step in range(count):
        lk = step
        uk = count - 1 - step
        lsrc = lax.dot_general(lcols_ref[lk], rhs_ref[lk], (((0,), (0,)), ((), ())), preferred_element_type=F32)
        usrc = lax.dot_general(ucols_ref[uk], rhs_ref[uk], (((0,), (0,)), ((), ())), preferred_element_type=F32)
        ltrans = ltrans_ref[lk]
        utrans = utrans_ref[uk]
        if step == 0:
            lstate = lsrc
            ustate = usrc
            lmap = ltrans.astype(F32)
            umap = utrans.astype(F32)
        else:
            lstate = split_dot(ltrans, lstate) + lsrc
            ustate = split_dot(utrans, ustate) + usrc
            lmap = split_dot(ltrans, lmap)
            umap = split_dot(utrans, umap)
    rank = lmap.shape[0]
    first = flag_ref[0] == 0

    @pl.when(first)
    def _():
        lmap_ref[:, :rank] = lmap
        lmap_ref[:, rank:] = lstate
        umap_ref[:, :rank] = umap
        umap_ref[:, rank:] = ustate

    @pl.when(jnp.logical_not(first))
    def _():
        lmap_ref[:, :rank] = umap
        lmap_ref[:, rank:] = ustate
        umap_ref[:, :rank] = lmap
        umap_ref[:, rank:] = lstate


def apply_kernel(
    flag_ref, enter_ref, other_ref, ltrans_ref, utrans_ref, lcols_ref, ucols_ref, rhs_ref,
    diag_ref, lrows_ref, urows_ref, out_ref, lround_ref, uround_ref,
):
    count = ltrans_ref.shape[0]
    first = flag_ref[0] == 0
    lstate = jnp.where(first, enter_ref[...], other_ref[...])
    ustate = jnp.where(first, other_ref[...], enter_ref[...])
    for step in range(count):
        lk = step
        uk = count - 1 - step
        lround_ref[lk] = lstate.astype(BF16)
        uround_ref[uk] = ustate.astype(BF16)
        if step + 1 < count:
            lsrc = lax.dot_general(lcols_ref[lk], rhs_ref[lk], (((0,), (0,)), ((), ())), preferred_element_type=F32)
            usrc = lax.dot_general(ucols_ref[uk], rhs_ref[uk], (((0,), (0,)), ((), ())), preferred_element_type=F32)
            lstate = split_dot(ltrans_ref[lk], lstate) + lsrc
            ustate = split_dot(utrans_ref[uk], ustate) + usrc
    for k in range(count):
        total = diag_ref[k]
        total = total + jnp.dot(lrows_ref[k], lround_ref[k], preferred_element_type=F32)
        total = total + jnp.dot(urows_ref[k], uround_ref[k], preferred_element_type=F32)
        out_ref[k] = total.astype(out_ref.dtype)


def shifted(value, axis, count, shift, reverse):
    if reverse:
        pairs = [(i + shift, i) for i in range(count - shift)]
    else:
        pairs = [(i, i + shift) for i in range(count - shift)]
    return lax.ppermute(value, axis, pairs)


def scan_enter(summary_map, summary_state, axis, reverse):
    count = lax.axis_size(axis)
    rank = summary_map.shape[0]
    both = jnp.concatenate([summary_map, summary_state], axis=1)
    rounds = 0
    while 2 ** (rounds + 1) < count - 1:
        rounds += 1
    shift = 1
    for _ in range(rounds):
        got = shifted(both, axis, count, shift, reverse)
        joined = jnp.dot(both[:, :rank], got, precision=HIGHEST)
        both = joined + jnp.concatenate(
            [jnp.zeros_like(summary_map), both[:, rank:]], axis=1
        )
        shift *= 2
    near = shifted(both, axis, count, 1, reverse)
    far = shifted(both[:, rank:], axis, count, 1 + shift, reverse)
    return jnp.dot(near[:, :rank], far, precision=HIGHEST) + near[:, rank:]


def chip_shift(value, axis, chips, shift):
    pairs = [(2 * c, 2 * (c + shift)) for c in range(chips - shift)]
    pairs += [(2 * c + 1, 2 * (c - shift) + 1) for c in range(shift, chips)]
    return lax.ppermute(value, axis, pairs)


def scan_chips(lower, upper, axis):
    count = lax.axis_size(axis)
    chips = count // 2
    rank = lower.shape[0]
    first = lax.axis_index(axis) % 2 == 0
    own = jnp.where(first, lower, upper)
    partner = [(2 * c, 2 * c + 1) for c in range(chips)]
    partner += [(2 * c + 1, 2 * c) for c in range(chips)]
    got = lax.ppermute(jnp.where(first, upper, lower), axis, partner)
    tail = jnp.concatenate([jnp.zeros((rank, rank), F32), got[:, rank:]], axis=1)
    both = jnp.dot(got[:, :rank], own, precision=HIGHEST) + tail
    rounds = 0
    while 2 ** (rounds + 1) < chips - 1:
        rounds += 1
    shift = 1
    for _ in range(rounds):
        got = chip_shift(both, axis, chips, shift)
        tail = jnp.concatenate([jnp.zeros((rank, rank), F32), both[:, rank:]], axis=1)
        both = jnp.dot(both[:, :rank], got, precision=HIGHEST) + tail
        shift *= 2
    near = chip_shift(both, axis, chips, 1)
    far = chip_shift(both[:, rank:], axis, chips, 1 + shift)
    enter = jnp.dot(near[:, :rank], far, precision=HIGHEST) + near[:, rank:]
    send = jnp.dot(own[:, :rank], enter, precision=HIGHEST) + own[:, rank:]
    other = lax.ppermute(send, axis, partner)
    return enter, other


def group_shift(value, axis, groups, shift):
    pairs = [(4 * g + 2, 4 * (g + shift) + 2) for g in range(groups - shift)]
    pairs += [(4 * g + 1, 4 * (g - shift) + 1) for g in range(shift, groups)]
    return lax.ppermute(value, axis, pairs)


def scan_groups(own, give, axis):
    count = lax.axis_size(axis)
    groups = count // 4
    rank = own.shape[0]
    place = lax.axis_index(axis) % 4
    zeros = jnp.zeros((rank, rank), F32)
    partner = [(2 * c, 2 * c + 1) for c in range(count // 2)]
    partner += [(2 * c + 1, 2 * c) for c in range(count // 2)]
    got = lax.ppermute(give, axis, partner)
    both = jnp.dot(got[:, :rank], own, precision=HIGHEST) + jnp.concatenate(
        [zeros, got[:, rank:]], axis=1
    )
    pair = [(4 * g, 4 * g + 2) for g in range(groups)]
    pair += [(4 * g + 3, 4 * g + 1) for g in range(groups)]
    beside_state = lax.ppermute(both[:, rank:], axis, pair)
    beside_map = lax.ppermute(both[:, :rank], axis, pair)
    group_state = jnp.dot(both[:, :rank], beside_state, precision=HIGHEST) + both[:, rank:]
    group_map = jnp.dot(both[:, :rank], beside_map, precision=HIGHEST)
    beside = jnp.concatenate([beside_map, beside_state], axis=1)
    both = jnp.concatenate([group_map, group_state], axis=1)
    if groups <= 4:
        out = group_state
        for step in range(groups - 1):
            start = group_shift(out, axis, groups, 1)
            if step + 2 < groups:
                out = jnp.dot(group_map, start, precision=HIGHEST) + group_state
    else:
        rounds = 0
        while 2 ** (rounds + 1) < groups - 1:
            rounds += 1
        shift = 1
        for _ in range(rounds):
            got = group_shift(both, axis, groups, shift)
            tail = jnp.concatenate([zeros, both[:, rank:]], axis=1)
            both = jnp.dot(both[:, :rank], got, precision=HIGHEST) + tail
            shift *= 2
        near = group_shift(both, axis, groups, 1)
        far = group_shift(both[:, rank:], axis, groups, 1 + shift)
        start = jnp.dot(near[:, :rank], far, precision=HIGHEST) + near[:, rank:]
    back = [(4 * g + 2, 4 * g) for g in range(groups)]
    back += [(4 * g + 1, 4 * g + 3) for g in range(groups)]
    sent = lax.ppermute(start, axis, back)
    mine = jnp.dot(beside_map, start, precision=HIGHEST) + beside_state
    mine, sent = lax.optimization_barrier((mine, sent))
    holder = jnp.logical_or(place == 1, place == 2)
    enter = jnp.where(holder, mine, sent)
    send = jnp.dot(own[:, :rank], enter, precision=HIGHEST) + own[:, rank:]
    other = lax.ppermute(send, axis, partner)
    return enter, other


def shards(
    right_sides,
    diagonal_blocks,
    lower_rows,
    lower_cols,
    lower_trans,
    upper_rows,
    upper_cols,
    upper_trans,
):
    count, rows, rhs = right_sides.shape
    rank = lower_trans.shape[1]
    count_row = lax.axis_size("row")
    grouped = count_row % 4 == 0 and count_row >= 8
    if grouped:
        flag = jnp.full((1,), lax.axis_index("row") % 2, jnp.int32)
    else:
        flag = jnp.zeros((1,), jnp.int32)
    lboth, uboth = pl.pallas_call(
        sweep_kernel,
        out_shape=(
            jax.ShapeDtypeStruct((rank, rank + rhs), F32),
            jax.ShapeDtypeStruct((rank, rank + rhs), F32),
        ),
        in_specs=[pl.BlockSpec(memory_space=pltpu.SMEM)] + [pl.BlockSpec(memory_space=pltpu.VMEM)] * 5,
        name="sweep",
    )(flag, right_sides, lower_cols, lower_trans, upper_cols, upper_trans)
    diag = jnp.einsum(
        "kab,kbc->kac", diagonal_blocks, right_sides, preferred_element_type=F32
    )
    count_row = lax.axis_size("row")
    if grouped:
        enter, other = scan_groups(lboth, uboth, "row")
    elif count_row % 2 == 0 and count_row >= 4:
        enter, other = scan_chips(lboth, uboth, "row")
        flag = jnp.full((1,), lax.axis_index("row") % 2, jnp.int32)
    else:
        enter = scan_enter(lboth[:, :rank], lboth[:, rank:], "row", False)
        other = scan_enter(uboth[:, :rank], uboth[:, rank:], "row", True)
        flag = jnp.zeros((1,), jnp.int32)
    vmem = pl.BlockSpec(memory_space=pltpu.VMEM)
    return pl.pallas_call(
        apply_kernel,
        out_shape=jax.ShapeDtypeStruct((count, rows, rhs), BF16),
        scratch_shapes=[
            pltpu.VMEM((count, rank, rhs), BF16),
            pltpu.VMEM((count, rank, rhs), BF16),
        ],
        in_specs=[pl.BlockSpec(memory_space=pltpu.SMEM)] + [vmem] * 10,
        compiler_params=pltpu.CompilerParams(vmem_limit_bytes=LIMIT),
        name="apply",
    )(flag, enter, other, lower_trans, upper_trans, lower_cols, upper_cols, right_sides, diag, lower_rows, upper_rows)


def solution(mesh):
    spec = P(("sep", "row"), None, None)
    return jax.shard_map(
        shards, mesh=mesh, in_specs=(spec,) * 8, out_specs=spec, check_vma=False
    )
```

```python
import jax
import jax.numpy as jnp
from jax import lax
from jax.experimental import pallas as pl
from jax.experimental.pallas import tpu as pltpu
from jax.sharding import PartitionSpec as P

F32 = jnp.float32
BF16 = jnp.bfloat16
HIGHEST = lax.Precision.HIGHEST
LIMIT = 20 * 1024 * 1024


def split_dot(matrix, value):
    high = value.astype(BF16)
    low = (value - high.astype(F32)).astype(BF16)
    return jnp.dot(matrix, high, preferred_element_type=F32) + jnp.dot(
        matrix, low, preferred_element_type=F32
    )


def sweep_kernel(
    flag_ref, rhs_ref, lcols_ref, ltrans_ref, ucols_ref, utrans_ref,
    lmap_ref, lsrc_ref, umap_ref, usrc_ref,
):
    count = rhs_ref.shape[0]
    lmap = lstate = umap = ustate = None
    for step in range(count):
        lk = step
        uk = count - 1 - step
        lsrc = lax.dot_general(lcols_ref[lk], rhs_ref[lk], (((0,), (0,)), ((), ())), preferred_element_type=F32)
        usrc = lax.dot_general(ucols_ref[uk], rhs_ref[uk], (((0,), (0,)), ((), ())), preferred_element_type=F32)
        lsrc_ref[lk] = lsrc
        usrc_ref[uk] = usrc
        ltrans = ltrans_ref[lk]
        utrans = utrans_ref[uk]
        if step == 0:
            lstate = lsrc
            ustate = usrc
            lmap = ltrans.astype(F32)
            umap = utrans.astype(F32)
        else:
            lstate = split_dot(ltrans, lstate) + lsrc
            ustate = split_dot(utrans, ustate) + usrc
            lmap = split_dot(ltrans, lmap)
            umap = split_dot(utrans, umap)
    rank = lmap.shape[0]
    first = flag_ref[0] == 0

    @pl.when(first)
    def _():
        lmap_ref[:, :rank] = lmap
        lmap_ref[:, rank:] = lstate
        umap_ref[:, :rank] = umap
        umap_ref[:, rank:] = ustate

    @pl.when(jnp.logical_not(first))
    def _():
        lmap_ref[:, :rank] = umap
        lmap_ref[:, rank:] = ustate
        umap_ref[:, :rank] = lmap
        umap_ref[:, rank:] = lstate


def apply_kernel(
    flag_ref, enter_ref, other_ref, ltrans_ref, utrans_ref, lsrc_ref, usrc_ref,
    diag_ref, lrows_ref, urows_ref, out_ref, lround_ref, uround_ref,
):
    count = ltrans_ref.shape[0]
    first = flag_ref[0] == 0
    lstate = jnp.where(first, enter_ref[...], other_ref[...])
    ustate = jnp.where(first, other_ref[...], enter_ref[...])
    for step in range(count):
        lk = step
        uk = count - 1 - step
        lround_ref[lk] = lstate.astype(BF16)
        uround_ref[uk] = ustate.astype(BF16)
        if step + 1 < count:
            lstate = split_dot(ltrans_ref[lk], lstate) + lsrc_ref[lk]
            ustate = split_dot(utrans_ref[uk], ustate) + usrc_ref[uk]
    for k in range(count):
        total = diag_ref[k]
        total = total + jnp.dot(lrows_ref[k], lround_ref[k], preferred_element_type=F32)
        total = total + jnp.dot(urows_ref[k], uround_ref[k], preferred_element_type=F32)
        out_ref[k] = total.astype(out_ref.dtype)


def shifted(value, axis, count, shift, reverse):
    if reverse:
        pairs = [(i + shift, i) for i in range(count - shift)]
    else:
        pairs = [(i, i + shift) for i in range(count - shift)]
    return lax.ppermute(value, axis, pairs)


def scan_enter(summary_map, summary_state, axis, reverse):
    count = lax.axis_size(axis)
    rank = summary_map.shape[0]
    both = jnp.concatenate([summary_map, summary_state], axis=1)
    rounds = 0
    while 2 ** (rounds + 1) < count - 1:
        rounds += 1
    shift = 1
    for _ in range(rounds):
        got = shifted(both, axis, count, shift, reverse)
        joined = jnp.dot(both[:, :rank], got, precision=HIGHEST)
        both = joined + jnp.concatenate(
            [jnp.zeros_like(summary_map), both[:, rank:]], axis=1
        )
        shift *= 2
    near = shifted(both, axis, count, 1, reverse)
    far = shifted(both[:, rank:], axis, count, 1 + shift, reverse)
    return jnp.dot(near[:, :rank], far, precision=HIGHEST) + near[:, rank:]


def chip_shift(value, axis, chips, shift):
    pairs = [(2 * c, 2 * (c + shift)) for c in range(chips - shift)]
    pairs += [(2 * c + 1, 2 * (c - shift) + 1) for c in range(shift, chips)]
    return lax.ppermute(value, axis, pairs)


def scan_chips(lower, upper, axis):
    count = lax.axis_size(axis)
    chips = count // 2
    rank = lower.shape[0]
    first = lax.axis_index(axis) % 2 == 0
    own = jnp.where(first, lower, upper)
    partner = [(2 * c, 2 * c + 1) for c in range(chips)]
    partner += [(2 * c + 1, 2 * c) for c in range(chips)]
    got = lax.ppermute(jnp.where(first, upper, lower), axis, partner)
    tail = jnp.concatenate([jnp.zeros((rank, rank), F32), got[:, rank:]], axis=1)
    both = jnp.dot(got[:, :rank], own, precision=HIGHEST) + tail
    rounds = 0
    while 2 ** (rounds + 1) < chips - 1:
        rounds += 1
    shift = 1
    for _ in range(rounds):
        got = chip_shift(both, axis, chips, shift)
        tail = jnp.concatenate([jnp.zeros((rank, rank), F32), both[:, rank:]], axis=1)
        both = jnp.dot(both[:, :rank], got, precision=HIGHEST) + tail
        shift *= 2
    near = chip_shift(both, axis, chips, 1)
    far = chip_shift(both[:, rank:], axis, chips, 1 + shift)
    enter = jnp.dot(near[:, :rank], far, precision=HIGHEST) + near[:, rank:]
    send = jnp.dot(own[:, :rank], enter, precision=HIGHEST) + own[:, rank:]
    other = lax.ppermute(send, axis, partner)
    return enter, other


def group_shift(value, axis, groups, shift):
    pairs = [(4 * g + 2, 4 * (g + shift) + 2) for g in range(groups - shift)]
    pairs += [(4 * g + 1, 4 * (g - shift) + 1) for g in range(shift, groups)]
    return lax.ppermute(value, axis, pairs)


def scan_groups(own, give, axis):
    count = lax.axis_size(axis)
    groups = count // 4
    rank = own.shape[0]
    place = lax.axis_index(axis) % 4
    zeros = jnp.zeros((rank, rank), F32)
    partner = [(2 * c, 2 * c + 1) for c in range(count // 2)]
    partner += [(2 * c + 1, 2 * c) for c in range(count // 2)]
    got = lax.ppermute(give, axis, partner)
    both = jnp.dot(got[:, :rank], own, precision=lax.Precision.HIGH) + jnp.concatenate(
        [zeros, got[:, rank:]], axis=1
    )
    pair = [(4 * g, 4 * g + 2) for g in range(groups)]
    pair += [(4 * g + 3, 4 * g + 1) for g in range(groups)]
    beside_state = lax.ppermute(both[:, rank:], axis, pair)
    beside_map = lax.ppermute(both[:, :rank], axis, pair)
    group_state = jnp.dot(both[:, :rank], beside_state, precision=lax.Precision.HIGH) + both[:, rank:]
    group_map = jnp.dot(both[:, :rank], beside_map, precision=lax.Precision.HIGH)
    beside = jnp.concatenate([beside_map, beside_state], axis=1)
    both = jnp.concatenate([group_map, group_state], axis=1)
    if groups <= 4:
        out = group_state
        for step in range(groups - 1):
            start = group_shift(out, axis, groups, 1)
            if step + 2 < groups:
                out = jnp.dot(group_map, start, precision=lax.Precision.HIGH) + group_state
    else:
        rounds = 0
        while 2 ** (rounds + 1) < groups - 1:
            rounds += 1
        shift = 1
        for _ in range(rounds):
            got = group_shift(both, axis, groups, shift)
            tail = jnp.concatenate([zeros, both[:, rank:]], axis=1)
            both = jnp.dot(both[:, :rank], got, precision=lax.Precision.HIGH) + tail
            shift *= 2
        near = group_shift(both, axis, groups, 1)
        far = group_shift(both[:, rank:], axis, groups, 1 + shift)
        start = jnp.dot(near[:, :rank], far, precision=lax.Precision.HIGH) + near[:, rank:]
    back = [(4 * g + 2, 4 * g) for g in range(groups)]
    back += [(4 * g + 1, 4 * g + 3) for g in range(groups)]
    sent = lax.ppermute(start, axis, back)
    mine = jnp.dot(beside_map, start, precision=lax.Precision.HIGH) + beside_state
    mine, sent = lax.optimization_barrier((mine, sent))
    holder = jnp.logical_or(place == 1, place == 2)
    enter = jnp.where(holder, mine, sent)
    send = jnp.dot(own[:, :rank], enter, precision=lax.Precision.HIGH) + own[:, rank:]
    other = lax.ppermute(send, axis, partner)
    return enter, other


def shards(
    right_sides,
    diagonal_blocks,
    lower_rows,
    lower_cols,
    lower_trans,
    upper_rows,
    upper_cols,
    upper_trans,
):
    count, rows, rhs = right_sides.shape
    rank = lower_trans.shape[1]
    count_row = lax.axis_size("row")
    grouped = count_row % 4 == 0 and count_row >= 8
    if grouped:
        flag = jnp.full((1,), lax.axis_index("row") % 2, jnp.int32)
    else:
        flag = jnp.zeros((1,), jnp.int32)
    lboth, lsrc, uboth, usrc = pl.pallas_call(
        sweep_kernel,
        out_shape=(
            jax.ShapeDtypeStruct((rank, rank + rhs), F32),
            jax.ShapeDtypeStruct((count, rank, rhs), F32),
            jax.ShapeDtypeStruct((rank, rank + rhs), F32),
            jax.ShapeDtypeStruct((count, rank, rhs), F32),
        ),
        in_specs=[pl.BlockSpec(memory_space=pltpu.SMEM)] + [pl.BlockSpec(memory_space=pltpu.VMEM)] * 5,
        name="sweep",
    )(flag, right_sides, lower_cols, lower_trans, upper_cols, upper_trans)
    diag = jnp.einsum(
        "kab,kbc->kac", diagonal_blocks, right_sides, preferred_element_type=F32
    )
    count_row = lax.axis_size("row")
    if grouped:
        enter, other = scan_groups(lboth, uboth, "row")
    elif count_row % 2 == 0 and count_row >= 4:
        enter, other = scan_chips(lboth, uboth, "row")
        flag = jnp.full((1,), lax.axis_index("row") % 2, jnp.int32)
    else:
        enter = scan_enter(lboth[:, :rank], lboth[:, rank:], "row", False)
        other = scan_enter(uboth[:, :rank], uboth[:, rank:], "row", True)
        flag = jnp.zeros((1,), jnp.int32)
    vmem = pl.BlockSpec(memory_space=pltpu.VMEM)
    return pl.pallas_call(
        apply_kernel,
        out_shape=jax.ShapeDtypeStruct((count, rows, rhs), BF16),
        scratch_shapes=[
            pltpu.VMEM((count, rank, rhs), BF16),
            pltpu.VMEM((count, rank, rhs), BF16),
        ],
        in_specs=[pl.BlockSpec(memory_space=pltpu.SMEM)] + [vmem] * 9,
        compiler_params=pltpu.CompilerParams(vmem_limit_bytes=LIMIT),
        name="apply",
    )(flag, enter, other, lower_trans, upper_trans, lsrc, usrc, diag, lower_rows, upper_rows)


def solution(mesh):
    spec = P(("sep", "row"), None, None)
    return jax.shard_map(
        shards, mesh=mesh, in_specs=(spec,) * 8, out_specs=spec, check_vma=False
    )
```

```python
import jax
import jax.numpy as jnp
from jax import lax
from jax.experimental import pallas as pl
from jax.experimental.pallas import tpu as pltpu
from jax.sharding import PartitionSpec as P

F32 = jnp.float32
BF16 = jnp.bfloat16
HIGHEST = lax.Precision.HIGHEST
LIMIT = 20 * 1024 * 1024


def split_dot(matrix, value):
    high = value.astype(BF16)
    low = (value - high.astype(F32)).astype(BF16)
    return jnp.dot(matrix, high, preferred_element_type=F32) + jnp.dot(
        matrix, low, preferred_element_type=F32
    )


def sweep_kernel(
    flag_ref, rhs_ref, lcols_ref, ltrans_ref, ucols_ref, utrans_ref,
    lmap_ref, umap_ref,
):
    count = rhs_ref.shape[0]
    lmap = lstate = umap = ustate = None
    for step in range(count):
        lk = step
        uk = count - 1 - step
        lsrc = lax.dot_general(lcols_ref[lk], rhs_ref[lk], (((0,), (0,)), ((), ())), preferred_element_type=F32)
        usrc = lax.dot_general(ucols_ref[uk], rhs_ref[uk], (((0,), (0,)), ((), ())), preferred_element_type=F32)
        ltrans = ltrans_ref[lk]
        utrans = utrans_ref[uk]
        if step == 0:
            lstate = lsrc
            ustate = usrc
            lmap = ltrans.astype(F32)
            umap = utrans.astype(F32)
        else:
            lstate = split_dot(ltrans, lstate) + lsrc
            ustate = split_dot(utrans, ustate) + usrc
            lmap = split_dot(ltrans, lmap)
            umap = split_dot(utrans, umap)
    rank = lmap.shape[0]
    first = flag_ref[0] == 0

    @pl.when(first)
    def _():
        lmap_ref[:, :rank] = lmap
        lmap_ref[:, rank:] = lstate
        umap_ref[:, :rank] = umap
        umap_ref[:, rank:] = ustate

    @pl.when(jnp.logical_not(first))
    def _():
        lmap_ref[:, :rank] = umap
        lmap_ref[:, rank:] = ustate
        umap_ref[:, :rank] = lmap
        umap_ref[:, rank:] = lstate


def apply_kernel(
    flag_ref, enter_ref, other_ref, ltrans_ref, utrans_ref, lcols_ref, ucols_ref, rhs_ref,
    diag_ref, lrows_ref, urows_ref, out_ref, lround_ref, uround_ref,
):
    count = ltrans_ref.shape[0]
    first = flag_ref[0] == 0
    lstate = jnp.where(first, enter_ref[...], other_ref[...])
    ustate = jnp.where(first, other_ref[...], enter_ref[...])
    for step in range(count):
        lk = step
        uk = count - 1 - step
        lround_ref[lk] = lstate.astype(BF16)
        uround_ref[uk] = ustate.astype(BF16)
        if step + 1 < count:
            lsrc = lax.dot_general(lcols_ref[lk], rhs_ref[lk], (((0,), (0,)), ((), ())), preferred_element_type=F32)
            usrc = lax.dot_general(ucols_ref[uk], rhs_ref[uk], (((0,), (0,)), ((), ())), preferred_element_type=F32)
            lstate = split_dot(ltrans_ref[lk], lstate) + lsrc
            ustate = split_dot(utrans_ref[uk], ustate) + usrc
    for k in range(count):
        total = diag_ref[k]
        total = total + jnp.dot(lrows_ref[k], lround_ref[k], preferred_element_type=F32)
        total = total + jnp.dot(urows_ref[k], uround_ref[k], preferred_element_type=F32)
        out_ref[k] = total.astype(out_ref.dtype)


def shifted(value, axis, count, shift, reverse):
    if reverse:
        pairs = [(i + shift, i) for i in range(count - shift)]
    else:
        pairs = [(i, i + shift) for i in range(count - shift)]
    return lax.ppermute(value, axis, pairs)


def scan_enter(summary_map, summary_state, axis, reverse):
    count = lax.axis_size(axis)
    rank = summary_map.shape[0]
    both = jnp.concatenate([summary_map, summary_state], axis=1)
    rounds = 0
    while 2 ** (rounds + 1) < count - 1:
        rounds += 1
    shift = 1
    for _ in range(rounds):
        got = shifted(both, axis, count, shift, reverse)
        joined = jnp.dot(both[:, :rank], got, precision=HIGHEST)
        both = joined + jnp.concatenate(
            [jnp.zeros_like(summary_map), both[:, rank:]], axis=1
        )
        shift *= 2
    near = shifted(both, axis, count, 1, reverse)
    far = shifted(both[:, rank:], axis, count, 1 + shift, reverse)
    return jnp.dot(near[:, :rank], far, precision=HIGHEST) + near[:, rank:]


def chip_shift(value, axis, chips, shift):
    pairs = [(2 * c, 2 * (c + shift)) for c in range(chips - shift)]
    pairs += [(2 * c + 1, 2 * (c - shift) + 1) for c in range(shift, chips)]
    return lax.ppermute(value, axis, pairs)


def scan_chips(lower, upper, axis):
    count = lax.axis_size(axis)
    chips = count // 2
    rank = lower.shape[0]
    first = lax.axis_index(axis) % 2 == 0
    own = jnp.where(first, lower, upper)
    partner = [(2 * c, 2 * c + 1) for c in range(chips)]
    partner += [(2 * c + 1, 2 * c) for c in range(chips)]
    got = lax.ppermute(jnp.where(first, upper, lower), axis, partner)
    tail = jnp.concatenate([jnp.zeros((rank, rank), F32), got[:, rank:]], axis=1)
    both = jnp.dot(got[:, :rank], own, precision=HIGHEST) + tail
    rounds = 0
    while 2 ** (rounds + 1) < chips - 1:
        rounds += 1
    shift = 1
    for _ in range(rounds):
        got = chip_shift(both, axis, chips, shift)
        tail = jnp.concatenate([jnp.zeros((rank, rank), F32), both[:, rank:]], axis=1)
        both = jnp.dot(both[:, :rank], got, precision=HIGHEST) + tail
        shift *= 2
    near = chip_shift(both, axis, chips, 1)
    far = chip_shift(both[:, rank:], axis, chips, 1 + shift)
    enter = jnp.dot(near[:, :rank], far, precision=HIGHEST) + near[:, rank:]
    send = jnp.dot(own[:, :rank], enter, precision=HIGHEST) + own[:, rank:]
    other = lax.ppermute(send, axis, partner)
    return enter, other


def group_shift(value, axis, groups, shift):
    pairs = [(4 * g + 2, 4 * (g + shift) + 2) for g in range(groups - shift)]
    pairs += [(4 * g + 1, 4 * (g - shift) + 1) for g in range(shift, groups)]
    return lax.ppermute(value, axis, pairs)


def scan_groups(own, give, axis):
    count = lax.axis_size(axis)
    groups = count // 4
    rank = own.shape[0]
    place = lax.axis_index(axis) % 4
    zeros = jnp.zeros((rank, rank), F32)
    partner = [(2 * c, 2 * c + 1) for c in range(count // 2)]
    partner += [(2 * c + 1, 2 * c) for c in range(count // 2)]
    got = lax.ppermute(give, axis, partner)
    both = jnp.dot(got[:, :rank], own, precision=lax.Precision.HIGH) + jnp.concatenate(
        [zeros, got[:, rank:]], axis=1
    )
    pair = [(4 * g, 4 * g + 2) for g in range(groups)]
    pair += [(4 * g + 3, 4 * g + 1) for g in range(groups)]
    beside_state = lax.ppermute(both[:, rank:], axis, pair)
    beside_map = lax.ppermute(both[:, :rank], axis, pair)
    group_state = jnp.dot(both[:, :rank], beside_state, precision=lax.Precision.HIGH) + both[:, rank:]
    group_map = jnp.dot(both[:, :rank], beside_map, precision=lax.Precision.HIGH)
    beside = jnp.concatenate([beside_map, beside_state], axis=1)
    both = jnp.concatenate([group_map, group_state], axis=1)
    if groups <= 4:
        out = group_state
        for step in range(groups - 1):
            start = group_shift(out, axis, groups, 1)
            if step + 2 < groups:
                out = jnp.dot(group_map, start, precision=lax.Precision.HIGH) + group_state
    else:
        rounds = 0
        while 2 ** (rounds + 1) < groups - 1:
            rounds += 1
        shift = 1
        for _ in range(rounds):
            got = group_shift(both, axis, groups, shift)
            tail = jnp.concatenate([zeros, both[:, rank:]], axis=1)
            both = jnp.dot(both[:, :rank], got, precision=lax.Precision.HIGH) + tail
            shift *= 2
        near = group_shift(both, axis, groups, 1)
        far = group_shift(both[:, rank:], axis, groups, 1 + shift)
        start = jnp.dot(near[:, :rank], far, precision=lax.Precision.HIGH) + near[:, rank:]
    back = [(4 * g + 2, 4 * g) for g in range(groups)]
    back += [(4 * g + 1, 4 * g + 3) for g in range(groups)]
    sent = lax.ppermute(start, axis, back)
    mine = jnp.dot(beside_map, start, precision=lax.Precision.HIGH) + beside_state
    mine, sent = lax.optimization_barrier((mine, sent))
    holder = jnp.logical_or(place == 1, place == 2)
    enter = jnp.where(holder, mine, sent)
    send = jnp.dot(own[:, :rank], enter, precision=lax.Precision.HIGH) + own[:, rank:]
    other = lax.ppermute(send, axis, partner)
    return enter, other


def shards(
    right_sides,
    diagonal_blocks,
    lower_rows,
    lower_cols,
    lower_trans,
    upper_rows,
    upper_cols,
    upper_trans,
):
    count, rows, rhs = right_sides.shape
    rank = lower_trans.shape[1]
    count_row = lax.axis_size("row")
    grouped = count_row % 4 == 0 and count_row >= 8
    if grouped:
        flag = jnp.full((1,), lax.axis_index("row") % 2, jnp.int32)
    else:
        flag = jnp.zeros((1,), jnp.int32)
    lboth, uboth = pl.pallas_call(
        sweep_kernel,
        out_shape=(
            jax.ShapeDtypeStruct((rank, rank + rhs), F32),
            jax.ShapeDtypeStruct((rank, rank + rhs), F32),
        ),
        in_specs=[pl.BlockSpec(memory_space=pltpu.SMEM)] + [pl.BlockSpec(memory_space=pltpu.VMEM)] * 5,
        name="sweep",
    )(flag, right_sides, lower_cols, lower_trans, upper_cols, upper_trans)
    diag = jnp.einsum(
        "kab,kbc->kac", diagonal_blocks, right_sides, preferred_element_type=F32
    )
    count_row = lax.axis_size("row")
    if grouped:
        enter, other = scan_groups(lboth, uboth, "row")
    elif count_row % 2 == 0 and count_row >= 4:
        enter, other = scan_chips(lboth, uboth, "row")
        flag = jnp.full((1,), lax.axis_index("row") % 2, jnp.int32)
    else:
        enter = scan_enter(lboth[:, :rank], lboth[:, rank:], "row", False)
        other = scan_enter(uboth[:, :rank], uboth[:, rank:], "row", True)
        flag = jnp.zeros((1,), jnp.int32)
    vmem = pl.BlockSpec(memory_space=pltpu.VMEM)
    return pl.pallas_call(
        apply_kernel,
        out_shape=jax.ShapeDtypeStruct((count, rows, rhs), BF16),
        scratch_shapes=[
            pltpu.VMEM((count, rank, rhs), BF16),
            pltpu.VMEM((count, rank, rhs), BF16),
        ],
        in_specs=[pl.BlockSpec(memory_space=pltpu.SMEM)] + [vmem] * 10,
        compiler_params=pltpu.CompilerParams(vmem_limit_bytes=LIMIT),
        name="apply",
    )(flag, enter, other, lower_trans, upper_trans, lower_cols, upper_cols, right_sides, diag, lower_rows, upper_rows)


def solution(mesh):
    spec = P(("sep", "row"), None, None)
    return jax.shard_map(
        shards, mesh=mesh, in_specs=(spec,) * 8, out_specs=spec, check_vma=False
    )
```
